32 devices in a mesh: seq: 4 (over y, x), shard: 8 (over z, core).
Axes of the slice: x: 2, y: 2, z: 4, core: 2. Of those that a mesh axis runs over, the one named last changes fastest.
Arguments:
- layer_in: bfloat16 [32, 1024, 768], P('shard', 'seq'), may hold values from -6 to 6
- layer_cotangent: bfloat16 [32, 1024, 768], P('shard', 'seq'), may hold values from -6 to 6
- doc_starts: int32 [32, 17], P('shard'), may hold values from 0 to 1024, as said below
- query_weight: float32 [768, 768], P(('seq', 'shard')), may hold values from -0.21875 to 0.21875
- key_weight: float32 [768, 768], P(('seq', 'shard')), may hold values from -0.21875 to 0.21875
- value_weight: float32 [768, 768], P(('seq', 'shard')), may hold values from -0.21875 to 0.21875
- out_weight: float32 [768, 768], P(('seq', 'shard')), may hold values from -3.5 to 3.5
- up_weight: float32 [768, 3072], P(('seq', 'shard')), may hold values from -0.21875 to 0.21875
- down_weight: float32 [3072, 768], P(('seq', 'shard')), may hold values from -0.109375 to 0.109375
- query_bias: float32 [768], P(('seq', 'shard')), may hold values from -0.625 to 0.625
- value_bias: float32 [768], P(('seq', 'shard')), may hold values from -0.1875 to 0.1875
- out_bias: float32 [768], P(('seq', 'shard')), may hold values from -0.625 to 0.625
- up_bias: float32 [3072], P(('seq', 'shard')), may hold values from -0.625 to 0.625
- down_bias: float32 [768], P(('seq', 'shard')), may hold values from -0.625 to 0.625
- mixer_gain: float32 [768], P(('seq', 'shard')), may hold values from 0.5 to 1.5
- mixer_shift: float32 [768], P(('seq', 'shard')), may hold values from -0.625 to 0.625
- final_gain: float32 [768], P(('seq', 'shard')), may hold values from 0.5 to 1.5
- final_shift: float32 [768], P(('seq', 'shard')), may hold values from -0.625 to 0.625
Outputs:
- layer_out: bfloat16 [32, 1024, 768], P('shard', 'seq')
- input_grad: float32 [32, 1024, 768], P('shard', 'seq')
- grad_query_weight: float32 [768, 768], P(('seq', 'shard'))
- grad_key_weight: float32 [768, 768], P(('seq', 'shard'))
- grad_value_weight: float32 [768, 768], P(('seq', 'shard'))
- grad_out_weight: float32 [768, 768], P(('seq', 'shard'))
- grad_up_weight: float32 [768, 3072], P(('seq', 'shard'))
- grad_down_weight: float32 [3072, 768], P(('seq', 'shard'))
- grad_query_bias: float32 [768], P(('seq', 'shard'))
- grad_value_bias: float32 [768], P(('seq', 'shard'))
- grad_out_bias: float32 [768], P(('seq', 'shard'))
- grad_up_bias: float32 [3072], P(('seq', 'shard'))
- grad_down_bias: float32 [768], P(('seq', 'shard'))
- grad_mixer_gain: float32 [768], P(('seq', 'shard'))
- grad_mixer_shift: float32 [768], P(('seq', 'shard'))
- grad_final_gain: float32 [768], P(('seq', 'shard'))
- grad_final_shift: float32 [768], P(('seq', 'shard'))
The draws below stay inside these ranges and needn't reach their ends.
Inputs may be any that keep to these rules, and one draw needn't show every extreme that they name: `doc_starts`: each row lists the first positions of the documents of its stream in rising order; it begins with 0, entries equal to 1024 mark unused slots, and the last entry is always 1024. A document spans at most 512 positions, some document of every stream exactly that; every document but the last of a stream spans at least 64.
All inputs are finite; a program needn't handle non-finite values.
Results may differ from the reference program's by a relative error of at most 0.017.
Values may be sent and summed in bfloat16 or wider, within the bound.
No kernel may reach another device: no remote copies, remote signals or barrier semaphores. Data moves between devices by JAX's collectives and lax.ppermute only.
A program may use at most 192 MiB of HBM per device.

```python
import math
import jax
import jax.numpy as jnp
from jax import lax

D = 768
DH = 64
FF = 3072
LEN = 1024
DOCS = 17
SEQUENCES = 32


def draw_doc_starts(key, part):
    first, second = jax.random.split(jax.random.fold_in(key, 11))
    gaps = jax.random.randint(first, (SEQUENCES, DOCS), LEN // 16, LEN // 2 + 1)
    which = jax.random.randint(second, (SEQUENCES, 1), 0, 2)
    columns = jnp.arange(DOCS, dtype=jnp.int32)[None, :]
    gaps = jnp.where(columns == which, LEN // 2, gaps).astype(jnp.int32)
    ends = jnp.cumsum(gaps, axis=1).astype(jnp.int32)
    starts = jnp.concatenate([jnp.zeros((SEQUENCES, 1), jnp.int32), ends[:, :-1]], axis=1)
    return jnp.minimum(starts, LEN).astype(jnp.int32)


def block_levels(stream_key, dims, cuts, low, high):
    factor_of, own = 1.0, jax.random.fold_in(stream_key, 6)
    for dim, parts in cuts:
        heights = jnp.exp(jax.random.uniform(jax.random.fold_in(own, dim), (parts,), jnp.float32, low / len(cuts), high / len(cuts)))
        factor_of = factor_of * jnp.repeat(heights, dims[dim] // parts).reshape([-1 if axis == dim else 1 for axis in range(len(dims))])
    return factor_of


def normal_values(key, dims, scale, most, pieces=(), held_as=jnp.bfloat16):
    values = jax.random.normal(key, dims, jnp.float32) * scale
    if len(pieces) > 0:
        values = block_levels(key, dims, pieces, -0.22, 0.18) * values
    return jnp.clip(values, min=-most, max=most).astype(held_as)


def setup_inputs(seed: int = 0) -> dict:
    key_of = jax.random.split(jax.random.key(seed), 19)
    layer_in = normal_values(key_of[0], (SEQUENCES, LEN, D), 1.0, 6.0, ((0, 8), (1, 4)))
    layer_cotangent = normal_values(key_of[1], (SEQUENCES, LEN, D), 1.0, 6.0, ((0, 8), (1, 4)))
    doc_starts = draw_doc_starts(jax.random.fold_in(key_of[18], 71), 0)
    query_weight = normal_values(key_of[3], (D, D), D ** -0.5, 0.21875, ((0, 32),), jnp.float32)
    key_weight = normal_values(key_of[4], (D, D), D ** -0.5, 0.21875, ((0, 32),), jnp.float32)
    value_weight = normal_values(key_of[5], (D, D), D ** -0.5, 0.21875, ((0, 32),), jnp.float32)
    out_weight = normal_values(key_of[6], (D, D), (max(1, D // 256)) ** -0.5, 3.5, ((0, 32),), jnp.float32)
    up_weight = normal_values(key_of[7], (D, FF), D ** -0.5, 0.21875, ((0, 32),), jnp.float32)
    down_weight = normal_values(key_of[8], (FF, D), FF ** -0.5, 0.109375, ((0, 32),), jnp.float32)
    query_bias = normal_values(key_of[9], (D,), 0.1, 0.625, ((0, 32),), jnp.float32)
    value_bias = normal_values(key_of[10], (D,), 0.03, 0.1875, ((0, 32),), jnp.float32)
    out_bias = normal_values(key_of[11], (D,), 0.1, 0.625, ((0, 32),), jnp.float32)
    up_bias = normal_values(key_of[12], (FF,), 0.1, 0.625, ((0, 32),), jnp.float32)
    down_bias = normal_values(key_of[13], (D,), 0.1, 0.625, ((0, 32),), jnp.float32)
    mixer_gain = jnp.clip(1.0 + 0.1 * jax.random.normal(key_of[14], (D,), jnp.float32), 0.5, 1.5)
    mixer_shift = normal_values(key_of[15], (D,), 0.1, 0.625, ((0, 32),), jnp.float32)
    final_gain = jnp.clip(1.0 + 0.1 * jax.random.normal(key_of[16], (D,), jnp.float32), 0.5, 1.5)
    final_shift = normal_values(key_of[17], (D,), 0.1, 0.625, ((0, 32),), jnp.float32)
    return {"layer_in": layer_in, "layer_cotangent": layer_cotangent, "doc_starts": doc_starts, "query_weight": query_weight, "key_weight": key_weight, "value_weight": value_weight, "out_weight": out_weight, "up_weight": up_weight, "down_weight": down_weight, "query_bias": query_bias, "value_bias": value_bias, "out_bias": out_bias, "up_bias": up_bias, "down_bias": down_bias, "mixer_gain": mixer_gain, "mixer_shift": mixer_shift, "final_gain": final_gain, "final_shift": final_shift}


@jax.custom_vjp
def low(v):
    return lax.optimization_barrier(v.astype(jnp.bfloat16)).astype(jnp.float32)

@jax.custom_vjp
def low_back(v):
    return v

def low_keep(v):
    return (low(v), None)

def low_pass(kept, grad):
    return (grad,)

def back_keep(v):
    return (v, None)

def back_low(kept, grad):
    return (low(grad),)
low.defvjp(low_keep, low_pass)
low_back.defvjp(back_keep, back_low)
EPS = 1e-06
NEG = -1e+30
HIGH = lax.Precision.HIGHEST
ROOT_HALF = 0.7071067811865476

def product(left, right):
    return jnp.dot(left, right, precision=HIGH, preferred_element_type=jnp.float32)

def segment_ids(starts, length):
    places = lax.broadcasted_iota(jnp.int32, (1, length, 1), 1)
    return lax.optimization_barrier(jnp.sum((starts[:, None, :] <= places).astype(jnp.int32), axis=2))

def layer_norm(rows, gain, shift):
    middle = lax.optimization_barrier(jnp.mean(rows, axis=-1, keepdims=True))
    centred = rows - middle
    spread = lax.optimization_barrier(jnp.mean(centred * centred, axis=-1, keepdims=True))
    return centred * lax.rsqrt(spread + EPS) * gain + shift

def gelu_value(value):
    return 0.5 * value * (1.0 + lax.erf(value * ROOT_HALF))

def attend(item):
    queries, keys, values, segment = item
    scores = jnp.einsum('qhd,khd->hqk', queries, keys, precision=HIGH)
    scores = low_back(scores * DH ** (-0.5))
    allowed = segment[:, None] == segment[None, :]
    scores = jnp.where(allowed[None], scores, NEG)
    highest = lax.optimization_barrier(jnp.max(scores, axis=-1, keepdims=True))
    raised = jnp.exp(scores - highest)
    weights = low(raised / lax.optimization_barrier(jnp.sum(raised, axis=-1, keepdims=True)))
    return jnp.einsum('hqk,khd->qhd', weights, values, precision=HIGH)

def forward(block, params, segment):
    w_query, w_key, w_value, w_out, w_up, w_down, b_query, b_value, b_out, b_up, b_down, g_mixer, e_mixer, g_final, e_final = [low(p) for p in params]
    group, length, width = block.shape
    flat = block.reshape(group * length, width)
    queries = low(low_back(product(flat, w_query) + b_query))
    keys = low(low_back(product(flat, w_key)))
    values = low(low_back(product(flat, w_value) + b_value))
    shape = (group, length, width // DH, DH)
    context = lax.map(jax.checkpoint(attend), (queries.reshape(shape), keys.reshape(shape), values.reshape(shape), segment))
    context = low(low_back(context.reshape(group * length, width)))
    attn = low_back(product(context, w_out) + b_out)
    mixed = layer_norm(flat + attn, g_mixer, e_mixer)
    upper = low(mixed)
    preact = low_back(product(upper, w_up) + b_up)
    hidden = low(gelu_value(preact))
    ffout = low_back(product(hidden, w_down) + b_down)
    result = layer_norm(mixed + ffout, g_final, e_final)
    return result.reshape(group, length, width)

def reference(layer_in, layer_cotangent, doc_starts, query_weight, key_weight, value_weight, out_weight, up_weight, down_weight, query_bias, value_bias, out_bias, up_bias, down_bias, mixer_gain, mixer_shift, final_gain, final_shift):
    params = (query_weight, key_weight, value_weight, out_weight, up_weight, down_weight, query_bias, value_bias, out_bias, up_bias, down_bias, mixer_gain, mixer_shift, final_gain, final_shift)
    params = tuple((p.astype(jnp.float32) for p in params))
    segment = segment_ids(doc_starts, LEN)
    group = math.gcd(SEQUENCES, 4)
    count = SEQUENCES // group
    inputs = layer_in.astype(jnp.float32).reshape(count, group, LEN, D)
    upstream = layer_cotangent.astype(jnp.float32).reshape(count, group, LEN, D)
    segments = segment.reshape(count, group, LEN)

    def step(totals, item):
        block, block_up, block_seg = item

        def run(block_in, *weights):
            return forward(block_in, weights, block_seg)
        result, pull = jax.vjp(run, block, *params)
        grads = pull(block_up)
        totals = tuple((t + g for t, g in zip(totals, grads[1:])))
        return (totals, (result.astype(jnp.bfloat16), grads[0]))
    zeros = tuple((jnp.zeros(p.shape, jnp.float32) for p in params))
    totals, (outputs, input_grads) = lax.scan(step, zeros, (inputs, upstream, segments))
    return (outputs.reshape(SEQUENCES, LEN, D), input_grads.reshape(SEQUENCES, LEN, D), totals[0], totals[1], totals[2], totals[3], totals[4], totals[5], totals[6], totals[7], totals[8], totals[9], totals[10], totals[11], totals[12], totals[13], totals[14])
```

```python
import jax
import jax.numpy as jnp
from jax import lax
from jax.experimental.layout import Layout, with_layout_constraint
from jax.sharding import PartitionSpec as P


DH = 64
LEN = 1024


EPS = 1e-06
NEG = -1e30
ROOT_HALF = 0.7071067811865476
INV_ROOT_TWO_PI = 0.3989422804014327


def contract_rows(left, right):
    return lax.dot_general(
        left, right, (((0,), (0,)), ((), ())), preferred_element_type=jnp.float32
    )


def times_transpose(left, right):
    return lax.dot_general(
        left, right, (((1,), (1,)), ((), ())), preferred_element_type=jnp.float32
    )


def segment_ids(starts, length):
    places = lax.broadcasted_iota(jnp.int32, (1, length, 1), 1)
    return jnp.sum((starts[:, None, :] <= places).astype(jnp.int32), axis=2)


def norm_forward(rows, gain, shift):
    middle = jnp.mean(rows, axis=-1, keepdims=True)
    centred = rows - middle
    spread = jnp.mean(centred * centred, axis=-1, keepdims=True)
    inverse = lax.rsqrt(spread + EPS)
    normed = centred * inverse
    return (normed * gain + shift, normed, inverse)


def norm_backward(upstream, gain, normed, inverse):
    scaled = upstream * gain
    inner = jnp.mean(scaled, axis=-1, keepdims=True)
    along = jnp.mean(scaled * normed, axis=-1, keepdims=True)
    return inverse * (scaled - inner - normed * along)


def gelu_value(value):
    return 0.5 * value * (1.0 + lax.erf(value * ROOT_HALF))


def gelu_slope(value):
    return (
        0.5 * (1.0 + lax.erf(value * ROOT_HALF))
        + value * jnp.exp(-0.5 * value * value) * INV_ROOT_TWO_PI
    )


def masked_scores(queries, keys, seg_rows, seg_all, scale):
    scores = jnp.einsum("qhd,khd->hqk", queries, keys, preferred_element_type=jnp.float32) * scale
    allowed = seg_rows[:, None] == seg_all[None, :]
    return jnp.where(allowed[None], scores, NEG)


def attend_forward(item):
    qkv, segment = item
    queries, keys, values = qkv[:, 0], qkv[:, 1], qkv[:, 2]
    length, heads, depth = queries.shape
    rows = min(512, length)
    blocks = length // rows
    scale = depth ** (-0.5)

    def one(piece):
        block_q, block_seg = piece
        scores = masked_scores(block_q, keys, block_seg, segment, scale)
        highest = jnp.max(scores, axis=-1, keepdims=True)
        raised = jnp.exp(scores - highest)
        total = jnp.sum(raised, axis=-1, keepdims=True)
        weights = (raised / total).astype(jnp.bfloat16)
        context = jnp.einsum("hqk,khd->qhd", weights, values, preferred_element_type=jnp.float32)
        return (context.astype(jnp.bfloat16), (highest + jnp.log(total))[..., 0])

    context, logsum = lax.map(
        one, (queries.reshape(blocks, rows, heads, depth), segment.reshape(blocks, rows))
    )
    return (context.reshape(length, heads, depth), logsum)


def attend_backward(item):
    qkv, segment, logsum, upstream = item
    queries, keys, values = qkv[:, 0], qkv[:, 1], qkv[:, 2]
    length, heads, depth = queries.shape
    rows = min(512, length)
    blocks = length // rows
    scale = depth ** (-0.5)

    def one(carry, piece):
        key_acc, value_acc = carry
        block_q, block_seg, block_sum, block_up = piece
        scores = masked_scores(block_q, keys, block_seg, segment, scale)
        weights = jnp.exp(scores - block_sum[..., None])
        value_acc = value_acc + jnp.einsum(
            "hqk,qhd->khd",
            weights.astype(jnp.bfloat16),
            block_up,
            preferred_element_type=jnp.float32,
        )
        slope = jnp.einsum("qhd,khd->hqk", block_up, values, preferred_element_type=jnp.float32)
        inner = jnp.sum(weights * slope, axis=-1, keepdims=True)
        score_grad = (weights * (slope - inner)).astype(jnp.bfloat16)
        query_grad = (
            jnp.einsum("hqk,khd->qhd", score_grad, keys, preferred_element_type=jnp.float32) * scale
        )
        key_acc = (
            key_acc
            + jnp.einsum("hqk,qhd->khd", score_grad, block_q, preferred_element_type=jnp.float32)
            * scale
        )
        return ((key_acc, value_acc), query_grad.astype(jnp.bfloat16))

    empty = jnp.zeros((length, heads, depth), jnp.float32)
    pieces = (
        queries.reshape(blocks, rows, heads, depth),
        segment.reshape(blocks, rows),
        logsum,
        upstream.reshape(blocks, rows, heads, depth),
    )
    (key_grad, value_grad), query_grad = lax.scan(one, (empty, empty), pieces)
    return jnp.stack(
        [
            query_grad.reshape(length, heads, depth),
            key_grad.astype(jnp.bfloat16),
            value_grad.astype(jnp.bfloat16),
        ],
        axis=1,
    )


def lane_pick(block, index):
    lanes = lax.broadcasted_iota(jnp.int32, block.shape, 1)
    return jnp.sum(jnp.where(lanes == index, block, 0.0), axis=1)


def pad_lanes(block):
    extra = -block.shape[1] % 256
    block = jnp.pad(block, ((0, 0), (0, extra))) if extra else block
    return with_layout_constraint(block, Layout(major_to_minor=(0, 1)))


def per_device(
    layer_in,
    layer_cotangent,
    doc_starts,
    query_weight,
    key_weight,
    value_weight,
    out_weight,
    up_weight,
    down_weight,
    query_bias,
    value_bias,
    out_bias,
    up_bias,
    down_bias,
    mixer_gain,
    mixer_shift,
    final_gain,
    final_shift,
):
    axes = ("seq", "shard")
    rows, width = query_weight.shape
    ff = up_weight.shape[1]

    def column(vector):
        return vector.reshape(rows, -1)

    packed = jnp.concatenate(
        [
            query_weight,
            key_weight,
            value_weight,
            out_weight,
            up_weight,
            down_weight.reshape(rows, -1),
            column(query_bias),
            column(value_bias),
            column(out_bias),
            column(down_bias),
            column(mixer_gain),
            column(mixer_shift),
            column(final_gain),
            column(final_shift),
            column(up_bias),
        ],
        axis=1,
    ).astype(jnp.bfloat16)
    full = lax.all_gather(packed, axes, axis=0, tiled=True)
    model = full.shape[0]
    full_qkv = full[:, : 3 * width]
    full_out = full[:, 3 * width : 4 * width]
    full_up = full[:, 4 * width : 4 * width + ff]
    full_down = full[:, 4 * width + ff : 4 * width + 2 * ff].reshape(ff, width)
    base = 4 * width + 2 * ff
    bias_query, bias_value, bias_out, bias_down, gain_mixer, shift_mixer, gain_final, shift_final = (
        full[:, base + i].astype(jnp.float32) for i in range(8)
    )
    bias_up = full[:, base + 8 :].reshape(ff).astype(jnp.float32)

    streams, part_len, _ = layer_in.shape
    row_count = streams * part_len
    heads = width // DH
    flat = layer_in.reshape(row_count, width)
    qkv_bias = jnp.concatenate([bias_query, jnp.zeros_like(bias_query), bias_value])
    qkv = (jnp.dot(flat, full_qkv, preferred_element_type=jnp.float32) + qkv_bias).astype(
        jnp.bfloat16
    )
    head_qkv = lax.all_to_all(
        qkv.reshape(streams, part_len, 3, heads, DH), "seq", split_axis=3, concat_axis=1, tiled=True
    )
    segment = segment_ids(doc_starts, LEN)
    context, logsum = lax.map(attend_forward, (head_qkv, segment))
    context_rows = lax.all_to_all(context, "seq", split_axis=1, concat_axis=2, tiled=True).reshape(
        row_count, width
    )
    attn = jnp.dot(context_rows, full_out, preferred_element_type=jnp.float32) + bias_out
    mixed, normed_mixer, inverse_mixer = norm_forward(
        flat.astype(jnp.float32) + attn, gain_mixer, shift_mixer
    )
    upper = mixed.astype(jnp.bfloat16)
    preact = jnp.dot(upper, full_up, preferred_element_type=jnp.float32) + bias_up
    hidden = gelu_value(preact).astype(jnp.bfloat16)
    ffout = jnp.dot(hidden, full_down, preferred_element_type=jnp.float32) + bias_down
    result, normed_final, inverse_final = norm_forward(mixed + ffout, gain_final, shift_final)
    layer_out = result.astype(jnp.bfloat16).reshape(streams, part_len, width)

    upstream = layer_cotangent.reshape(row_count, width).astype(jnp.float32)
    grad_final_gain = jnp.sum(upstream * normed_final, axis=0)
    grad_final_shift = jnp.sum(upstream, axis=0)
    back_final = norm_backward(upstream, gain_final, normed_final, inverse_final)
    back_ffout = back_final.astype(jnp.bfloat16)
    grad_down_weight = contract_rows(hidden, back_ffout)
    grad_down_bias = jnp.sum(back_ffout.astype(jnp.float32), axis=0)
    back_preact = (times_transpose(back_ffout, full_down) * gelu_slope(preact)).astype(jnp.bfloat16)
    grad_up_weight = contract_rows(upper, back_preact)
    grad_up_bias = jnp.sum(back_preact.astype(jnp.float32), axis=0)
    back_mixed = back_final + times_transpose(back_preact, full_up)
    grad_mixer_gain = jnp.sum(back_mixed * normed_mixer, axis=0)
    grad_mixer_shift = jnp.sum(back_mixed, axis=0)
    back_first = norm_backward(back_mixed, gain_mixer, normed_mixer, inverse_mixer)
    back_attn = back_first.astype(jnp.bfloat16)
    grad_out_weight = contract_rows(context_rows, back_attn)
    grad_out_bias = jnp.sum(back_attn.astype(jnp.float32), axis=0)

    early = jnp.concatenate(
        [
            grad_out_weight,
            grad_up_weight,
            grad_down_weight.reshape(model, -1),
            grad_out_bias[:, None],
            grad_down_bias[:, None],
            grad_mixer_gain[:, None],
            grad_mixer_shift[:, None],
            grad_final_gain[:, None],
            grad_final_shift[:, None],
            grad_up_bias.reshape(model, -1),
        ],
        axis=1,
    )
    early = pad_lanes(early)
    early, back_attn = lax.optimization_barrier((early, back_attn))
    early_sum = lax.psum_scatter(early, axes, scatter_dimension=0, tiled=True)

    back_context = times_transpose(back_attn, full_out).astype(jnp.bfloat16)
    head_back = lax.all_to_all(
        back_context.reshape(streams, part_len, heads, DH), "seq", split_axis=2, concat_axis=1, tiled=True
    )
    qkv_back = lax.map(attend_backward, (head_qkv, segment, logsum, head_back))
    rows_back = lax.all_to_all(qkv_back, "seq", split_axis=1, concat_axis=3, tiled=True).reshape(
        row_count, 3 * width
    )
    grad_qkv_weight = contract_rows(flat, rows_back)
    grad_query_bias = jnp.sum(rows_back[:, :width].astype(jnp.float32), axis=0)
    grad_value_bias = jnp.sum(rows_back[:, 2 * width :].astype(jnp.float32), axis=0)
    input_grad = (back_first + times_transpose(rows_back, full_qkv)).reshape(
        streams, part_len, width
    )
    late = pad_lanes(
        jnp.concatenate([grad_qkv_weight, grad_query_bias[:, None], grad_value_bias[:, None]], axis=1)
    )
    late_sum = lax.psum_scatter(late, axes, scatter_dimension=0, tiled=True)

    base = width + 2 * ff
    late_tail = late_sum[:, 3 * width :]
    early_tail = early_sum[:, base:]
    return (
        layer_out,
        input_grad,
        late_sum[:, :width],
        late_sum[:, width : 2 * width],
        late_sum[:, 2 * width : 3 * width],
        early_sum[:, :width],
        early_sum[:, width : width + ff],
        early_sum[:, width + ff : width + 2 * ff].reshape(-1, width),
        lane_pick(late_tail, 0),
        lane_pick(late_tail, 1),
        lane_pick(early_tail, 0),
        jnp.stack([lane_pick(early_tail, 6 + i) for i in range(ff // width)], axis=1).reshape(-1),
        lane_pick(early_tail, 1),
        lane_pick(early_tail, 2),
        lane_pick(early_tail, 3),
        lane_pick(early_tail, 4),
        lane_pick(early_tail, 5),
    )


def solution(mesh):
    in_specs = (
        P("shard", "seq", None),
        P("shard", "seq", None),
        P("shard", None),
        P(("seq", "shard"), None),
        P(("seq", "shard"), None),
        P(("seq", "shard"), None),
        P(("seq", "shard"), None),
        P(("seq", "shard"), None),
        P(("seq", "shard"), None),
        P(("seq", "shard")),
        P(("seq", "shard")),
        P(("seq", "shard")),
        P(("seq", "shard")),
        P(("seq", "shard")),
        P(("seq", "shard")),
        P(("seq", "shard")),
        P(("seq", "shard")),
        P(("seq", "shard")),
    )
    out_specs = (
        P("shard", "seq", None),
        P("shard", "seq", None),
        P(("seq", "shard"), None),
        P(("seq", "shard"), None),
        P(("seq", "shard"), None),
        P(("seq", "shard"), None),
        P(("seq", "shard"), None),
        P(("seq", "shard"), None),
        P(("seq", "shard")),
        P(("seq", "shard")),
        P(("seq", "shard")),
        P(("seq", "shard")),
        P(("seq", "shard")),
        P(("seq", "shard")),
        P(("seq", "shard")),
        P(("seq", "shard")),
        P(("seq", "shard")),
    )

    return jax.shard_map(per_device, mesh=mesh, in_specs=in_specs, out_specs=out_specs, check_vma=False)
```

```python
import jax
import jax.numpy as jnp
from jax import lax
from jax.experimental.layout import Layout, with_layout_constraint
from jax.sharding import PartitionSpec as P


DH = 64
LEN = 1024


EPS = 1e-06
NEG = -1e30
ROOT_HALF = 0.7071067811865476
INV_ROOT_TWO_PI = 0.3989422804014327


def contract_rows(left, right):
    return lax.dot_general(
        left, right, (((0,), (0,)), ((), ())), preferred_element_type=jnp.float32
    )


def times_transpose(left, right):
    return lax.dot_general(
        left, right, (((1,), (1,)), ((), ())), preferred_element_type=jnp.float32
    )


def segment_ids(starts, length):
    places = lax.broadcasted_iota(jnp.int32, (1, length, 1), 1)
    return jnp.sum((starts[:, None, :] <= places).astype(jnp.int32), axis=2)


def norm_forward(rows, gain, shift):
    middle = jnp.mean(rows, axis=-1, keepdims=True)
    centred = rows - middle
    spread = jnp.mean(centred * centred, axis=-1, keepdims=True)
    inverse = lax.rsqrt(spread + EPS)
    normed = centred * inverse
    return (normed * gain + shift, normed, inverse)


def norm_backward(upstream, gain, normed, inverse):
    scaled = upstream * gain
    inner = jnp.mean(scaled, axis=-1, keepdims=True)
    along = jnp.mean(scaled * normed, axis=-1, keepdims=True)
    return inverse * (scaled - inner - normed * along)


def gelu_value(value):
    return 0.5 * value * (1.0 + lax.erf(value * ROOT_HALF))


def gelu_slope(value):
    return (
        0.5 * (1.0 + lax.erf(value * ROOT_HALF))
        + value * jnp.exp(-0.5 * value * value) * INV_ROOT_TWO_PI
    )


def masked_scores(queries, keys, seg_rows, seg_all, scale):
    scores = jnp.einsum("qhd,khd->hqk", queries, keys, preferred_element_type=jnp.float32) * scale
    allowed = seg_rows[:, None] == seg_all[None, :]
    return jnp.where(allowed[None], scores, NEG)


def attend_forward(item):
    qkv, segment = item
    queries, keys, values = qkv[:, 0], qkv[:, 1], qkv[:, 2]
    length, heads, depth = queries.shape
    rows = min(512, length)
    blocks = length // rows
    scale = depth ** (-0.5)

    def one(piece):
        block_q, block_seg = piece
        scores = masked_scores(block_q, keys, block_seg, segment, scale)
        highest = jnp.max(scores, axis=-1, keepdims=True)
        raised = jnp.exp(scores - highest)
        total = jnp.sum(raised, axis=-1, keepdims=True)
        weights = (raised / total).astype(jnp.bfloat16)
        context = jnp.einsum("hqk,khd->qhd", weights, values, preferred_element_type=jnp.float32)
        return (context.astype(jnp.bfloat16), (highest + jnp.log(total))[..., 0])

    context, logsum = lax.map(
        one, (queries.reshape(blocks, rows, heads, depth), segment.reshape(blocks, rows))
    )
    return (context.reshape(length, heads, depth), logsum)


def attend_backward(item):
    qkv, segment, logsum, upstream = item
    queries, keys, values = qkv[:, 0], qkv[:, 1], qkv[:, 2]
    length, heads, depth = queries.shape
    rows = min(512, length)
    blocks = length // rows
    scale = depth ** (-0.5)

    def one(carry, piece):
        key_acc, value_acc = carry
        block_q, block_seg, block_sum, block_up = piece
        scores = masked_scores(block_q, keys, block_seg, segment, scale)
        weights = jnp.exp(scores - block_sum[..., None])
        value_acc = value_acc + jnp.einsum(
            "hqk,qhd->khd",
            weights.astype(jnp.bfloat16),
            block_up,
            preferred_element_type=jnp.float32,
        )
        slope = jnp.einsum("qhd,khd->hqk", block_up, values, preferred_element_type=jnp.float32)
        inner = jnp.sum(weights * slope, axis=-1, keepdims=True)
        score_grad = (weights * (slope - inner)).astype(jnp.bfloat16)
        query_grad = (
            jnp.einsum("hqk,khd->qhd", score_grad, keys, preferred_element_type=jnp.float32) * scale
        )
        key_acc = (
            key_acc
            + jnp.einsum("hqk,qhd->khd", score_grad, block_q, preferred_element_type=jnp.float32)
            * scale
        )
        return ((key_acc, value_acc), query_grad.astype(jnp.bfloat16))

    empty = jnp.zeros((length, heads, depth), jnp.float32)
    pieces = (
        queries.reshape(blocks, rows, heads, depth),
        segment.reshape(blocks, rows),
        logsum,
        upstream.reshape(blocks, rows, heads, depth),
    )
    (key_grad, value_grad), query_grad = lax.scan(one, (empty, empty), pieces)
    return jnp.stack(
        [
            query_grad.reshape(length, heads, depth),
            key_grad.astype(jnp.bfloat16),
            value_grad.astype(jnp.bfloat16),
        ],
        axis=1,
    )


def lane_pick(block, index):
    lanes = lax.broadcasted_iota(jnp.int32, block.shape, 1)
    return jnp.sum(jnp.where(lanes == index, block, 0.0), axis=1)


def pack_lanes(pieces):
    pieces = [p.astype(jnp.bfloat16) for p in pieces]
    extra = -sum(p.shape[1] for p in pieces) % 256
    if extra:
        pieces.append(jnp.zeros((pieces[0].shape[0], extra), jnp.bfloat16))
    block = jnp.concatenate(pieces, axis=1)
    return with_layout_constraint(block, Layout(major_to_minor=(0, 1)))


def per_device(
    layer_in,
    layer_cotangent,
    doc_starts,
    query_weight,
    key_weight,
    value_weight,
    out_weight,
    up_weight,
    down_weight,
    query_bias,
    value_bias,
    out_bias,
    up_bias,
    down_bias,
    mixer_gain,
    mixer_shift,
    final_gain,
    final_shift,
):
    axes = ("seq", "shard")
    rows, width = query_weight.shape
    ff = up_weight.shape[1]

    def column(vector):
        return vector.reshape(rows, -1)

    first = jnp.concatenate(
        [
            query_weight,
            key_weight,
            value_weight,
            column(query_bias),
            column(value_bias),
            column(out_bias),
            column(down_bias),
            column(mixer_gain),
            column(mixer_shift),
            column(final_gain),
            column(final_shift),
            column(up_bias),
        ],
        axis=1,
    ).astype(jnp.bfloat16)
    second = jnp.concatenate(
        [out_weight, up_weight, down_weight.reshape(rows, -1)], axis=1
    ).astype(jnp.bfloat16)
    full_first = lax.all_gather(first, axes, axis=0, tiled=True)
    full_second = lax.all_gather(second, axes, axis=0, tiled=True)
    model = full_first.shape[0]
    full_qkv = full_first[:, : 3 * width]
    full_out = full_second[:, :width]
    full_up = full_second[:, width : width + ff]
    full_down = full_second[:, width + ff : width + 2 * ff].reshape(ff, width)
    base = 3 * width
    bias_query, bias_value, bias_out, bias_down, gain_mixer, shift_mixer, gain_final, shift_final = (
        full_first[:, base + i].astype(jnp.float32) for i in range(8)
    )
    bias_up = full_first[:, base + 8 :].reshape(ff).astype(jnp.float32)

    streams, part_len, _ = layer_in.shape
    row_count = streams * part_len
    heads = width // DH
    flat = layer_in.reshape(row_count, width)
    qkv_bias = jnp.concatenate([bias_query, jnp.zeros_like(bias_query), bias_value])
    qkv = (jnp.dot(flat, full_qkv, preferred_element_type=jnp.float32) + qkv_bias).astype(
        jnp.bfloat16
    )
    head_qkv = lax.all_to_all(
        qkv.reshape(streams, part_len, 3, heads, DH), "seq", split_axis=3, concat_axis=1, tiled=True
    )
    segment = segment_ids(doc_starts, LEN)
    context, logsum = lax.map(attend_forward, (head_qkv, segment))
    context_rows = lax.all_to_all(context, "seq", split_axis=1, concat_axis=2, tiled=True).reshape(
        row_count, width
    )
    attn = jnp.dot(context_rows, full_out, preferred_element_type=jnp.float32) + bias_out
    mixed, normed_mixer, inverse_mixer = norm_forward(
        flat.astype(jnp.float32) + attn, gain_mixer, shift_mixer
    )
    upper = mixed.astype(jnp.bfloat16)
    preact = jnp.dot(upper, full_up, preferred_element_type=jnp.float32) + bias_up
    hidden = gelu_value(preact).astype(jnp.bfloat16)
    ffout = jnp.dot(hidden, full_down, preferred_element_type=jnp.float32) + bias_down
    result, normed_final, inverse_final = norm_forward(mixed + ffout, gain_final, shift_final)
    layer_out = result.astype(jnp.bfloat16).reshape(streams, part_len, width)

    upstream = layer_cotangent.reshape(row_count, width).astype(jnp.float32)
    grad_final_gain = jnp.sum(upstream * normed_final, axis=0)
    grad_final_shift = jnp.sum(upstream, axis=0)
    back_final = norm_backward(upstream, gain_final, normed_final, inverse_final)
    back_ffout = back_final.astype(jnp.bfloat16)
    grad_down_weight = contract_rows(hidden, back_ffout)
    grad_down_bias = jnp.sum(back_ffout.astype(jnp.float32), axis=0)
    back_preact = (times_transpose(back_ffout, full_down) * gelu_slope(preact)).astype(jnp.bfloat16)
    grad_up_weight = contract_rows(upper, back_preact)
    grad_up_bias = jnp.sum(back_preact.astype(jnp.float32), axis=0)
    back_mixed = back_final + times_transpose(back_preact, full_up)
    grad_mixer_gain = jnp.sum(back_mixed * normed_mixer, axis=0)
    grad_mixer_shift = jnp.sum(back_mixed, axis=0)
    back_first = norm_backward(back_mixed, gain_mixer, normed_mixer, inverse_mixer)
    back_attn = back_first.astype(jnp.bfloat16)
    grad_out_weight = contract_rows(context_rows, back_attn)
    grad_out_bias = jnp.sum(back_attn.astype(jnp.float32), axis=0)

    early = pack_lanes(
        [
            grad_out_weight,
            grad_up_weight,
            grad_down_weight.reshape(model, -1),
            grad_out_bias[:, None],
            grad_down_bias[:, None],
            grad_mixer_gain[:, None],
            grad_mixer_shift[:, None],
            grad_final_gain[:, None],
            grad_final_shift[:, None],
            grad_up_bias.reshape(model, -1),
        ]
    )
    early, back_attn = lax.optimization_barrier((early, back_attn))
    early_sum = lax.psum_scatter(early, axes, scatter_dimension=0, tiled=True).astype(jnp.float32)

    back_context = times_transpose(back_attn, full_out).astype(jnp.bfloat16)
    head_back = lax.all_to_all(
        back_context.reshape(streams, part_len, heads, DH), "seq", split_axis=2, concat_axis=1, tiled=True
    )
    qkv_back = lax.map(attend_backward, (head_qkv, segment, logsum, head_back))
    rows_back = lax.all_to_all(qkv_back, "seq", split_axis=1, concat_axis=3, tiled=True).reshape(
        row_count, 3 * width
    )
    grad_qkv_weight = contract_rows(flat, rows_back)
    grad_query_bias = jnp.sum(rows_back[:, :width].astype(jnp.float32), axis=0)
    grad_value_bias = jnp.sum(rows_back[:, 2 * width :].astype(jnp.float32), axis=0)
    input_grad = (back_first + times_transpose(rows_back, full_qkv)).reshape(
        streams, part_len, width
    )
    late = pack_lanes([grad_qkv_weight, grad_query_bias[:, None], grad_value_bias[:, None]])
    late_sum = lax.psum_scatter(late, axes, scatter_dimension=0, tiled=True).astype(jnp.float32)

    base = width + 2 * ff
    late_tail = late_sum[:, 3 * width :]
    early_tail = early_sum[:, base:]
    return (
        layer_out,
        input_grad,
        late_sum[:, :width],
        late_sum[:, width : 2 * width],
        late_sum[:, 2 * width : 3 * width],
        early_sum[:, :width],
        early_sum[:, width : width + ff],
        early_sum[:, width + ff : width + 2 * ff].reshape(-1, width),
        lane_pick(late_tail, 0),
        lane_pick(late_tail, 1),
        lane_pick(early_tail, 0),
        jnp.stack([lane_pick(early_tail, 6 + i) for i in range(ff // width)], axis=1).reshape(-1),
        lane_pick(early_tail, 1),
        lane_pick(early_tail, 2),
        lane_pick(early_tail, 3),
        lane_pick(early_tail, 4),
        lane_pick(early_tail, 5),
    )


def solution(mesh):
    in_specs = (
        P("shard", "seq", None),
        P("shard", "seq", None),
        P("shard", None),
        P(("seq", "shard"), None),
        P(("seq", "shard"), None),
        P(("seq", "shard"), None),
        P(("seq", "shard"), None),
        P(("seq", "shard"), None),
        P(("seq", "shard"), None),
        P(("seq", "shard")),
        P(("seq", "shard")),
        P(("seq", "shard")),
        P(("seq", "shard")),
        P(("seq", "shard")),
        P(("seq", "shard")),
        P(("seq", "shard")),
        P(("seq", "shard")),
        P(("seq", "shard")),
    )
    out_specs = (
        P("shard", "seq", None),
        P("shard", "seq", None),
        P(("seq", "shard"), None),
        P(("seq", "shard"), None),
        P(("seq", "shard"), None),
        P(("seq", "shard"), None),
        P(("seq", "shard"), None),
        P(("seq", "shard"), None),
        P(("seq", "shard")),
        P(("seq", "shard")),
        P(("seq", "shard")),
        P(("seq", "shard")),
        P(("seq", "shard")),
        P(("seq", "shard")),
        P(("seq", "shard")),
        P(("seq", "shard")),
        P(("seq", "shard")),
    )

    return jax.shard_map(per_device, mesh=mesh, in_specs=in_specs, out_specs=out_specs, check_vma=False)
```

```python
import jax
import jax.numpy as jnp
from jax import lax
from jax.experimental.layout import Layout, with_layout_constraint
from jax.sharding import PartitionSpec as P


DH = 64
LEN = 1024


EPS = 1e-06
NEG = -1e30
ROOT_HALF = 0.7071067811865476
INV_ROOT_TWO_PI = 0.3989422804014327


def contract_rows(left, right):
    return lax.dot_general(
        left, right, (((0,), (0,)), ((), ())), preferred_element_type=jnp.float32
    )


def times_transpose(left, right):
    return lax.dot_general(
        left, right, (((1,), (1,)), ((), ())), preferred_element_type=jnp.float32
    )


def segment_ids(starts, length):
    places = lax.broadcasted_iota(jnp.int32, (1, length, 1), 1)
    return jnp.sum((starts[:, None, :] <= places).astype(jnp.int32), axis=2)


def norm_forward(rows, gain, shift):
    middle = jnp.mean(rows, axis=-1, keepdims=True)
    centred = rows - middle
    spread = jnp.mean(centred * centred, axis=-1, keepdims=True)
    inverse = lax.rsqrt(spread + EPS)
    normed = centred * inverse
    return (normed * gain + shift, normed, inverse)


def norm_backward(upstream, gain, normed, inverse):
    scaled = upstream * gain
    inner = jnp.mean(scaled, axis=-1, keepdims=True)
    along = jnp.mean(scaled * normed, axis=-1, keepdims=True)
    return inverse * (scaled - inner - normed * along)


def gelu_value(value):
    return 0.5 * value * (1.0 + lax.erf(value * ROOT_HALF))


def gelu_slope(value):
    return (
        0.5 * (1.0 + lax.erf(value * ROOT_HALF))
        + value * jnp.exp(-0.5 * value * value) * INV_ROOT_TWO_PI
    )


def masked_scores(queries, keys, seg_rows, seg_all, scale):
    scores = jnp.einsum("qhd,khd->hqk", queries, keys, preferred_element_type=jnp.float32) * scale
    allowed = seg_rows[:, None] == seg_all[None, :]
    return jnp.where(allowed[None], scores, NEG)


def attend_forward(item):
    qkv, segment = item
    queries, keys, values = qkv[:, 0], qkv[:, 1], qkv[:, 2]
    length, heads, depth = queries.shape
    rows = min(512, length)
    blocks = length // rows
    scale = depth ** (-0.5)

    def one(piece):
        block_q, block_seg = piece
        scores = masked_scores(block_q, keys, block_seg, segment, scale)
        highest = jnp.max(scores, axis=-1, keepdims=True)
        raised = jnp.exp(scores - highest)
        total = jnp.sum(raised, axis=-1, keepdims=True)
        weights = (raised / total).astype(jnp.bfloat16)
        context = jnp.einsum("hqk,khd->qhd", weights, values, preferred_element_type=jnp.float32)
        return (context.astype(jnp.bfloat16), (highest + jnp.log(total))[..., 0])

    context, logsum = lax.map(
        one, (queries.reshape(blocks, rows, heads, depth), segment.reshape(blocks, rows))
    )
    return (context.reshape(length, heads, depth), logsum)


def attend_backward(item):
    qkv, segment, logsum, upstream = item
    queries, keys, values = qkv[:, 0], qkv[:, 1], qkv[:, 2]
    length, heads, depth = queries.shape
    rows = min(512, length)
    blocks = length // rows
    scale = depth ** (-0.5)

    def one(carry, piece):
        key_acc, value_acc = carry
        block_q, block_seg, block_sum, block_up = piece
        scores = masked_scores(block_q, keys, block_seg, segment, scale)
        weights = jnp.exp(scores - block_sum[..., None])
        value_acc = value_acc + jnp.einsum(
            "hqk,qhd->khd",
            weights.astype(jnp.bfloat16),
            block_up,
            preferred_element_type=jnp.float32,
        )
        slope = jnp.einsum("qhd,khd->hqk", block_up, values, preferred_element_type=jnp.float32)
        inner = jnp.sum(weights * slope, axis=-1, keepdims=True)
        score_grad = (weights * (slope - inner)).astype(jnp.bfloat16)
        query_grad = (
            jnp.einsum("hqk,khd->qhd", score_grad, keys, preferred_element_type=jnp.float32) * scale
        )
        key_acc = (
            key_acc
            + jnp.einsum("hqk,qhd->khd", score_grad, block_q, preferred_element_type=jnp.float32)
            * scale
        )
        return ((key_acc, value_acc), query_grad.astype(jnp.bfloat16))

    empty = jnp.zeros((length, heads, depth), jnp.float32)
    pieces = (
        queries.reshape(blocks, rows, heads, depth),
        segment.reshape(blocks, rows),
        logsum,
        upstream.reshape(blocks, rows, heads, depth),
    )
    (key_grad, value_grad), query_grad = lax.scan(one, (empty, empty), pieces)
    return jnp.stack(
        [
            query_grad.reshape(length, heads, depth),
            key_grad.astype(jnp.bfloat16),
            value_grad.astype(jnp.bfloat16),
        ],
        axis=1,
    )


def lane_pick(block, index):
    lanes = lax.broadcasted_iota(jnp.int32, block.shape, 1)
    return jnp.sum(jnp.where(lanes == index, block, 0.0), axis=1)


def pack_lanes(pieces):
    pieces = [p.astype(jnp.bfloat16) for p in pieces]
    extra = -sum(p.shape[1] for p in pieces) % 256
    if extra:
        pieces.append(jnp.zeros((pieces[0].shape[0], extra), jnp.bfloat16))
    block = jnp.concatenate(pieces, axis=1)
    return with_layout_constraint(block, Layout(major_to_minor=(0, 1)))


def scatter_two_stage(block):
    outer = lax.axis_size("seq")
    part = lax.psum_scatter(
        block.reshape(outer, block.shape[0] // outer, -1), "shard", scatter_dimension=1, tiled=True
    )
    return lax.psum_scatter(part.reshape(-1, block.shape[1]), "seq", scatter_dimension=0, tiled=True)


def per_device(
    layer_in,
    layer_cotangent,
    doc_starts,
    query_weight,
    key_weight,
    value_weight,
    out_weight,
    up_weight,
    down_weight,
    query_bias,
    value_bias,
    out_bias,
    up_bias,
    down_bias,
    mixer_gain,
    mixer_shift,
    final_gain,
    final_shift,
):
    axes = ("seq", "shard")
    rows, width = query_weight.shape
    ff = up_weight.shape[1]

    def column(vector):
        return vector.reshape(rows, -1)

    first = jnp.concatenate(
        [
            query_weight,
            key_weight,
            value_weight,
            column(query_bias),
            column(value_bias),
            column(out_bias),
            column(down_bias),
            column(mixer_gain),
            column(mixer_shift),
            column(final_gain),
            column(final_shift),
            column(up_bias),
        ],
        axis=1,
    ).astype(jnp.bfloat16)
    second = jnp.concatenate(
        [out_weight, up_weight, down_weight.reshape(rows, -1)], axis=1
    ).astype(jnp.bfloat16)
    full_first = lax.all_gather(first, axes, axis=0, tiled=True)
    full_second = lax.all_gather(second, axes, axis=0, tiled=True)
    model = full_first.shape[0]
    full_qkv = full_first[:, : 3 * width]
    full_out = full_second[:, :width]
    full_up = full_second[:, width : width + ff]
    full_down = full_second[:, width + ff : width + 2 * ff].reshape(ff, width)
    base = 3 * width
    bias_query, bias_value, bias_out, bias_down, gain_mixer, shift_mixer, gain_final, shift_final = (
        full_first[:, base + i].astype(jnp.float32) for i in range(8)
    )
    bias_up = full_first[:, base + 8 :].reshape(ff).astype(jnp.float32)

    streams, part_len, _ = layer_in.shape
    row_count = streams * part_len
    heads = width // DH
    flat = layer_in.reshape(row_count, width)
    qkv_bias = jnp.concatenate([bias_query, jnp.zeros_like(bias_query), bias_value])
    segment = segment_ids(doc_starts, LEN)
    head_qkv, context_parts, logsum = [], [], []
    for s in range(streams):
        qkv = (
            jnp.dot(flat[s * part_len : (s + 1) * part_len], full_qkv, preferred_element_type=jnp.float32)
            + qkv_bias
        ).astype(jnp.bfloat16)
        one_qkv = lax.all_to_all(
            qkv.reshape(part_len, 3, heads, DH), "seq", split_axis=2, concat_axis=0, tiled=True
        )
        context, one_sum = attend_forward((one_qkv, segment[s]))
        context_parts.append(
            lax.all_to_all(context, "seq", split_axis=0, concat_axis=1, tiled=True)
        )
        head_qkv.append(one_qkv)
        logsum.append(one_sum)
    context_rows = jnp.stack(context_parts).reshape(row_count, width)
    attn = jnp.dot(context_rows, full_out, preferred_element_type=jnp.float32) + bias_out
    mixed, normed_mixer, inverse_mixer = norm_forward(
        flat.astype(jnp.float32) + attn, gain_mixer, shift_mixer
    )
    upper = mixed.astype(jnp.bfloat16)
    preact = jnp.dot(upper, full_up, preferred_element_type=jnp.float32) + bias_up
    hidden = gelu_value(preact).astype(jnp.bfloat16)
    ffout = jnp.dot(hidden, full_down, preferred_element_type=jnp.float32) + bias_down
    result, normed_final, inverse_final = norm_forward(mixed + ffout, gain_final, shift_final)
    layer_out = result.astype(jnp.bfloat16).reshape(streams, part_len, width)

    upstream = layer_cotangent.reshape(row_count, width).astype(jnp.float32)
    grad_final_gain = jnp.sum(upstream * normed_final, axis=0)
    grad_final_shift = jnp.sum(upstream, axis=0)
    back_final = norm_backward(upstream, gain_final, normed_final, inverse_final)
    back_ffout = back_final.astype(jnp.bfloat16)
    grad_down_weight = contract_rows(hidden, back_ffout)
    grad_down_bias = jnp.sum(back_ffout.astype(jnp.float32), axis=0)
    back_preact = (times_transpose(back_ffout, full_down) * gelu_slope(preact)).astype(jnp.bfloat16)
    grad_up_weight = contract_rows(upper, back_preact)
    grad_up_bias = jnp.sum(back_preact.astype(jnp.float32), axis=0)
    back_mixed = back_final + times_transpose(back_preact, full_up)
    grad_mixer_gain = jnp.sum(back_mixed * normed_mixer, axis=0)
    grad_mixer_shift = jnp.sum(back_mixed, axis=0)
    back_first = norm_backward(back_mixed, gain_mixer, normed_mixer, inverse_mixer)
    back_attn = back_first.astype(jnp.bfloat16)
    grad_out_weight = contract_rows(context_rows, back_attn)
    grad_out_bias = jnp.sum(back_attn.astype(jnp.float32), axis=0)

    early = pack_lanes(
        [
            grad_out_weight,
            grad_up_weight,
            grad_down_weight.reshape(model, -1),
            grad_out_bias[:, None],
            grad_down_bias[:, None],
            grad_mixer_gain[:, None],
            grad_mixer_shift[:, None],
            grad_final_gain[:, None],
            grad_final_shift[:, None],
            grad_up_bias.reshape(model, -1),
        ]
    )
    early, back_attn = lax.optimization_barrier((early, back_attn))
    early_sum = lax.psum_scatter(early, axes, scatter_dimension=0, tiled=True).astype(jnp.float32)

    back_context = times_transpose(back_attn, full_out).astype(jnp.bfloat16)
    back_parts = []
    for s in range(streams):
        one_back = lax.all_to_all(
            back_context[s * part_len : (s + 1) * part_len].reshape(part_len, heads, DH),
            "seq",
            split_axis=1,
            concat_axis=0,
            tiled=True,
        )
        one_grads = attend_backward((head_qkv[s], segment[s], logsum[s], one_back))
        back_parts.append(lax.all_to_all(one_grads, "seq", split_axis=0, concat_axis=2, tiled=True))
    rows_back = jnp.stack(back_parts).reshape(row_count, 3 * width)
    grad_qkv_weight = contract_rows(flat, rows_back)
    grad_query_bias = jnp.sum(rows_back[:, :width].astype(jnp.float32), axis=0)
    grad_value_bias = jnp.sum(rows_back[:, 2 * width :].astype(jnp.float32), axis=0)
    input_grad = (back_first + times_transpose(rows_back, full_qkv)).reshape(
        streams, part_len, width
    )
    late = pack_lanes([grad_qkv_weight, grad_query_bias[:, None], grad_value_bias[:, None]])
    late_sum = scatter_two_stage(late).astype(jnp.float32)

    base = width + 2 * ff
    late_tail = late_sum[:, 3 * width :]
    early_tail = early_sum[:, base:]
    return (
        layer_out,
        input_grad,
        late_sum[:, :width],
        late_sum[:, width : 2 * width],
        late_sum[:, 2 * width : 3 * width],
        early_sum[:, :width],
        early_sum[:, width : width + ff],
        early_sum[:, width + ff : width + 2 * ff].reshape(-1, width),
        lane_pick(late_tail, 0),
        lane_pick(late_tail, 1),
        lane_pick(early_tail, 0),
        jnp.stack([lane_pick(early_tail, 6 + i) for i in range(ff // width)], axis=1).reshape(-1),
        lane_pick(early_tail, 1),
        lane_pick(early_tail, 2),
        lane_pick(early_tail, 3),
        lane_pick(early_tail, 4),
        lane_pick(early_tail, 5),
    )


def solution(mesh):
    in_specs = (
        P("shard", "seq", None),
        P("shard", "seq", None),
        P("shard", None),
        P(("seq", "shard"), None),
        P(("seq", "shard"), None),
        P(("seq", "shard"), None),
        P(("seq", "shard"), None),
        P(("seq", "shard"), None),
        P(("seq", "shard"), None),
        P(("seq", "shard")),
        P(("seq", "shard")),
        P(("seq", "shard")),
        P(("seq", "shard")),
        P(("seq", "shard")),
        P(("seq", "shard")),
        P(("seq", "shard")),
        P(("seq", "shard")),
        P(("seq", "shard")),
    )
    out_specs = (
        P("shard", "seq", None),
        P("shard", "seq", None),
        P(("seq", "shard"), None),
        P(("seq", "shard"), None),
        P(("seq", "shard"), None),
        P(("seq", "shard"), None),
        P(("seq", "shard"), None),
        P(("seq", "shard"), None),
        P(("seq", "shard")),
        P(("seq", "shard")),
        P(("seq", "shard")),
        P(("seq", "shard")),
        P(("seq", "shard")),
        P(("seq", "shard")),
        P(("seq", "shard")),
        P(("seq", "shard")),
        P(("seq", "shard")),
    )

    return jax.shard_map(per_device, mesh=mesh, in_specs=in_specs, out_specs=out_specs, check_vma=False)
```

```python
import jax
import jax.numpy as jnp
from jax import lax
from jax.experimental import pallas as pl
from jax.experimental.pallas import tpu as pltpu
from jax.experimental.layout import Layout, with_layout_constraint
from jax.sharding import PartitionSpec as P


DH = 64
LEN = 1024


EPS = 1e-06
NEG = -1e30
ROOT_HALF = 0.7071067811865476
INV_ROOT_TWO_PI = 0.3989422804014327


def contract_rows(left, right):
    return lax.dot_general(
        left, right, (((0,), (0,)), ((), ())), preferred_element_type=jnp.float32
    )


def times_transpose(left, right):
    return lax.dot_general(
        left, right, (((1,), (1,)), ((), ())), preferred_element_type=jnp.float32
    )


def segment_ids(starts, length):
    places = lax.broadcasted_iota(jnp.int32, (1, length, 1), 1)
    return jnp.sum((starts[:, None, :] <= places).astype(jnp.int32), axis=2)


def norm_forward(rows, gain, shift):
    middle = jnp.mean(rows, axis=-1, keepdims=True)
    centred = rows - middle
    spread = jnp.mean(centred * centred, axis=-1, keepdims=True)
    inverse = lax.rsqrt(spread + EPS)
    normed = centred * inverse
    return (normed * gain + shift, normed, inverse)


def norm_backward(upstream, gain, normed, inverse):
    scaled = upstream * gain
    inner = jnp.mean(scaled, axis=-1, keepdims=True)
    along = jnp.mean(scaled * normed, axis=-1, keepdims=True)
    return inverse * (scaled - inner - normed * along)


def gelu_value(value):
    return 0.5 * value * (1.0 + lax.erf(value * ROOT_HALF))


def gelu_slope(value):
    return (
        0.5 * (1.0 + lax.erf(value * ROOT_HALF))
        + value * jnp.exp(-0.5 * value * value) * INV_ROOT_TWO_PI
    )


def lane_pick(block, index):
    lanes = lax.broadcasted_iota(jnp.int32, block.shape, 1)
    return jnp.sum(jnp.where(lanes == index, block, 0.0), axis=1)


def pack_lanes(pieces):
    pieces = [p.astype(jnp.bfloat16) for p in pieces]
    extra = -sum(p.shape[1] for p in pieces) % 256
    if extra:
        pieces.append(jnp.zeros((pieces[0].shape[0], extra), jnp.bfloat16))
    block = jnp.concatenate(pieces, axis=1)
    return with_layout_constraint(block, Layout(major_to_minor=(0, 1)))


ROWS_PER_STEP = 256


def attention_forward_kernel(qkv_ref, seg_col_ref, seg_row_ref, ctx_ref, lse_ref):
    length = qkv_ref.shape[0]
    heads = ctx_ref.shape[1] // DH
    scale = DH ** (-0.5)
    seg_row = seg_row_ref[...]
    for h in range(heads):
        keys = qkv_ref[:, pl.ds((heads + h) * DH, DH)]
        values = qkv_ref[:, pl.ds((2 * heads + h) * DH, DH)]
        for c in range(length // ROWS_PER_STEP):
            rows = pl.ds(c * ROWS_PER_STEP, ROWS_PER_STEP)
            queries = qkv_ref[rows, pl.ds(h * DH, DH)]
            scores = times_transpose(queries, keys) * scale
            scores = jnp.where(seg_col_ref[rows, :] == seg_row, scores, NEG)
            highest = jnp.max(scores, axis=-1, keepdims=True)
            raised = jnp.exp(scores - highest)
            total = jnp.sum(raised, axis=-1, keepdims=True)
            weights = (raised / total).astype(jnp.bfloat16)
            context = jnp.dot(weights, values, preferred_element_type=jnp.float32)
            ctx_ref[rows, pl.ds(h * DH, DH)] = context.astype(ctx_ref.dtype)
            lse_ref[rows, pl.ds(h, 1)] = highest + jnp.log(total)


def attention_backward_kernel(qkv_ref, seg_col_ref, seg_row_ref, lse_ref, up_ref, grad_ref):
    length = qkv_ref.shape[0]
    heads = up_ref.shape[1] // DH
    scale = DH ** (-0.5)
    seg_row = seg_row_ref[...]
    for h in range(heads):
        keys = qkv_ref[:, pl.ds((heads + h) * DH, DH)]
        values = qkv_ref[:, pl.ds((2 * heads + h) * DH, DH)]
        key_acc = jnp.zeros((length, DH), jnp.float32)
        value_acc = jnp.zeros((length, DH), jnp.float32)
        for c in range(length // ROWS_PER_STEP):
            rows = pl.ds(c * ROWS_PER_STEP, ROWS_PER_STEP)
            queries = qkv_ref[rows, pl.ds(h * DH, DH)]
            upstream = up_ref[rows, pl.ds(h * DH, DH)]
            scores = times_transpose(queries, keys) * scale
            scores = jnp.where(seg_col_ref[rows, :] == seg_row, scores, NEG)
            weights = jnp.exp(scores - lse_ref[rows, pl.ds(h, 1)])
            value_acc = value_acc + contract_rows(weights.astype(jnp.bfloat16), upstream)
            slope = times_transpose(upstream, values)
            inner = jnp.sum(weights * slope, axis=-1, keepdims=True)
            score_grad = (weights * (slope - inner)).astype(jnp.bfloat16)
            query_grad = jnp.dot(score_grad, keys, preferred_element_type=jnp.float32) * scale
            grad_ref[rows, pl.ds(h * DH, DH)] = query_grad.astype(grad_ref.dtype)
            key_acc = key_acc + contract_rows(score_grad, queries) * scale
        grad_ref[:, pl.ds((heads + h) * DH, DH)] = key_acc.astype(grad_ref.dtype)
        grad_ref[:, pl.ds((2 * heads + h) * DH, DH)] = value_acc.astype(grad_ref.dtype)


def attention_forward(qkv, segment):
    length, width = qkv.shape
    heads = width // (3 * DH)
    flops = 4 * heads * length * length * DH
    return pl.pallas_call(
        attention_forward_kernel,
        out_shape=(
            jax.ShapeDtypeStruct((length, heads * DH), jnp.bfloat16),
            jax.ShapeDtypeStruct((length, heads), jnp.float32),
        ),
        in_specs=[pl.BlockSpec(memory_space=pltpu.VMEM)] * 3,
        out_specs=(pl.BlockSpec(memory_space=pltpu.VMEM),) * 2,
        cost_estimate=pl.CostEstimate(
            flops=flops, transcendentals=heads * length * length, bytes_accessed=3 * length * width
        ),
    )(qkv, segment.reshape(length, 1), segment.reshape(1, length))


def attention_backward(qkv, segment, logsum, upstream):
    length, width = qkv.shape
    heads = width // (3 * DH)
    flops = 10 * heads * length * length * DH
    return pl.pallas_call(
        attention_backward_kernel,
        out_shape=jax.ShapeDtypeStruct((length, width), jnp.bfloat16),
        in_specs=[pl.BlockSpec(memory_space=pltpu.VMEM)] * 5,
        out_specs=pl.BlockSpec(memory_space=pltpu.VMEM),
        cost_estimate=pl.CostEstimate(
            flops=flops, transcendentals=heads * length * length, bytes_accessed=5 * length * width
        ),
    )(qkv, segment.reshape(length, 1), segment.reshape(1, length), logsum, upstream)


def scatter_two_stage(block):
    outer = lax.axis_size("seq")
    part = lax.psum_scatter(
        block.reshape(outer, block.shape[0] // outer, -1), "shard", scatter_dimension=1, tiled=True
    )
    return lax.psum_scatter(part.reshape(-1, block.shape[1]), "seq", scatter_dimension=0, tiled=True)


def per_device(
    layer_in,
    layer_cotangent,
    doc_starts,
    query_weight,
    key_weight,
    value_weight,
    out_weight,
    up_weight,
    down_weight,
    query_bias,
    value_bias,
    out_bias,
    up_bias,
    down_bias,
    mixer_gain,
    mixer_shift,
    final_gain,
    final_shift,
):
    axes = ("seq", "shard")
    rows, width = query_weight.shape
    ff = up_weight.shape[1]

    def column(vector):
        return vector.reshape(rows, -1)

    first = jnp.concatenate(
        [
            query_weight,
            key_weight,
            value_weight,
            column(query_bias),
            column(value_bias),
            column(out_bias),
            column(down_bias),
            column(mixer_gain),
            column(mixer_shift),
            column(final_gain),
            column(final_shift),
            column(up_bias),
        ],
        axis=1,
    ).astype(jnp.bfloat16)
    second = jnp.concatenate(
        [out_weight, up_weight, down_weight.reshape(rows, -1)], axis=1
    ).astype(jnp.bfloat16)
    full_first = lax.all_gather(first, axes, axis=0, tiled=True)
    full_second = lax.all_gather(second, axes, axis=0, tiled=True)
    model = full_first.shape[0]
    full_qkv = full_first[:, : 3 * width]
    full_out = full_second[:, :width]
    full_up = full_second[:, width : width + ff]
    full_down = full_second[:, width + ff : width + 2 * ff].reshape(ff, width)
    base = 3 * width
    bias_query, bias_value, bias_out, bias_down, gain_mixer, shift_mixer, gain_final, shift_final = (
        full_first[:, base + i].astype(jnp.float32) for i in range(8)
    )
    bias_up = full_first[:, base + 8 :].reshape(ff).astype(jnp.float32)

    streams, part_len, _ = layer_in.shape
    row_count = streams * part_len
    heads = width // DH
    flat = layer_in.reshape(row_count, width)
    qkv_bias = jnp.concatenate([bias_query, jnp.zeros_like(bias_query), bias_value])
    segment = segment_ids(doc_starts, LEN)
    head_qkv, context_parts, logsum = [], [], []
    for s in range(streams):
        qkv = (
            jnp.dot(flat[s * part_len : (s + 1) * part_len], full_qkv, preferred_element_type=jnp.float32)
            + qkv_bias
        ).astype(jnp.bfloat16)
        one_qkv = lax.all_to_all(
            qkv.reshape(part_len, 3, heads, DH), "seq", split_axis=2, concat_axis=0, tiled=True
        )
        local_heads = one_qkv.shape[2]
        context, one_sum = attention_forward(one_qkv.reshape(LEN, -1), segment[s])
        context_parts.append(
            lax.all_to_all(
                context.reshape(LEN, local_heads, DH), "seq", split_axis=0, concat_axis=1, tiled=True
            )
        )
        head_qkv.append(one_qkv)
        logsum.append(one_sum)
    context_rows = jnp.stack(context_parts).reshape(row_count, width)
    attn = jnp.dot(context_rows, full_out, preferred_element_type=jnp.float32) + bias_out
    mixed, normed_mixer, inverse_mixer = norm_forward(
        flat.astype(jnp.float32) + attn, gain_mixer, shift_mixer
    )
    upper = mixed.astype(jnp.bfloat16)
    preact = jnp.dot(upper, full_up, preferred_element_type=jnp.float32) + bias_up
    hidden = gelu_value(preact).astype(jnp.bfloat16)
    ffout = jnp.dot(hidden, full_down, preferred_element_type=jnp.float32) + bias_down
    result, normed_final, inverse_final = norm_forward(mixed + ffout, gain_final, shift_final)
    layer_out = result.astype(jnp.bfloat16).reshape(streams, part_len, width)

    upstream = layer_cotangent.reshape(row_count, width).astype(jnp.float32)
    grad_final_gain = jnp.sum(upstream * normed_final, axis=0)
    grad_final_shift = jnp.sum(upstream, axis=0)
    back_final = norm_backward(upstream, gain_final, normed_final, inverse_final)
    back_ffout = back_final.astype(jnp.bfloat16)
    grad_down_weight = contract_rows(hidden, back_ffout)
    grad_down_bias = jnp.sum(back_ffout.astype(jnp.float32), axis=0)
    back_preact = (times_transpose(back_ffout, full_down) * gelu_slope(preact)).astype(jnp.bfloat16)
    grad_up_weight = contract_rows(upper, back_preact)
    grad_up_bias = jnp.sum(back_preact.astype(jnp.float32), axis=0)
    back_mixed = back_final + times_transpose(back_preact, full_up)
    grad_mixer_gain = jnp.sum(back_mixed * normed_mixer, axis=0)
    grad_mixer_shift = jnp.sum(back_mixed, axis=0)
    back_first = norm_backward(back_mixed, gain_mixer, normed_mixer, inverse_mixer)
    back_attn = back_first.astype(jnp.bfloat16)
    grad_out_weight = contract_rows(context_rows, back_attn)
    grad_out_bias = jnp.sum(back_attn.astype(jnp.float32), axis=0)

    early = pack_lanes(
        [
            grad_out_weight,
            grad_up_weight,
            grad_down_weight.reshape(model, -1),
            grad_out_bias[:, None],
            grad_down_bias[:, None],
            grad_mixer_gain[:, None],
            grad_mixer_shift[:, None],
            grad_final_gain[:, None],
            grad_final_shift[:, None],
            grad_up_bias.reshape(model, -1),
        ]
    )
    early, back_attn = lax.optimization_barrier((early, back_attn))
    early_sum = lax.psum_scatter(early, axes, scatter_dimension=0, tiled=True).astype(jnp.float32)

    back_context = times_transpose(back_attn, full_out).astype(jnp.bfloat16)
    back_parts = []
    for s in range(streams):
        one_back = lax.all_to_all(
            back_context[s * part_len : (s + 1) * part_len].reshape(part_len, heads, DH),
            "seq",
            split_axis=1,
            concat_axis=0,
            tiled=True,
        )
        local_heads = one_back.shape[1]
        one_grads = attention_backward(
            head_qkv[s].reshape(LEN, -1), segment[s], logsum[s], one_back.reshape(LEN, -1)
        )
        back_parts.append(
            lax.all_to_all(
                one_grads.reshape(LEN, 3, local_heads, DH), "seq", split_axis=0, concat_axis=2, tiled=True
            )
        )
    rows_back = jnp.stack(back_parts).reshape(row_count, 3 * width)
    grad_qkv_weight = contract_rows(flat, rows_back)
    grad_query_bias = jnp.sum(rows_back[:, :width].astype(jnp.float32), axis=0)
    grad_value_bias = jnp.sum(rows_back[:, 2 * width :].astype(jnp.float32), axis=0)
    input_grad = (back_first + times_transpose(rows_back, full_qkv)).reshape(
        streams, part_len, width
    )
    late = pack_lanes([grad_qkv_weight, grad_query_bias[:, None], grad_value_bias[:, None]])
    late_sum = scatter_two_stage(late).astype(jnp.float32)

    base = width + 2 * ff
    late_tail = late_sum[:, 3 * width :]
    early_tail = early_sum[:, base:]
    return (
        layer_out,
        input_grad,
        late_sum[:, :width],
        late_sum[:, width : 2 * width],
        late_sum[:, 2 * width : 3 * width],
        early_sum[:, :width],
        early_sum[:, width : width + ff],
        early_sum[:, width + ff : width + 2 * ff].reshape(-1, width),
        lane_pick(late_tail, 0),
        lane_pick(late_tail, 1),
        lane_pick(early_tail, 0),
        jnp.stack([lane_pick(early_tail, 6 + i) for i in range(ff // width)], axis=1).reshape(-1),
        lane_pick(early_tail, 1),
        lane_pick(early_tail, 2),
        lane_pick(early_tail, 3),
        lane_pick(early_tail, 4),
        lane_pick(early_tail, 5),
    )


def solution(mesh):
    in_specs = (
        P("shard", "seq", None),
        P("shard", "seq", None),
        P("shard", None),
        P(("seq", "shard"), None),
        P(("seq", "shard"), None),
        P(("seq", "shard"), None),
        P(("seq", "shard"), None),
        P(("seq", "shard"), None),
        P(("seq", "shard"), None),
        P(("seq", "shard")),
        P(("seq", "shard")),
        P(("seq", "shard")),
        P(("seq", "shard")),
        P(("seq", "shard")),
        P(("seq", "shard")),
        P(("seq", "shard")),
        P(("seq", "shard")),
        P(("seq", "shard")),
    )
    out_specs = (
        P("shard", "seq", None),
        P("shard", "seq", None),
        P(("seq", "shard"), None),
        P(("seq", "shard"), None),
        P(("seq", "shard"), None),
        P(("seq", "shard"), None),
        P(("seq", "shard"), None),
        P(("seq", "shard"), None),
        P(("seq", "shard")),
        P(("seq", "shard")),
        P(("seq", "shard")),
        P(("seq", "shard")),
        P(("seq", "shard")),
        P(("seq", "shard")),
        P(("seq", "shard")),
        P(("seq", "shard")),
        P(("seq", "shard")),
    )

    return jax.shard_map(per_device, mesh=mesh, in_specs=in_specs, out_specs=out_specs, check_vma=False)
```

```python
import jax
import jax.numpy as jnp
from jax import lax
from jax.experimental import pallas as pl
from jax.experimental.pallas import tpu as pltpu
from jax.experimental.layout import Layout, with_layout_constraint
from jax.sharding import PartitionSpec as P


DH = 64
LEN = 1024


EPS = 1e-06
NEG = -1e30
ROOT_HALF = 0.7071067811865476
INV_ROOT_TWO_PI = 0.3989422804014327


def contract_rows(left, right):
    return lax.dot_general(
        left, right, (((0,), (0,)), ((), ())), preferred_element_type=jnp.float32
    )


def times_transpose(left, right):
    return lax.dot_general(
        left, right, (((1,), (1,)), ((), ())), preferred_element_type=jnp.float32
    )


def segment_ids(starts, length):
    places = lax.broadcasted_iota(jnp.int32, (1, length, 1), 1)
    return jnp.sum((starts[:, None, :] <= places).astype(jnp.int32), axis=2)


def norm_forward(rows, gain, shift):
    middle = jnp.mean(rows, axis=-1, keepdims=True)
    centred = rows - middle
    spread = jnp.mean(centred * centred, axis=-1, keepdims=True)
    inverse = lax.rsqrt(spread + EPS)
    normed = centred * inverse
    return (normed * gain + shift, normed, inverse)


def norm_backward(upstream, gain, normed, inverse):
    scaled = upstream * gain
    inner = jnp.mean(scaled, axis=-1, keepdims=True)
    along = jnp.mean(scaled * normed, axis=-1, keepdims=True)
    return inverse * (scaled - inner - normed * along)


def gelu_value(value):
    return 0.5 * value * (1.0 + lax.erf(value * ROOT_HALF))


def gelu_slope(value):
    return (
        0.5 * (1.0 + lax.erf(value * ROOT_HALF))
        + value * jnp.exp(-0.5 * value * value) * INV_ROOT_TWO_PI
    )


def lane_pick(block, index):
    lanes = lax.broadcasted_iota(jnp.int32, block.shape, 1)
    return jnp.sum(jnp.where(lanes == index, block, 0.0), axis=1)


def pack_lanes(pieces):
    pieces = [p.astype(jnp.bfloat16) for p in pieces]
    extra = -sum(p.shape[1] for p in pieces) % 256
    if extra:
        pieces.append(jnp.zeros((pieces[0].shape[0], extra), jnp.bfloat16))
    block = jnp.concatenate(pieces, axis=1)
    return with_layout_constraint(block, Layout(major_to_minor=(0, 1)))


ROWS_PER_STEP = 256


def attention_forward_kernel(qkv_ref, seg_col_ref, seg_row_ref, ctx_ref, lse_ref):
    length = qkv_ref.shape[0]
    heads = ctx_ref.shape[1] // DH
    scale = DH ** (-0.5)
    seg_row = seg_row_ref[...]
    for h in range(heads):
        keys = qkv_ref[:, pl.ds((heads + h) * DH, DH)]
        values = qkv_ref[:, pl.ds((2 * heads + h) * DH, DH)]
        for c in range(length // ROWS_PER_STEP):
            rows = pl.ds(c * ROWS_PER_STEP, ROWS_PER_STEP)
            queries = qkv_ref[rows, pl.ds(h * DH, DH)]
            scores = times_transpose(queries, keys) * scale
            scores = jnp.where(seg_col_ref[rows, :] == seg_row, scores, NEG)
            highest = jnp.max(scores, axis=-1, keepdims=True)
            raised = jnp.exp(scores - highest)
            total = jnp.sum(raised, axis=-1, keepdims=True)
            weights = (raised / total).astype(jnp.bfloat16)
            context = jnp.dot(weights, values, preferred_element_type=jnp.float32)
            ctx_ref[rows, pl.ds(h * DH, DH)] = context.astype(ctx_ref.dtype)
            lse_ref[rows, pl.ds(h, 1)] = highest + jnp.log(total)


def attention_backward_kernel(qkv_ref, seg_col_ref, seg_row_ref, lse_ref, up_ref, grad_ref):
    length = qkv_ref.shape[0]
    heads = up_ref.shape[1] // DH
    scale = DH ** (-0.5)
    seg_row = seg_row_ref[...]
    for h in range(heads):
        keys = qkv_ref[:, pl.ds((heads + h) * DH, DH)]
        values = qkv_ref[:, pl.ds((2 * heads + h) * DH, DH)]
        key_acc = jnp.zeros((length, DH), jnp.float32)
        value_acc = jnp.zeros((length, DH), jnp.float32)
        for c in range(length // ROWS_PER_STEP):
            rows = pl.ds(c * ROWS_PER_STEP, ROWS_PER_STEP)
            queries = qkv_ref[rows, pl.ds(h * DH, DH)]
            upstream = up_ref[rows, pl.ds(h * DH, DH)]
            scores = times_transpose(queries, keys) * scale
            scores = jnp.where(seg_col_ref[rows, :] == seg_row, scores, NEG)
            weights = jnp.exp(scores - lse_ref[rows, pl.ds(h, 1)])
            value_acc = value_acc + contract_rows(weights.astype(jnp.bfloat16), upstream)
            slope = times_transpose(upstream, values)
            inner = jnp.sum(weights * slope, axis=-1, keepdims=True)
            score_grad = (weights * (slope - inner)).astype(jnp.bfloat16)
            query_grad = jnp.dot(score_grad, keys, preferred_element_type=jnp.float32) * scale
            grad_ref[rows, pl.ds(h * DH, DH)] = query_grad.astype(grad_ref.dtype)
            key_acc = key_acc + contract_rows(score_grad, queries) * scale
        grad_ref[:, pl.ds((heads + h) * DH, DH)] = key_acc.astype(grad_ref.dtype)
        grad_ref[:, pl.ds((2 * heads + h) * DH, DH)] = value_acc.astype(grad_ref.dtype)


def attention_forward(qkv, segment):
    length, width = qkv.shape
    heads = width // (3 * DH)
    flops = 4 * heads * length * length * DH
    return pl.pallas_call(
        attention_forward_kernel,
        out_shape=(
            jax.ShapeDtypeStruct((length, heads * DH), jnp.bfloat16),
            jax.ShapeDtypeStruct((length, heads), jnp.float32),
        ),
        in_specs=[pl.BlockSpec(memory_space=pltpu.VMEM)] * 3,
        out_specs=(pl.BlockSpec(memory_space=pltpu.VMEM),) * 2,
        cost_estimate=pl.CostEstimate(
            flops=flops, transcendentals=heads * length * length, bytes_accessed=3 * length * width
        ),
    )(qkv, segment.reshape(length, 1), segment.reshape(1, length))


def attention_backward(qkv, segment, logsum, upstream):
    length, width = qkv.shape
    heads = width // (3 * DH)
    flops = 10 * heads * length * length * DH
    return pl.pallas_call(
        attention_backward_kernel,
        out_shape=jax.ShapeDtypeStruct((length, width), jnp.bfloat16),
        in_specs=[pl.BlockSpec(memory_space=pltpu.VMEM)] * 5,
        out_specs=pl.BlockSpec(memory_space=pltpu.VMEM),
        cost_estimate=pl.CostEstimate(
            flops=flops, transcendentals=heads * length * length, bytes_accessed=5 * length * width
        ),
    )(qkv, segment.reshape(length, 1), segment.reshape(1, length), logsum, upstream)


def scatter_two_stage(block):
    outer = lax.axis_size("seq")
    part = lax.psum_scatter(
        block.reshape(outer, block.shape[0] // outer, -1), "shard", scatter_dimension=1, tiled=True
    )
    return lax.psum_scatter(part.reshape(-1, block.shape[1]), "seq", scatter_dimension=0, tiled=True)


def per_device(
    layer_in,
    layer_cotangent,
    doc_starts,
    query_weight,
    key_weight,
    value_weight,
    out_weight,
    up_weight,
    down_weight,
    query_bias,
    value_bias,
    out_bias,
    up_bias,
    down_bias,
    mixer_gain,
    mixer_shift,
    final_gain,
    final_shift,
):
    axes = ("seq", "shard")
    rows, width = query_weight.shape
    ff = up_weight.shape[1]

    def column(vector):
        return vector.reshape(rows, -1)

    first = jnp.concatenate(
        [
            query_weight,
            key_weight,
            value_weight,
            column(query_bias),
            column(value_bias),
            column(out_bias),
            column(down_bias),
            column(mixer_gain),
            column(mixer_shift),
            column(final_gain),
            column(final_shift),
            column(up_bias),
        ],
        axis=1,
    ).astype(jnp.bfloat16)
    second = jnp.concatenate(
        [out_weight, up_weight, down_weight.reshape(rows, -1)], axis=1
    ).astype(jnp.bfloat16)
    full_first = lax.all_gather(first, axes, axis=0, tiled=True)
    full_second = lax.all_gather(second, axes, axis=0, tiled=True)
    model = full_first.shape[0]
    full_qkv = full_first[:, : 3 * width]
    full_out = full_second[:, :width]
    full_up = full_second[:, width : width + ff]
    full_down = full_second[:, width + ff : width + 2 * ff].reshape(ff, width)
    base = 3 * width
    bias_query, bias_value, bias_out, bias_down, gain_mixer, shift_mixer, gain_final, shift_final = (
        full_first[:, base + i].astype(jnp.float32) for i in range(8)
    )
    bias_up = full_first[:, base + 8 :].reshape(ff).astype(jnp.float32)

    streams, part_len, _ = layer_in.shape
    row_count = streams * part_len
    heads = width // DH
    flat = layer_in.reshape(row_count, width)
    qkv_bias = jnp.concatenate([bias_query, jnp.zeros_like(bias_query), bias_value])
    ways = lax.axis_size("seq")
    local_heads = heads // ways

    def by_owner(columns):
        lead = columns.shape[:-1]
        split = columns.reshape(*lead, 3, ways, local_heads * DH)
        return jnp.swapaxes(split, -3, -2).reshape(*lead, 3 * width)

    def by_kind(columns):
        lead = columns.shape[:-1]
        split = columns.reshape(*lead, ways, 3, local_heads * DH)
        return jnp.swapaxes(split, -3, -2).reshape(*lead, 3 * width)

    owner_qkv = by_owner(full_qkv)
    owner_bias = by_owner(qkv_bias)
    segment = segment_ids(doc_starts, LEN)
    head_qkv, context_parts, logsum = [], [], []
    for s in range(streams):
        qkv = (
            jnp.dot(flat[s * part_len : (s + 1) * part_len], owner_qkv, preferred_element_type=jnp.float32)
            + owner_bias
        ).astype(jnp.bfloat16)
        one_qkv = lax.all_to_all(
            qkv.reshape(part_len, ways, -1), "seq", split_axis=1, concat_axis=0, tiled=True
        ).reshape(LEN, -1)
        context, one_sum = attention_forward(one_qkv, segment[s])
        context_parts.append(
            lax.all_to_all(
                context.reshape(LEN, 1, -1), "seq", split_axis=0, concat_axis=1, tiled=True
            )
        )
        head_qkv.append(one_qkv)
        logsum.append(one_sum)
    context_rows = jnp.stack(context_parts).reshape(row_count, width)
    attn = jnp.dot(context_rows, full_out, preferred_element_type=jnp.float32) + bias_out
    mixed, normed_mixer, inverse_mixer = norm_forward(
        flat.astype(jnp.float32) + attn, gain_mixer, shift_mixer
    )
    upper = mixed.astype(jnp.bfloat16)
    preact = jnp.dot(upper, full_up, preferred_element_type=jnp.float32) + bias_up
    hidden = gelu_value(preact).astype(jnp.bfloat16)
    ffout = jnp.dot(hidden, full_down, preferred_element_type=jnp.float32) + bias_down
    result, normed_final, inverse_final = norm_forward(mixed + ffout, gain_final, shift_final)
    layer_out = result.astype(jnp.bfloat16).reshape(streams, part_len, width)

    upstream = layer_cotangent.reshape(row_count, width).astype(jnp.float32)
    grad_final_gain = jnp.sum(upstream * normed_final, axis=0)
    grad_final_shift = jnp.sum(upstream, axis=0)
    back_final = norm_backward(upstream, gain_final, normed_final, inverse_final)
    back_ffout = back_final.astype(jnp.bfloat16)
    grad_down_weight = contract_rows(hidden, back_ffout)
    grad_down_bias = jnp.sum(back_ffout.astype(jnp.float32), axis=0)
    back_preact = (times_transpose(back_ffout, full_down) * gelu_slope(preact)).astype(jnp.bfloat16)
    grad_up_weight = contract_rows(upper, back_preact)
    grad_up_bias = jnp.sum(back_preact.astype(jnp.float32), axis=0)
    back_mixed = back_final + times_transpose(back_preact, full_up)
    grad_mixer_gain = jnp.sum(back_mixed * normed_mixer, axis=0)
    grad_mixer_shift = jnp.sum(back_mixed, axis=0)
    back_first = norm_backward(back_mixed, gain_mixer, normed_mixer, inverse_mixer)
    back_attn = back_first.astype(jnp.bfloat16)
    grad_out_weight = contract_rows(context_rows, back_attn)
    grad_out_bias = jnp.sum(back_attn.astype(jnp.float32), axis=0)

    early = pack_lanes(
        [
            grad_out_weight,
            grad_up_weight,
            grad_down_weight.reshape(model, -1),
            grad_out_bias[:, None],
            grad_down_bias[:, None],
            grad_mixer_gain[:, None],
            grad_mixer_shift[:, None],
            grad_final_gain[:, None],
            grad_final_shift[:, None],
            grad_up_bias.reshape(model, -1),
        ]
    )
    early, back_attn = lax.optimization_barrier((early, back_attn))
    early_sum = lax.psum_scatter(early, axes, scatter_dimension=0, tiled=True).astype(jnp.float32)

    back_context = times_transpose(back_attn, full_out).astype(jnp.bfloat16)
    back_parts = []
    for s in range(streams):
        one_back = lax.all_to_all(
            back_context[s * part_len : (s + 1) * part_len].reshape(part_len, ways, -1),
            "seq",
            split_axis=1,
            concat_axis=0,
            tiled=True,
        ).reshape(LEN, -1)
        one_grads = attention_backward(head_qkv[s], segment[s], logsum[s], one_back)
        back_parts.append(
            lax.all_to_all(
                one_grads.reshape(LEN, 1, -1), "seq", split_axis=0, concat_axis=1, tiled=True
            )
        )
    rows_back = jnp.stack(back_parts).reshape(row_count, 3 * width)
    grad_qkv_weight = by_kind(contract_rows(flat, rows_back))
    grad_qkv_bias = by_kind(jnp.sum(rows_back.astype(jnp.float32), axis=0))
    grad_query_bias = grad_qkv_bias[:width]
    grad_value_bias = grad_qkv_bias[2 * width :]
    input_grad = (back_first + times_transpose(rows_back, owner_qkv)).reshape(
        streams, part_len, width
    )
    late = pack_lanes([grad_qkv_weight, grad_query_bias[:, None], grad_value_bias[:, None]])
    late_sum = scatter_two_stage(late).astype(jnp.float32)

    base = width + 2 * ff
    late_tail = late_sum[:, 3 * width :]
    early_tail = early_sum[:, base:]
    return (
        layer_out,
        input_grad,
        late_sum[:, :width],
        late_sum[:, width : 2 * width],
        late_sum[:, 2 * width : 3 * width],
        early_sum[:, :width],
        early_sum[:, width : width + ff],
        early_sum[:, width + ff : width + 2 * ff].reshape(-1, width),
        lane_pick(late_tail, 0),
        lane_pick(late_tail, 1),
        lane_pick(early_tail, 0),
        jnp.stack([lane_pick(early_tail, 6 + i) for i in range(ff // width)], axis=1).reshape(-1),
        lane_pick(early_tail, 1),
        lane_pick(early_tail, 2),
        lane_pick(early_tail, 3),
        lane_pick(early_tail, 4),
        lane_pick(early_tail, 5),
    )


def solution(mesh):
    in_specs = (
        P("shard", "seq", None),
        P("shard", "seq", None),
        P("shard", None),
        P(("seq", "shard"), None),
        P(("seq", "shard"), None),
        P(("seq", "shard"), None),
        P(("seq", "shard"), None),
        P(("seq", "shard"), None),
        P(("seq", "shard"), None),
        P(("seq", "shard")),
        P(("seq", "shard")),
        P(("seq", "shard")),
        P(("seq", "shard")),
        P(("seq", "shard")),
        P(("seq", "shard")),
        P(("seq", "shard")),
        P(("seq", "shard")),
        P(("seq", "shard")),
    )
    out_specs = (
        P("shard", "seq", None),
        P("shard", "seq", None),
        P(("seq", "shard"), None),
        P(("seq", "shard"), None),
        P(("seq", "shard"), None),
        P(("seq", "shard"), None),
        P(("seq", "shard"), None),
        P(("seq", "shard"), None),
        P(("seq", "shard")),
        P(("seq", "shard")),
        P(("seq", "shard")),
        P(("seq", "shard")),
        P(("seq", "shard")),
        P(("seq", "shard")),
        P(("seq", "shard")),
        P(("seq", "shard")),
        P(("seq", "shard")),
    )

    return jax.shard_map(per_device, mesh=mesh, in_specs=in_specs, out_specs=out_specs, check_vma=False)
```

```python
import jax
import jax.numpy as jnp
from jax import lax
from jax.experimental import pallas as pl
from jax.experimental.pallas import tpu as pltpu
from jax.experimental.layout import Layout, with_layout_constraint
from jax.sharding import PartitionSpec as P


DH = 64
LEN = 1024


EPS = 1e-06
NEG = -1e30
ROOT_HALF = 0.7071067811865476
INV_ROOT_TWO_PI = 0.3989422804014327


def contract_rows(left, right):
    return lax.dot_general(
        left, right, (((0,), (0,)), ((), ())), preferred_element_type=jnp.float32
    )


def times_transpose(left, right):
    return lax.dot_general(
        left, right, (((1,), (1,)), ((), ())), preferred_element_type=jnp.float32
    )


def segment_ids(starts, length):
    places = lax.broadcasted_iota(jnp.int32, (1, length, 1), 1)
    return jnp.sum((starts[:, None, :] <= places).astype(jnp.int32), axis=2)


def norm_forward(rows, gain, shift):
    middle = jnp.mean(rows, axis=-1, keepdims=True)
    centred = rows - middle
    spread = jnp.mean(centred * centred, axis=-1, keepdims=True)
    inverse = lax.rsqrt(spread + EPS)
    normed = centred * inverse
    return (normed * gain + shift, normed, inverse)


def norm_backward(upstream, gain, normed, inverse):
    scaled = upstream * gain
    inner = jnp.mean(scaled, axis=-1, keepdims=True)
    along = jnp.mean(scaled * normed, axis=-1, keepdims=True)
    return inverse * (scaled - inner - normed * along)


def gelu_value(value):
    return 0.5 * value * (1.0 + lax.erf(value * ROOT_HALF))


def gelu_slope(value):
    return (
        0.5 * (1.0 + lax.erf(value * ROOT_HALF))
        + value * jnp.exp(-0.5 * value * value) * INV_ROOT_TWO_PI
    )


def lane_pick(block, index):
    lanes = lax.broadcasted_iota(jnp.int32, block.shape, 1)
    return jnp.sum(jnp.where(lanes == index, block, 0.0), axis=1)


def pack_lanes(pieces):
    pieces = [p.astype(jnp.bfloat16) for p in pieces]
    extra = -sum(p.shape[1] for p in pieces) % 256
    if extra:
        pieces.append(jnp.zeros((pieces[0].shape[0], extra), jnp.bfloat16))
    block = jnp.concatenate(pieces, axis=1)
    return with_layout_constraint(block, Layout(major_to_minor=(0, 1)))


ROWS_PER_STEP = 256


def attention_forward_kernel(qkv_ref, seg_col_ref, seg_row_ref, ctx_ref, lse_ref):
    length = qkv_ref.shape[0]
    heads = ctx_ref.shape[1] // DH
    scale = DH ** (-0.5)
    seg_row = seg_row_ref[...]
    for h in range(heads):
        keys = qkv_ref[:, pl.ds((heads + h) * DH, DH)]
        values = qkv_ref[:, pl.ds((2 * heads + h) * DH, DH)]
        for c in range(length // ROWS_PER_STEP):
            rows = pl.ds(c * ROWS_PER_STEP, ROWS_PER_STEP)
            queries = qkv_ref[rows, pl.ds(h * DH, DH)]
            scores = times_transpose(queries, keys) * scale
            scores = jnp.where(seg_col_ref[rows, :] == seg_row, scores, NEG)
            highest = jnp.max(scores, axis=-1, keepdims=True)
            raised = jnp.exp(scores - highest)
            total = jnp.sum(raised, axis=-1, keepdims=True)
            weights = (raised / total).astype(jnp.bfloat16)
            context = jnp.dot(weights, values, preferred_element_type=jnp.float32)
            ctx_ref[rows, pl.ds(h * DH, DH)] = context.astype(ctx_ref.dtype)
            lse_ref[rows, pl.ds(h, 1)] = highest + jnp.log(total)


def attention_backward_kernel(qkv_ref, seg_col_ref, seg_row_ref, lse_ref, up_ref, grad_ref):
    length = qkv_ref.shape[0]
    heads = up_ref.shape[1] // DH
    scale = DH ** (-0.5)
    seg_row = seg_row_ref[...]
    for h in range(heads):
        keys = qkv_ref[:, pl.ds((heads + h) * DH, DH)]
        values = qkv_ref[:, pl.ds((2 * heads + h) * DH, DH)]
        key_acc = jnp.zeros((length, DH), jnp.float32)
        value_acc = jnp.zeros((length, DH), jnp.float32)
        for c in range(length // ROWS_PER_STEP):
            rows = pl.ds(c * ROWS_PER_STEP, ROWS_PER_STEP)
            queries = qkv_ref[rows, pl.ds(h * DH, DH)]
            upstream = up_ref[rows, pl.ds(h * DH, DH)]
            scores = times_transpose(queries, keys) * scale
            scores = jnp.where(seg_col_ref[rows, :] == seg_row, scores, NEG)
            weights = jnp.exp(scores - lse_ref[rows, pl.ds(h, 1)])
            value_acc = value_acc + contract_rows(weights.astype(jnp.bfloat16), upstream)
            slope = times_transpose(upstream, values)
            inner = jnp.sum(weights * slope, axis=-1, keepdims=True)
            score_grad = (weights * (slope - inner)).astype(jnp.bfloat16)
            query_grad = jnp.dot(score_grad, keys, preferred_element_type=jnp.float32) * scale
            grad_ref[rows, pl.ds(h * DH, DH)] = query_grad.astype(grad_ref.dtype)
            key_acc = key_acc + contract_rows(score_grad, queries) * scale
        grad_ref[:, pl.ds((heads + h) * DH, DH)] = key_acc.astype(grad_ref.dtype)
        grad_ref[:, pl.ds((2 * heads + h) * DH, DH)] = value_acc.astype(grad_ref.dtype)


def attention_forward(qkv, segment):
    length, width = qkv.shape
    heads = width // (3 * DH)
    flops = 4 * heads * length * length * DH
    return pl.pallas_call(
        attention_forward_kernel,
        out_shape=(
            jax.ShapeDtypeStruct((length, heads * DH), jnp.bfloat16),
            jax.ShapeDtypeStruct((length, heads), jnp.float32),
        ),
        in_specs=[pl.BlockSpec(memory_space=pltpu.VMEM)] * 3,
        out_specs=(pl.BlockSpec(memory_space=pltpu.VMEM),) * 2,
        cost_estimate=pl.CostEstimate(
            flops=flops, transcendentals=heads * length * length, bytes_accessed=3 * length * width
        ),
    )(qkv, segment.reshape(length, 1), segment.reshape(1, length))


def attention_backward(qkv, segment, logsum, upstream):
    length, width = qkv.shape
    heads = width // (3 * DH)
    flops = 10 * heads * length * length * DH
    return pl.pallas_call(
        attention_backward_kernel,
        out_shape=jax.ShapeDtypeStruct((length, width), jnp.bfloat16),
        in_specs=[pl.BlockSpec(memory_space=pltpu.VMEM)] * 5,
        out_specs=pl.BlockSpec(memory_space=pltpu.VMEM),
        cost_estimate=pl.CostEstimate(
            flops=flops, transcendentals=heads * length * length, bytes_accessed=5 * length * width
        ),
    )(qkv, segment.reshape(length, 1), segment.reshape(1, length), logsum, upstream)


def scatter_two_stage(block):
    outer = lax.axis_size("seq")
    part = lax.psum_scatter(
        block.reshape(outer, block.shape[0] // outer, -1), "shard", scatter_dimension=1, tiled=True
    )
    return lax.psum_scatter(part.reshape(-1, block.shape[1]), "seq", scatter_dimension=0, tiled=True)


def per_device(
    layer_in,
    layer_cotangent,
    doc_starts,
    query_weight,
    key_weight,
    value_weight,
    out_weight,
    up_weight,
    down_weight,
    query_bias,
    value_bias,
    out_bias,
    up_bias,
    down_bias,
    mixer_gain,
    mixer_shift,
    final_gain,
    final_shift,
):
    axes = ("seq", "shard")
    rows, width = query_weight.shape
    ff = up_weight.shape[1]

    def column(vector):
        return vector.reshape(rows, -1)

    first = jnp.concatenate(
        [
            query_weight,
            key_weight,
            value_weight,
            column(query_bias),
            column(value_bias),
            column(out_bias),
            column(down_bias),
            column(mixer_gain),
            column(mixer_shift),
            column(final_gain),
            column(final_shift),
            column(up_bias),
        ],
        axis=1,
    ).astype(jnp.bfloat16)
    second = jnp.concatenate(
        [out_weight, up_weight, down_weight.reshape(rows, -1)], axis=1
    ).astype(jnp.bfloat16)
    full_first = lax.all_gather(first, axes, axis=0, tiled=True)
    full_second = lax.all_gather(second, axes, axis=0, tiled=True)
    model = full_first.shape[0]
    full_qkv = full_first[:, : 3 * width]
    full_out = full_second[:, :width]
    full_up = full_second[:, width : width + ff]
    full_down = full_second[:, width + ff : width + 2 * ff].reshape(ff, width)
    base = 3 * width
    bias_query, bias_value, bias_out, bias_down, gain_mixer, shift_mixer, gain_final, shift_final = (
        full_first[:, base + i].astype(jnp.float32) for i in range(8)
    )
    bias_up = full_first[:, base + 8 :].reshape(ff).astype(jnp.float32)

    streams, part_len, _ = layer_in.shape
    row_count = streams * part_len
    heads = width // DH
    flat = layer_in.reshape(row_count, width)
    qkv_bias = jnp.concatenate([bias_query, jnp.zeros_like(bias_query), bias_value])
    ways = lax.axis_size("seq")
    local_heads = heads // ways

    def by_owner(columns):
        lead = columns.shape[:-1]
        split = columns.reshape(*lead, 3, ways, local_heads * DH)
        return jnp.swapaxes(split, -3, -2).reshape(*lead, 3 * width)

    def by_kind(columns):
        lead = columns.shape[:-1]
        split = columns.reshape(*lead, ways, 3, local_heads * DH)
        return jnp.swapaxes(split, -3, -2).reshape(*lead, 3 * width)

    owner_qkv = by_owner(full_qkv)
    owner_bias = by_owner(qkv_bias)
    segment = segment_ids(doc_starts, LEN)
    head_qkv, context_parts, logsum = [], [], []
    for s in range(streams):
        qkv = (
            jnp.dot(flat[s * part_len : (s + 1) * part_len], owner_qkv, preferred_element_type=jnp.float32)
            + owner_bias
        ).astype(jnp.bfloat16)
        one_qkv = lax.all_to_all(
            qkv.reshape(part_len, ways, -1), "seq", split_axis=1, concat_axis=0, tiled=True
        ).reshape(LEN, -1)
        context, one_sum = attention_forward(one_qkv, segment[s])
        context_parts.append(
            lax.all_to_all(
                context.reshape(LEN, 1, -1), "seq", split_axis=0, concat_axis=1, tiled=True
            )
        )
        head_qkv.append(one_qkv)
        logsum.append(one_sum)
    context_rows = jnp.stack(context_parts).reshape(row_count, width)
    attn = jnp.dot(context_rows, full_out, preferred_element_type=jnp.float32) + bias_out
    mixed, normed_mixer, inverse_mixer = norm_forward(
        flat.astype(jnp.float32) + attn, gain_mixer, shift_mixer
    )
    upper = mixed.astype(jnp.bfloat16)
    preact = jnp.dot(upper, full_up, preferred_element_type=jnp.float32) + bias_up
    hidden = gelu_value(preact).astype(jnp.bfloat16)
    ffout = jnp.dot(hidden, full_down, preferred_element_type=jnp.float32) + bias_down
    result, normed_final, inverse_final = norm_forward(mixed + ffout, gain_final, shift_final)
    layer_out = result.astype(jnp.bfloat16).reshape(streams, part_len, width)

    upstream = layer_cotangent.reshape(row_count, width).astype(jnp.float32)
    grad_final_gain = jnp.sum(upstream * normed_final, axis=0)
    grad_final_shift = jnp.sum(upstream, axis=0)
    back_final = norm_backward(upstream, gain_final, normed_final, inverse_final)
    back_ffout = back_final.astype(jnp.bfloat16)
    grad_down_weight = contract_rows(hidden, back_ffout)
    grad_down_bias = jnp.sum(back_ffout.astype(jnp.float32), axis=0)
    back_preact = (times_transpose(back_ffout, full_down) * gelu_slope(preact)).astype(jnp.bfloat16)
    grad_up_weight = contract_rows(upper, back_preact)
    grad_up_bias = jnp.sum(back_preact.astype(jnp.float32), axis=0)
    back_mixed = back_final + times_transpose(back_preact, full_up)
    grad_mixer_gain = jnp.sum(back_mixed * normed_mixer, axis=0)
    grad_mixer_shift = jnp.sum(back_mixed, axis=0)
    back_first = norm_backward(back_mixed, gain_mixer, normed_mixer, inverse_mixer)
    back_attn = back_first.astype(jnp.bfloat16)
    grad_out_weight = contract_rows(context_rows, back_attn)
    grad_out_bias = jnp.sum(back_attn.astype(jnp.float32), axis=0)

    early = pack_lanes(
        [
            grad_out_weight,
            grad_up_weight,
            grad_down_weight.reshape(model, -1),
            grad_out_bias[:, None],
            grad_down_bias[:, None],
            grad_mixer_gain[:, None],
            grad_mixer_shift[:, None],
            grad_final_gain[:, None],
            grad_final_shift[:, None],
            grad_up_bias.reshape(model, -1),
        ]
    )
    early, back_attn = lax.optimization_barrier((early, back_attn))
    early_sum = lax.psum_scatter(early, axes, scatter_dimension=0, tiled=True).astype(jnp.float32)

    back_context = times_transpose(back_attn, full_out).astype(jnp.bfloat16)
    back_parts = []
    for s in range(streams):
        one_back = lax.all_to_all(
            back_context[s * part_len : (s + 1) * part_len].reshape(part_len, ways, -1),
            "seq",
            split_axis=1,
            concat_axis=0,
            tiled=True,
        ).reshape(LEN, -1)
        one_grads = attention_backward(head_qkv[s], segment[s], logsum[s], one_back)
        rows = lax.all_to_all(
            one_grads.reshape(LEN, 1, -1), "seq", split_axis=0, concat_axis=1, tiled=True
        ).reshape(part_len, 3 * width)
        block = slice(s * part_len, (s + 1) * part_len)
        weight_part = contract_rows(flat[block], rows)
        bias_part = jnp.sum(rows.astype(jnp.float32), axis=0)
        grad_qkv_weight = weight_part if s == 0 else grad_qkv_weight + weight_part
        grad_qkv_bias = bias_part if s == 0 else grad_qkv_bias + bias_part
        back_parts.append(back_first[block] + times_transpose(rows, owner_qkv))
    input_grad = jnp.stack(back_parts).reshape(streams, part_len, width)
    grad_qkv_bias = by_kind(grad_qkv_bias)
    late = pack_lanes(
        [grad_qkv_weight, grad_qkv_bias[:width, None], grad_qkv_bias[2 * width :, None]]
    )
    late_sum = scatter_two_stage(late).astype(jnp.float32)

    base = width + 2 * ff
    late_tail = late_sum[:, 3 * width :]
    late_weight = by_kind(late_sum[:, : 3 * width])
    early_tail = early_sum[:, base:]
    return (
        layer_out,
        input_grad,
        late_weight[:, :width],
        late_weight[:, width : 2 * width],
        late_weight[:, 2 * width : 3 * width],
        early_sum[:, :width],
        early_sum[:, width : width + ff],
        early_sum[:, width + ff : width + 2 * ff].reshape(-1, width),
        lane_pick(late_tail, 0),
        lane_pick(late_tail, 1),
        lane_pick(early_tail, 0),
        jnp.stack([lane_pick(early_tail, 6 + i) for i in range(ff // width)], axis=1).reshape(-1),
        lane_pick(early_tail, 1),
        lane_pick(early_tail, 2),
        lane_pick(early_tail, 3),
        lane_pick(early_tail, 4),
        lane_pick(early_tail, 5),
    )


def solution(mesh):
    in_specs = (
        P("shard", "seq", None),
        P("shard", "seq", None),
        P("shard", None),
        P(("seq", "shard"), None),
        P(("seq", "shard"), None),
        P(("seq", "shard"), None),
        P(("seq", "shard"), None),
        P(("seq", "shard"), None),
        P(("seq", "shard"), None),
        P(("seq", "shard")),
        P(("seq", "shard")),
        P(("seq", "shard")),
        P(("seq", "shard")),
        P(("seq", "shard")),
        P(("seq", "shard")),
        P(("seq", "shard")),
        P(("seq", "shard")),
        P(("seq", "shard")),
    )
    out_specs = (
        P("shard", "seq", None),
        P("shard", "seq", None),
        P(("seq", "shard"), None),
        P(("seq", "shard"), None),
        P(("seq", "shard"), None),
        P(("seq", "shard"), None),
        P(("seq", "shard"), None),
        P(("seq", "shard"), None),
        P(("seq", "shard")),
        P(("seq", "shard")),
        P(("seq", "shard")),
        P(("seq", "shard")),
        P(("seq", "shard")),
        P(("seq", "shard")),
        P(("seq", "shard")),
        P(("seq", "shard")),
        P(("seq", "shard")),
    )

    return jax.shard_map(per_device, mesh=mesh, in_specs=in_specs, out_specs=out_specs, check_vma=False)
```

```python
import jax
import jax.numpy as jnp
from jax import lax
from jax.experimental import pallas as pl
from jax.experimental.pallas import tpu as pltpu
from jax.experimental.layout import Layout, with_layout_constraint
from jax.sharding import PartitionSpec as P


DH = 64
LEN = 1024


EPS = 1e-06
NEG = -1e30
ROOT_HALF = 0.7071067811865476
INV_ROOT_TWO_PI = 0.3989422804014327


def contract_rows(left, right):
    return lax.dot_general(
        left, right, (((0,), (0,)), ((), ())), preferred_element_type=jnp.float32
    )


def times_transpose(left, right):
    return lax.dot_general(
        left, right, (((1,), (1,)), ((), ())), preferred_element_type=jnp.float32
    )


def segment_ids(starts, length):
    places = lax.broadcasted_iota(jnp.int32, (1, length, 1), 1)
    return jnp.sum((starts[:, None, :] <= places).astype(jnp.int32), axis=2)


def norm_forward(rows, gain, shift):
    middle = jnp.mean(rows, axis=-1, keepdims=True)
    centred = rows - middle
    spread = jnp.mean(centred * centred, axis=-1, keepdims=True)
    inverse = lax.rsqrt(spread + EPS)
    normed = centred * inverse
    return (normed * gain + shift, normed, inverse)


def norm_backward(upstream, gain, normed, inverse):
    scaled = upstream * gain
    inner = jnp.mean(scaled, axis=-1, keepdims=True)
    along = jnp.mean(scaled * normed, axis=-1, keepdims=True)
    return inverse * (scaled - inner - normed * along)


def gelu_value(value):
    return 0.5 * value * (1.0 + lax.erf(value * ROOT_HALF))


def gelu_slope(value):
    return (
        0.5 * (1.0 + lax.erf(value * ROOT_HALF))
        + value * jnp.exp(-0.5 * value * value) * INV_ROOT_TWO_PI
    )


def lane_pick(block, index):
    lanes = lax.broadcasted_iota(jnp.int32, block.shape, 1)
    return jnp.sum(jnp.where(lanes == index, block, 0.0), axis=1)


def pack_lanes(pieces):
    pieces = [p.astype(jnp.bfloat16) for p in pieces]
    extra = -sum(p.shape[1] for p in pieces) % 256
    if extra:
        pieces.append(jnp.zeros((pieces[0].shape[0], extra), jnp.bfloat16))
    block = jnp.concatenate(pieces, axis=1)
    return with_layout_constraint(block, Layout(major_to_minor=(0, 1)))


ROWS_PER_STEP = 256


def attention_forward_kernel(qkv_ref, seg_col_ref, seg_row_ref, ctx_ref, lse_ref):
    length = qkv_ref.shape[0]
    heads = ctx_ref.shape[1] // DH
    scale = DH ** (-0.5)
    seg_row = seg_row_ref[...]
    for h in range(heads):
        keys = qkv_ref[:, pl.ds((heads + h) * DH, DH)]
        values = qkv_ref[:, pl.ds((2 * heads + h) * DH, DH)]

        @pl.loop(0, length // ROWS_PER_STEP)
        def _(c):
            rows = pl.ds(pl.multiple_of(c * ROWS_PER_STEP, ROWS_PER_STEP), ROWS_PER_STEP)
            queries = qkv_ref[rows, pl.ds(h * DH, DH)]
            scores = times_transpose(queries, keys) * scale
            scores = jnp.where(seg_col_ref[rows, :] == seg_row, scores, NEG)
            highest = jnp.max(scores, axis=-1, keepdims=True)
            raised = jnp.exp(scores - highest)
            total = jnp.sum(raised, axis=-1, keepdims=True)
            weights = (raised / total).astype(jnp.bfloat16)
            context = jnp.dot(weights, values, preferred_element_type=jnp.float32)
            ctx_ref[rows, pl.ds(h * DH, DH)] = context.astype(ctx_ref.dtype)
            lse_ref[rows, pl.ds(h, 1)] = highest + jnp.log(total)


def attention_backward_kernel(
    qkv_ref, seg_col_ref, seg_row_ref, lse_ref, up_ref, grad_ref, key_acc_ref, value_acc_ref
):
    length = qkv_ref.shape[0]
    heads = up_ref.shape[1] // DH
    scale = DH ** (-0.5)
    seg_row = seg_row_ref[...]
    for h in range(heads):
        keys = qkv_ref[:, pl.ds((heads + h) * DH, DH)]
        values = qkv_ref[:, pl.ds((2 * heads + h) * DH, DH)]
        key_acc_ref[...] = jnp.zeros_like(key_acc_ref)
        value_acc_ref[...] = jnp.zeros_like(value_acc_ref)

        @pl.loop(0, length // ROWS_PER_STEP)
        def _(c):
            rows = pl.ds(pl.multiple_of(c * ROWS_PER_STEP, ROWS_PER_STEP), ROWS_PER_STEP)
            queries = qkv_ref[rows, pl.ds(h * DH, DH)]
            upstream = up_ref[rows, pl.ds(h * DH, DH)]
            scores = times_transpose(queries, keys) * scale
            scores = jnp.where(seg_col_ref[rows, :] == seg_row, scores, NEG)
            weights = jnp.exp(scores - lse_ref[rows, pl.ds(h, 1)])
            value_acc_ref[...] += contract_rows(weights.astype(jnp.bfloat16), upstream)
            slope = times_transpose(upstream, values)
            inner = jnp.sum(weights * slope, axis=-1, keepdims=True)
            score_grad = (weights * (slope - inner)).astype(jnp.bfloat16)
            query_grad = jnp.dot(score_grad, keys, preferred_element_type=jnp.float32) * scale
            grad_ref[rows, pl.ds(h * DH, DH)] = query_grad.astype(grad_ref.dtype)
            key_acc_ref[...] += contract_rows(score_grad, queries) * scale

        grad_ref[:, pl.ds((heads + h) * DH, DH)] = key_acc_ref[...].astype(grad_ref.dtype)
        grad_ref[:, pl.ds((2 * heads + h) * DH, DH)] = value_acc_ref[...].astype(grad_ref.dtype)


def attention_forward(qkv, segment):
    length, width = qkv.shape
    heads = width // (3 * DH)
    flops = 4 * heads * length * length * DH
    return pl.pallas_call(
        attention_forward_kernel,
        out_shape=(
            jax.ShapeDtypeStruct((length, heads * DH), jnp.bfloat16),
            jax.ShapeDtypeStruct((length, heads), jnp.float32),
        ),
        in_specs=[pl.BlockSpec(memory_space=pltpu.VMEM)] * 3,
        out_specs=(pl.BlockSpec(memory_space=pltpu.VMEM),) * 2,
        cost_estimate=pl.CostEstimate(
            flops=flops, transcendentals=heads * length * length, bytes_accessed=3 * length * width
        ),
    )(qkv, segment.reshape(length, 1), segment.reshape(1, length))


def attention_backward(qkv, segment, logsum, upstream):
    length, width = qkv.shape
    heads = width // (3 * DH)
    flops = 10 * heads * length * length * DH
    return pl.pallas_call(
        attention_backward_kernel,
        out_shape=jax.ShapeDtypeStruct((length, width), jnp.bfloat16),
        in_specs=[pl.BlockSpec(memory_space=pltpu.VMEM)] * 5,
        out_specs=pl.BlockSpec(memory_space=pltpu.VMEM),
        scratch_shapes=[pltpu.VMEM((length, DH), jnp.float32)] * 2,
        cost_estimate=pl.CostEstimate(
            flops=flops, transcendentals=heads * length * length, bytes_accessed=5 * length * width
        ),
    )(qkv, segment.reshape(length, 1), segment.reshape(1, length), logsum, upstream)


def scatter_two_stage(block):
    outer = lax.axis_size("seq")
    part = lax.psum_scatter(
        block.reshape(outer, block.shape[0] // outer, -1), "shard", scatter_dimension=1, tiled=True
    )
    return lax.psum_scatter(part.reshape(-1, block.shape[1]), "seq", scatter_dimension=0, tiled=True)


def per_device(
    layer_in,
    layer_cotangent,
    doc_starts,
    query_weight,
    key_weight,
    value_weight,
    out_weight,
    up_weight,
    down_weight,
    query_bias,
    value_bias,
    out_bias,
    up_bias,
    down_bias,
    mixer_gain,
    mixer_shift,
    final_gain,
    final_shift,
):
    axes = ("seq", "shard")
    rows, width = query_weight.shape
    ff = up_weight.shape[1]

    def column(vector):
        return vector.reshape(rows, -1)

    first = jnp.concatenate(
        [
            query_weight,
            key_weight,
            value_weight,
            column(query_bias),
            column(value_bias),
            column(out_bias),
            column(down_bias),
            column(mixer_gain),
            column(mixer_shift),
            column(final_gain),
            column(final_shift),
            column(up_bias),
        ],
        axis=1,
    ).astype(jnp.bfloat16)
    second = jnp.concatenate(
        [out_weight, up_weight, down_weight.reshape(rows, -1)], axis=1
    ).astype(jnp.bfloat16)
    full_first = lax.all_gather(first, axes, axis=0, tiled=True)
    full_second = lax.all_gather(second, axes, axis=0, tiled=True)
    model = full_first.shape[0]
    full_qkv = full_first[:, : 3 * width]
    full_out = full_second[:, :width]
    full_up = full_second[:, width : width + ff]
    full_down = full_second[:, width + ff : width + 2 * ff].reshape(ff, width)
    base = 3 * width
    bias_query, bias_value, bias_out, bias_down, gain_mixer, shift_mixer, gain_final, shift_final = (
        full_first[:, base + i].astype(jnp.float32) for i in range(8)
    )
    bias_up = full_first[:, base + 8 :].reshape(ff).astype(jnp.float32)

    streams, part_len, _ = layer_in.shape
    row_count = streams * part_len
    heads = width // DH
    flat = layer_in.reshape(row_count, width)
    qkv_bias = jnp.concatenate([bias_query, jnp.zeros_like(bias_query), bias_value])
    segment = segment_ids(doc_starts, LEN)
    head_qkv, context_parts, logsum = [], [], []
    for s in range(streams):
        qkv = (
            jnp.dot(flat[s * part_len : (s + 1) * part_len], full_qkv, preferred_element_type=jnp.float32)
            + qkv_bias
        ).astype(jnp.bfloat16)
        one_qkv = lax.all_to_all(
            qkv.reshape(part_len, 3, heads, DH), "seq", split_axis=2, concat_axis=0, tiled=True
        )
        local_heads = one_qkv.shape[2]
        context, one_sum = attention_forward(one_qkv.reshape(LEN, -1), segment[s])
        context_parts.append(
            lax.all_to_all(
                context.reshape(LEN, local_heads, DH), "seq", split_axis=0, concat_axis=1, tiled=True
            )
        )
        head_qkv.append(one_qkv)
        logsum.append(one_sum)
    context_rows = jnp.stack(context_parts).reshape(row_count, width)
    attn = jnp.dot(context_rows, full_out, preferred_element_type=jnp.float32) + bias_out
    mixed, normed_mixer, inverse_mixer = norm_forward(
        flat.astype(jnp.float32) + attn, gain_mixer, shift_mixer
    )
    upper = mixed.astype(jnp.bfloat16)
    preact = jnp.dot(upper, full_up, preferred_element_type=jnp.float32) + bias_up
    hidden = gelu_value(preact).astype(jnp.bfloat16)
    ffout = jnp.dot(hidden, full_down, preferred_element_type=jnp.float32) + bias_down
    result, normed_final, inverse_final = norm_forward(mixed + ffout, gain_final, shift_final)
    layer_out = result.astype(jnp.bfloat16).reshape(streams, part_len, width)

    upstream = layer_cotangent.reshape(row_count, width).astype(jnp.float32)
    grad_final_gain = jnp.sum(upstream * normed_final, axis=0)
    grad_final_shift = jnp.sum(upstream, axis=0)
    back_final = norm_backward(upstream, gain_final, normed_final, inverse_final)
    back_ffout = back_final.astype(jnp.bfloat16)
    grad_down_weight = contract_rows(hidden, back_ffout)
    grad_down_bias = jnp.sum(back_ffout.astype(jnp.float32), axis=0)
    back_preact = (times_transpose(back_ffout, full_down) * gelu_slope(preact)).astype(jnp.bfloat16)
    grad_up_weight = contract_rows(upper, back_preact)
    grad_up_bias = jnp.sum(back_preact.astype(jnp.float32), axis=0)
    back_mixed = back_final + times_transpose(back_preact, full_up)
    grad_mixer_gain = jnp.sum(back_mixed * normed_mixer, axis=0)
    grad_mixer_shift = jnp.sum(back_mixed, axis=0)
    back_first = norm_backward(back_mixed, gain_mixer, normed_mixer, inverse_mixer)
    back_attn = back_first.astype(jnp.bfloat16)
    grad_out_weight = contract_rows(context_rows, back_attn)
    grad_out_bias = jnp.sum(back_attn.astype(jnp.float32), axis=0)

    early = pack_lanes(
        [
            grad_out_weight,
            grad_up_weight,
            grad_down_weight.reshape(model, -1),
            grad_out_bias[:, None],
            grad_down_bias[:, None],
            grad_mixer_gain[:, None],
            grad_mixer_shift[:, None],
            grad_final_gain[:, None],
            grad_final_shift[:, None],
            grad_up_bias.reshape(model, -1),
        ]
    )
    early, back_attn = lax.optimization_barrier((early, back_attn))
    early_sum = lax.psum_scatter(early, axes, scatter_dimension=0, tiled=True).astype(jnp.float32)

    back_parts = []
    for s in range(streams):
        back_context = times_transpose(
            back_attn[s * part_len : (s + 1) * part_len], full_out
        ).astype(jnp.bfloat16)
        one_back = lax.all_to_all(
            back_context.reshape(part_len, heads, DH),
            "seq",
            split_axis=1,
            concat_axis=0,
            tiled=True,
        )
        local_heads = one_back.shape[1]
        one_grads = attention_backward(
            head_qkv[s].reshape(LEN, -1), segment[s], logsum[s], one_back.reshape(LEN, -1)
        )
        back_parts.append(
            lax.all_to_all(
                one_grads.reshape(LEN, 3, local_heads, DH), "seq", split_axis=0, concat_axis=2, tiled=True
            )
        )
    rows_back = jnp.stack(back_parts).reshape(row_count, 3 * width)
    grad_qkv_weight = contract_rows(flat, rows_back)
    grad_query_bias = jnp.sum(rows_back[:, :width].astype(jnp.float32), axis=0)
    grad_value_bias = jnp.sum(rows_back[:, 2 * width :].astype(jnp.float32), axis=0)
    input_grad = (back_first + times_transpose(rows_back, full_qkv)).reshape(
        streams, part_len, width
    )
    late = pack_lanes([grad_qkv_weight, grad_query_bias[:, None], grad_value_bias[:, None]])
    late_sum = scatter_two_stage(late).astype(jnp.float32)

    base = width + 2 * ff
    late_tail = late_sum[:, 3 * width :]
    early_tail = early_sum[:, base:]
    return (
        layer_out,
        input_grad,
        late_sum[:, :width],
        late_sum[:, width : 2 * width],
        late_sum[:, 2 * width : 3 * width],
        early_sum[:, :width],
        early_sum[:, width : width + ff],
        early_sum[:, width + ff : width + 2 * ff].reshape(-1, width),
        lane_pick(late_tail, 0),
        lane_pick(late_tail, 1),
        lane_pick(early_tail, 0),
        jnp.stack([lane_pick(early_tail, 6 + i) for i in range(ff // width)], axis=1).reshape(-1),
        lane_pick(early_tail, 1),
        lane_pick(early_tail, 2),
        lane_pick(early_tail, 3),
        lane_pick(early_tail, 4),
        lane_pick(early_tail, 5),
    )


def solution(mesh):
    in_specs = (
        P("shard", "seq", None),
        P("shard", "seq", None),
        P("shard", None),
        P(("seq", "shard"), None),
        P(("seq", "shard"), None),
        P(("seq", "shard"), None),
        P(("seq", "shard"), None),
        P(("seq", "shard"), None),
        P(("seq", "shard"), None),
        P(("seq", "shard")),
        P(("seq", "shard")),
        P(("seq", "shard")),
        P(("seq", "shard")),
        P(("seq", "shard")),
        P(("seq", "shard")),
        P(("seq", "shard")),
        P(("seq", "shard")),
        P(("seq", "shard")),
    )
    out_specs = (
        P("shard", "seq", None),
        P("shard", "seq", None),
        P(("seq", "shard"), None),
        P(("seq", "shard"), None),
        P(("seq", "shard"), None),
        P(("seq", "shard"), None),
        P(("seq", "shard"), None),
        P(("seq", "shard"), None),
        P(("seq", "shard")),
        P(("seq", "shard")),
        P(("seq", "shard")),
        P(("seq", "shard")),
        P(("seq", "shard")),
        P(("seq", "shard")),
        P(("seq", "shard")),
        P(("seq", "shard")),
        P(("seq", "shard")),
    )

    return jax.shard_map(per_device, mesh=mesh, in_specs=in_specs, out_specs=out_specs, check_vma=False)
```

```python
import jax
import jax.numpy as jnp
from jax import lax
from jax.experimental import pallas as pl
from jax.experimental.pallas import tpu as pltpu
from jax.experimental.layout import Layout, with_layout_constraint
from jax.sharding import PartitionSpec as P


DH = 64
LEN = 1024


EPS = 1e-06
NEG = -1e30
ROOT_HALF = 0.7071067811865476
INV_ROOT_TWO_PI = 0.3989422804014327


def contract_rows(left, right):
    return lax.dot_general(
        left, right, (((0,), (0,)), ((), ())), preferred_element_type=jnp.float32
    )


def times_transpose(left, right):
    return lax.dot_general(
        left, right, (((1,), (1,)), ((), ())), preferred_element_type=jnp.float32
    )


def segment_ids(starts, length):
    places = lax.broadcasted_iota(jnp.int32, (1, length, 1), 1)
    return jnp.sum((starts[:, None, :] <= places).astype(jnp.int32), axis=2)


def norm_forward(rows, gain, shift):
    middle = jnp.mean(rows, axis=-1, keepdims=True)
    centred = rows - middle
    spread = jnp.mean(centred * centred, axis=-1, keepdims=True)
    inverse = lax.rsqrt(spread + EPS)
    normed = centred * inverse
    return (normed * gain + shift, normed, inverse)


def norm_backward(upstream, gain, normed, inverse):
    scaled = upstream * gain
    inner = jnp.mean(scaled, axis=-1, keepdims=True)
    along = jnp.mean(scaled * normed, axis=-1, keepdims=True)
    return inverse * (scaled - inner - normed * along)


def gelu_value(value):
    return 0.5 * value * (1.0 + lax.erf(value * ROOT_HALF))


def gelu_slope(value):
    return (
        0.5 * (1.0 + lax.erf(value * ROOT_HALF))
        + value * jnp.exp(-0.5 * value * value) * INV_ROOT_TWO_PI
    )


def lane_pick(block, index):
    lanes = lax.broadcasted_iota(jnp.int32, block.shape, 1)
    return jnp.sum(jnp.where(lanes == index, block, 0.0), axis=1)


def pack_lanes(pieces):
    pieces = [p.astype(jnp.bfloat16) for p in pieces]
    extra = -sum(p.shape[1] for p in pieces) % 256
    if extra:
        pieces.append(jnp.zeros((pieces[0].shape[0], extra), jnp.bfloat16))
    block = jnp.concatenate(pieces, axis=1)
    return with_layout_constraint(block, Layout(major_to_minor=(0, 1)))


ROWS_PER_STEP = 256


def attention_forward_kernel(qkv_ref, seg_col_ref, seg_row_ref, ctx_ref, lse_ref):
    length = qkv_ref.shape[0]
    heads = ctx_ref.shape[1] // DH
    scale = DH ** (-0.5)
    seg_row = seg_row_ref[...]
    for h in range(heads):
        keys = qkv_ref[:, pl.ds((heads + h) * DH, DH)]
        values = qkv_ref[:, pl.ds((2 * heads + h) * DH, DH)]
        for c in range(length // ROWS_PER_STEP):
            rows = pl.ds(c * ROWS_PER_STEP, ROWS_PER_STEP)
            queries = qkv_ref[rows, pl.ds(h * DH, DH)]
            scores = times_transpose(queries, keys) * scale
            scores = jnp.where(seg_col_ref[rows, :] == seg_row, scores, NEG)
            highest = jnp.max(scores, axis=-1, keepdims=True)
            raised = jnp.exp(scores - highest)
            total = jnp.sum(raised, axis=-1, keepdims=True)
            weights = (raised / total).astype(jnp.bfloat16)
            context = jnp.dot(weights, values, preferred_element_type=jnp.float32)
            ctx_ref[rows, pl.ds(h * DH, DH)] = context.astype(ctx_ref.dtype)
            lse_ref[rows, pl.ds(h, 1)] = highest + jnp.log(total)


def attention_backward_kernel(qkv_ref, seg_col_ref, seg_row_ref, lse_ref, up_ref, grad_ref):
    length = qkv_ref.shape[0]
    heads = up_ref.shape[1] // DH
    scale = DH ** (-0.5)
    seg_row = seg_row_ref[...]
    for h in range(heads):
        keys = qkv_ref[:, pl.ds((heads + h) * DH, DH)]
        values = qkv_ref[:, pl.ds((2 * heads + h) * DH, DH)]
        key_acc = jnp.zeros((length, DH), jnp.float32)
        value_acc = jnp.zeros((length, DH), jnp.float32)
        for c in range(length // ROWS_PER_STEP):
            rows = pl.ds(c * ROWS_PER_STEP, ROWS_PER_STEP)
            queries = qkv_ref[rows, pl.ds(h * DH, DH)]
            upstream = up_ref[rows, pl.ds(h * DH, DH)]
            scores = times_transpose(queries, keys) * scale
            scores = jnp.where(seg_col_ref[rows, :] == seg_row, scores, NEG)
            weights = jnp.exp(scores - lse_ref[rows, pl.ds(h, 1)])
            value_acc = value_acc + contract_rows(weights.astype(jnp.bfloat16), upstream)
            slope = times_transpose(upstream, values)
            inner = jnp.sum(weights * slope, axis=-1, keepdims=True)
            score_grad = (weights * (slope - inner)).astype(jnp.bfloat16)
            query_grad = jnp.dot(score_grad, keys, preferred_element_type=jnp.float32) * scale
            grad_ref[rows, pl.ds(h * DH, DH)] = query_grad.astype(grad_ref.dtype)
            key_acc = key_acc + contract_rows(score_grad, queries) * scale
        grad_ref[:, pl.ds((heads + h) * DH, DH)] = key_acc.astype(grad_ref.dtype)
        grad_ref[:, pl.ds((2 * heads + h) * DH, DH)] = value_acc.astype(grad_ref.dtype)


def attention_forward(qkv, segment):
    length, width = qkv.shape
    heads = width // (3 * DH)
    flops = 4 * heads * length * length * DH
    return pl.pallas_call(
        attention_forward_kernel,
        out_shape=(
            jax.ShapeDtypeStruct((length, heads * DH), jnp.bfloat16),
            jax.ShapeDtypeStruct((length, heads), jnp.float32),
        ),
        in_specs=[pl.BlockSpec(memory_space=pltpu.VMEM)] * 3,
        out_specs=(pl.BlockSpec(memory_space=pltpu.VMEM),) * 2,
        cost_estimate=pl.CostEstimate(
            flops=flops, transcendentals=heads * length * length, bytes_accessed=3 * length * width
        ),
    )(qkv, segment.reshape(length, 1), segment.reshape(1, length))


def attention_backward(qkv, segment, logsum, upstream):
    length, width = qkv.shape
    heads = width // (3 * DH)
    flops = 10 * heads * length * length * DH
    return pl.pallas_call(
        attention_backward_kernel,
        out_shape=jax.ShapeDtypeStruct((length, width), jnp.bfloat16),
        in_specs=[pl.BlockSpec(memory_space=pltpu.VMEM)] * 5,
        out_specs=pl.BlockSpec(memory_space=pltpu.VMEM),
        cost_estimate=pl.CostEstimate(
            flops=flops, transcendentals=heads * length * length, bytes_accessed=5 * length * width
        ),
    )(qkv, segment.reshape(length, 1), segment.reshape(1, length), logsum, upstream)


def scatter_two_stage(block):
    outer = lax.axis_size("seq")
    part = lax.psum_scatter(
        block.reshape(outer, block.shape[0] // outer, -1), "shard", scatter_dimension=1, tiled=True
    )
    return lax.psum_scatter(part.reshape(-1, block.shape[1]), "seq", scatter_dimension=0, tiled=True)


def per_device(
    layer_in,
    layer_cotangent,
    doc_starts,
    query_weight,
    key_weight,
    value_weight,
    out_weight,
    up_weight,
    down_weight,
    query_bias,
    value_bias,
    out_bias,
    up_bias,
    down_bias,
    mixer_gain,
    mixer_shift,
    final_gain,
    final_shift,
):
    axes = ("seq", "shard")
    rows, width = query_weight.shape
    ff = up_weight.shape[1]

    def column(vector):
        return vector.reshape(rows, -1)

    first = jnp.concatenate(
        [
            query_weight,
            key_weight,
            value_weight,
            column(query_bias),
            column(value_bias),
            column(out_bias),
            column(down_bias),
            column(mixer_gain),
            column(mixer_shift),
            column(final_gain),
            column(final_shift),
            column(up_bias),
        ],
        axis=1,
    ).astype(jnp.bfloat16)
    second = jnp.concatenate(
        [out_weight, up_weight, down_weight.reshape(rows, -1)], axis=1
    ).astype(jnp.bfloat16)
    full_first = lax.all_gather(first, axes, axis=0, tiled=True)
    full_second = lax.all_gather(second, axes, axis=0, tiled=True)
    model = full_first.shape[0]
    full_qkv = full_first[:, : 3 * width]
    full_out = full_second[:, :width]
    full_up = full_second[:, width : width + ff]
    full_down = full_second[:, width + ff : width + 2 * ff].reshape(ff, width)
    base = 3 * width
    bias_query, bias_value, bias_out, bias_down, gain_mixer, shift_mixer, gain_final, shift_final = (
        full_first[:, base + i].astype(jnp.float32) for i in range(8)
    )
    bias_up = full_first[:, base + 8 :].reshape(ff).astype(jnp.float32)

    streams, part_len, _ = layer_in.shape
    row_count = streams * part_len
    heads = width // DH
    flat = layer_in.reshape(row_count, width)
    qkv_bias = jnp.concatenate([bias_query, jnp.zeros_like(bias_query), bias_value])
    segment = segment_ids(doc_starts, LEN)
    head_qkv, context_parts, logsum = [], [], []
    for s in range(streams):
        qkv = (
            jnp.dot(flat[s * part_len : (s + 1) * part_len], full_qkv, preferred_element_type=jnp.float32)
            + qkv_bias
        ).astype(jnp.bfloat16)
        one_qkv = lax.all_to_all(
            qkv.reshape(part_len, 3, heads, DH), "seq", split_axis=2, concat_axis=0, tiled=True
        )
        local_heads = one_qkv.shape[2]
        context, one_sum = attention_forward(one_qkv.reshape(LEN, -1), segment[s])
        context_parts.append(
            lax.all_to_all(
                context.reshape(LEN, local_heads, DH), "seq", split_axis=0, concat_axis=1, tiled=True
            )
        )
        head_qkv.append(one_qkv)
        logsum.append(one_sum)
    context_rows = jnp.stack(context_parts).reshape(row_count, width)
    attn = jnp.dot(context_rows, full_out, preferred_element_type=jnp.float32) + bias_out
    mixed, normed_mixer, inverse_mixer = norm_forward(
        flat.astype(jnp.float32) + attn, gain_mixer, shift_mixer
    )
    upper = mixed.astype(jnp.bfloat16)
    preact = jnp.dot(upper, full_up, preferred_element_type=jnp.float32) + bias_up
    hidden = gelu_value(preact).astype(jnp.bfloat16)
    ffout = jnp.dot(hidden, full_down, preferred_element_type=jnp.float32) + bias_down
    result, normed_final, inverse_final = norm_forward(mixed + ffout, gain_final, shift_final)
    layer_out = result.astype(jnp.bfloat16).reshape(streams, part_len, width)

    upstream = layer_cotangent.reshape(row_count, width).astype(jnp.float32)
    grad_final_gain = jnp.sum(upstream * normed_final, axis=0)
    grad_final_shift = jnp.sum(upstream, axis=0)
    back_final = norm_backward(upstream, gain_final, normed_final, inverse_final)
    back_ffout = back_final.astype(jnp.bfloat16)
    grad_down_weight = contract_rows(hidden, back_ffout)
    grad_down_bias = jnp.sum(back_ffout.astype(jnp.float32), axis=0)
    back_preact = (times_transpose(back_ffout, full_down) * gelu_slope(preact)).astype(jnp.bfloat16)
    grad_up_weight = contract_rows(upper, back_preact)
    grad_up_bias = jnp.sum(back_preact.astype(jnp.float32), axis=0)
    back_mixed = back_final + times_transpose(back_preact, full_up)
    grad_mixer_gain = jnp.sum(back_mixed * normed_mixer, axis=0)
    grad_mixer_shift = jnp.sum(back_mixed, axis=0)
    back_first = norm_backward(back_mixed, gain_mixer, normed_mixer, inverse_mixer)
    back_attn = back_first.astype(jnp.bfloat16)
    grad_out_weight = contract_rows(context_rows, back_attn)
    grad_out_bias = jnp.sum(back_attn.astype(jnp.float32), axis=0)

    early = pack_lanes(
        [
            grad_out_weight,
            grad_up_weight,
            grad_down_weight.reshape(model, -1),
            grad_out_bias[:, None],
            grad_down_bias[:, None],
            grad_mixer_gain[:, None],
            grad_mixer_shift[:, None],
            grad_final_gain[:, None],
            grad_final_shift[:, None],
            grad_up_bias.reshape(model, -1),
        ]
    )
    early, back_attn = lax.optimization_barrier((early, back_attn))
    early_sum = lax.psum_scatter(early, axes, scatter_dimension=0, tiled=True).astype(jnp.float32)

    back_parts = []
    for s in range(streams):
        back_context = times_transpose(
            back_attn[s * part_len : (s + 1) * part_len], full_out
        ).astype(jnp.bfloat16)
        one_back = lax.all_to_all(
            back_context.reshape(part_len, heads, DH),
            "seq",
            split_axis=1,
            concat_axis=0,
            tiled=True,
        )
        local_heads = one_back.shape[1]
        one_grads = attention_backward(
            head_qkv[s].reshape(LEN, -1), segment[s], logsum[s], one_back.reshape(LEN, -1)
        )
        back_parts.append(
            lax.all_to_all(
                one_grads.reshape(LEN, 3, local_heads, DH), "seq", split_axis=0, concat_axis=2, tiled=True
            )
        )
    rows_back = jnp.stack(back_parts).reshape(row_count, 3 * width)
    grad_qkv_weight = contract_rows(flat, rows_back)
    grad_query_bias = jnp.sum(rows_back[:, :width].astype(jnp.float32), axis=0)
    grad_value_bias = jnp.sum(rows_back[:, 2 * width :].astype(jnp.float32), axis=0)
    input_grad = (back_first + times_transpose(rows_back, full_qkv)).reshape(
        streams, part_len, width
    )
    late = pack_lanes([grad_qkv_weight, grad_query_bias[:, None], grad_value_bias[:, None]])
    late_sum = scatter_two_stage(late).astype(jnp.float32)

    base = width + 2 * ff
    late_tail = late_sum[:, 3 * width :]
    early_tail = early_sum[:, base:]
    return (
        layer_out,
        input_grad,
        late_sum[:, :width],
        late_sum[:, width : 2 * width],
        late_sum[:, 2 * width : 3 * width],
        early_sum[:, :width],
        early_sum[:, width : width + ff],
        early_sum[:, width + ff : width + 2 * ff].reshape(-1, width),
        lane_pick(late_tail, 0),
        lane_pick(late_tail, 1),
        lane_pick(early_tail, 0),
        jnp.stack([lane_pick(early_tail, 6 + i) for i in range(ff // width)], axis=1).reshape(-1),
        lane_pick(early_tail, 1),
        lane_pick(early_tail, 2),
        lane_pick(early_tail, 3),
        lane_pick(early_tail, 4),
        lane_pick(early_tail, 5),
    )


def solution(mesh):
    in_specs = (
        P("shard", "seq", None),
        P("shard", "seq", None),
        P("shard", None),
        P(("seq", "shard"), None),
        P(("seq", "shard"), None),
        P(("seq", "shard"), None),
        P(("seq", "shard"), None),
        P(("seq", "shard"), None),
        P(("seq", "shard"), None),
        P(("seq", "shard")),
        P(("seq", "shard")),
        P(("seq", "shard")),
        P(("seq", "shard")),
        P(("seq", "shard")),
        P(("seq", "shard")),
        P(("seq", "shard")),
        P(("seq", "shard")),
        P(("seq", "shard")),
    )
    out_specs = (
        P("shard", "seq", None),
        P("shard", "seq", None),
        P(("seq", "shard"), None),
        P(("seq", "shard"), None),
        P(("seq", "shard"), None),
        P(("seq", "shard"), None),
        P(("seq", "shard"), None),
        P(("seq", "shard"), None),
        P(("seq", "shard")),
        P(("seq", "shard")),
        P(("seq", "shard")),
        P(("seq", "shard")),
        P(("seq", "shard")),
        P(("seq", "shard")),
        P(("seq", "shard")),
        P(("seq", "shard")),
        P(("seq", "shard")),
    )

    return jax.shard_map(per_device, mesh=mesh, in_specs=in_specs, out_specs=out_specs, check_vma=False)
```

```python
import jax
import jax.numpy as jnp
from jax import lax
from jax.experimental import pallas as pl
from jax.experimental.pallas import tpu as pltpu
from jax.experimental.layout import Layout, with_layout_constraint
from jax.sharding import PartitionSpec as P


DH = 64
LEN = 1024


EPS = 1e-06
NEG = -1e30
ROOT_HALF = 0.7071067811865476
INV_ROOT_TWO_PI = 0.3989422804014327


def contract_rows(left, right):
    return lax.dot_general(
        left, right, (((0,), (0,)), ((), ())), preferred_element_type=jnp.float32
    )


def times_transpose(left, right):
    return lax.dot_general(
        left, right, (((1,), (1,)), ((), ())), preferred_element_type=jnp.float32
    )


def segment_ids(starts, length):
    places = lax.broadcasted_iota(jnp.int32, (1, length, 1), 1)
    return jnp.sum((starts[:, None, :] <= places).astype(jnp.int32), axis=2)


def norm_forward(rows, gain, shift):
    middle = jnp.mean(rows, axis=-1, keepdims=True)
    centred = rows - middle
    spread = jnp.mean(centred * centred, axis=-1, keepdims=True)
    inverse = lax.rsqrt(spread + EPS)
    normed = centred * inverse
    return (normed * gain + shift, normed, inverse)


def norm_backward(upstream, gain, normed, inverse):
    scaled = upstream * gain
    inner = jnp.mean(scaled, axis=-1, keepdims=True)
    along = jnp.mean(scaled * normed, axis=-1, keepdims=True)
    return inverse * (scaled - inner - normed * along)


def gelu_value(value):
    return 0.5 * value * (1.0 + lax.erf(value * ROOT_HALF))


def gelu_slope(value):
    return (
        0.5 * (1.0 + lax.erf(value * ROOT_HALF))
        + value * jnp.exp(-0.5 * value * value) * INV_ROOT_TWO_PI
    )


def lane_pick(block, index):
    lanes = lax.broadcasted_iota(jnp.int32, block.shape, 1)
    return jnp.sum(jnp.where(lanes == index, block, 0.0), axis=1)


def pack_lanes(pieces):
    pieces = [p.astype(jnp.bfloat16) for p in pieces]
    extra = -sum(p.shape[1] for p in pieces) % 256
    if extra:
        pieces.append(jnp.zeros((pieces[0].shape[0], extra), jnp.bfloat16))
    block = jnp.concatenate(pieces, axis=1)
    return with_layout_constraint(block, Layout(major_to_minor=(0, 1)))


ROWS_PER_STEP = 256


def attention_forward_kernel(qkv_ref, seg_col_ref, seg_row_ref, ctx_ref, lse_ref):
    length = qkv_ref.shape[0]
    heads = ctx_ref.shape[1] // DH
    scale = DH ** (-0.5)
    seg_row = seg_row_ref[...]
    for h in range(heads):
        keys = qkv_ref[:, pl.ds((heads + h) * DH, DH)]
        values = qkv_ref[:, pl.ds((2 * heads + h) * DH, DH)]
        for c in range(length // ROWS_PER_STEP):
            rows = pl.ds(c * ROWS_PER_STEP, ROWS_PER_STEP)
            queries = qkv_ref[rows, pl.ds(h * DH, DH)]
            scores = times_transpose(queries, keys) * scale
            scores = jnp.where(seg_col_ref[rows, :] == seg_row, scores, NEG)
            highest = jnp.max(scores, axis=-1, keepdims=True)
            raised = jnp.exp(scores - highest)
            total = jnp.sum(raised, axis=-1, keepdims=True)
            weights = (raised / total).astype(jnp.bfloat16)
            context = jnp.dot(weights, values, preferred_element_type=jnp.float32)
            ctx_ref[rows, pl.ds(h * DH, DH)] = context.astype(ctx_ref.dtype)
            lse_ref[rows, pl.ds(h, 1)] = highest + jnp.log(total)


def attention_backward_kernel(qkv_ref, seg_col_ref, seg_row_ref, lse_ref, up_ref, grad_ref):
    length = qkv_ref.shape[0]
    heads = up_ref.shape[1] // DH
    scale = DH ** (-0.5)
    seg_row = seg_row_ref[...]
    for h in range(heads):
        keys = qkv_ref[:, pl.ds((heads + h) * DH, DH)]
        values = qkv_ref[:, pl.ds((2 * heads + h) * DH, DH)]
        key_acc = jnp.zeros((length, DH), jnp.float32)
        value_acc = jnp.zeros((length, DH), jnp.float32)
        for c in range(length // ROWS_PER_STEP):
            rows = pl.ds(c * ROWS_PER_STEP, ROWS_PER_STEP)
            queries = qkv_ref[rows, pl.ds(h * DH, DH)]
            upstream = up_ref[rows, pl.ds(h * DH, DH)]
            scores = times_transpose(queries, keys) * scale
            scores = jnp.where(seg_col_ref[rows, :] == seg_row, scores, NEG)
            weights = jnp.exp(scores - lse_ref[rows, pl.ds(h, 1)])
            value_acc = value_acc + contract_rows(weights.astype(jnp.bfloat16), upstream)
            slope = times_transpose(upstream, values)
            inner = jnp.sum(weights * slope, axis=-1, keepdims=True)
            score_grad = (weights * (slope - inner)).astype(jnp.bfloat16)
            query_grad = jnp.dot(score_grad, keys, preferred_element_type=jnp.float32) * scale
            grad_ref[rows, pl.ds(h * DH, DH)] = query_grad.astype(grad_ref.dtype)
            key_acc = key_acc + contract_rows(score_grad, queries) * scale
        grad_ref[:, pl.ds((heads + h) * DH, DH)] = key_acc.astype(grad_ref.dtype)
        grad_ref[:, pl.ds((2 * heads + h) * DH, DH)] = value_acc.astype(grad_ref.dtype)


def attention_forward(qkv, segment):
    length, width = qkv.shape
    heads = width // (3 * DH)
    flops = 4 * heads * length * length * DH
    return pl.pallas_call(
        attention_forward_kernel,
        out_shape=(
            jax.ShapeDtypeStruct((length, heads * DH), jnp.bfloat16),
            jax.ShapeDtypeStruct((length, heads), jnp.float32),
        ),
        in_specs=[pl.BlockSpec(memory_space=pltpu.VMEM)] * 3,
        out_specs=(pl.BlockSpec(memory_space=pltpu.VMEM),) * 2,
        cost_estimate=pl.CostEstimate(
            flops=flops, transcendentals=heads * length * length, bytes_accessed=3 * length * width
        ),
    )(qkv, segment.reshape(length, 1), segment.reshape(1, length))


def attention_backward(qkv, segment, logsum, upstream):
    length, width = qkv.shape
    heads = width // (3 * DH)
    flops = 10 * heads * length * length * DH
    return pl.pallas_call(
        attention_backward_kernel,
        out_shape=jax.ShapeDtypeStruct((length, width), jnp.bfloat16),
        in_specs=[pl.BlockSpec(memory_space=pltpu.VMEM)] * 5,
        out_specs=pl.BlockSpec(memory_space=pltpu.VMEM),
        cost_estimate=pl.CostEstimate(
            flops=flops, transcendentals=heads * length * length, bytes_accessed=5 * length * width
        ),
    )(qkv, segment.reshape(length, 1), segment.reshape(1, length), logsum, upstream)


def scatter_two_stage(block):
    outer = lax.axis_size("seq")
    part = lax.psum_scatter(
        block.reshape(outer, block.shape[0] // outer, -1), "shard", scatter_dimension=1, tiled=True
    )
    return lax.psum_scatter(part.reshape(-1, block.shape[1]), "seq", scatter_dimension=0, tiled=True)


def per_device(
    layer_in,
    layer_cotangent,
    doc_starts,
    query_weight,
    key_weight,
    value_weight,
    out_weight,
    up_weight,
    down_weight,
    query_bias,
    value_bias,
    out_bias,
    up_bias,
    down_bias,
    mixer_gain,
    mixer_shift,
    final_gain,
    final_shift,
):
    axes = ("seq", "shard")
    rows, width = query_weight.shape
    ff = up_weight.shape[1]

    def column(vector):
        return vector.reshape(rows, -1)

    first = jnp.concatenate(
        [
            query_weight,
            key_weight,
            value_weight,
            column(query_bias),
            column(value_bias),
            column(out_bias),
            column(down_bias),
            column(mixer_gain),
            column(mixer_shift),
            column(final_gain),
            column(final_shift),
            column(up_bias),
        ],
        axis=1,
    ).astype(jnp.bfloat16)
    second = jnp.concatenate(
        [out_weight, up_weight, down_weight.reshape(rows, -1)], axis=1
    ).astype(jnp.bfloat16)
    full_first = lax.all_gather(first, axes, axis=0, tiled=True)
    full_second = lax.all_gather(second, axes, axis=0, tiled=True)
    model = full_first.shape[0]
    full_qkv = full_first[:, : 3 * width]
    full_out = full_second[:, :width]
    full_up = full_second[:, width : width + ff]
    full_down = full_second[:, width + ff : width + 2 * ff].reshape(ff, width)
    base = 3 * width
    bias_query, bias_value, bias_out, bias_down, gain_mixer, shift_mixer, gain_final, shift_final = (
        full_first[:, base + i].astype(jnp.float32) for i in range(8)
    )
    bias_up = full_first[:, base + 8 :].reshape(ff).astype(jnp.float32)

    streams, part_len, _ = layer_in.shape
    row_count = streams * part_len
    heads = width // DH
    flat = layer_in.reshape(row_count, width)
    qkv_bias = jnp.concatenate([bias_query, jnp.zeros_like(bias_query), bias_value])
    segment = segment_ids(doc_starts, LEN)
    head_qkv, context_parts, logsum = [], [], []
    for s in range(streams):
        qkv = (
            jnp.dot(flat[s * part_len : (s + 1) * part_len], full_qkv, preferred_element_type=jnp.float32)
            + qkv_bias
        ).astype(jnp.bfloat16)
        one_qkv = lax.all_to_all(
            qkv.reshape(part_len, 3, heads, DH), "seq", split_axis=2, concat_axis=0, tiled=True
        )
        local_heads = one_qkv.shape[2]
        context, one_sum = attention_forward(one_qkv.reshape(LEN, -1), segment[s])
        context_parts.append(
            lax.all_to_all(
                context.reshape(LEN, local_heads, DH), "seq", split_axis=0, concat_axis=1, tiled=True
            )
        )
        head_qkv.append(one_qkv)
        logsum.append(one_sum)
    context_rows = jnp.stack(context_parts).reshape(row_count, width)
    attn = jnp.dot(context_rows, full_out, preferred_element_type=jnp.float32) + bias_out
    mixed, normed_mixer, inverse_mixer = norm_forward(
        flat.astype(jnp.float32) + attn, gain_mixer, shift_mixer
    )
    upper = mixed.astype(jnp.bfloat16)
    preact = jnp.dot(upper, full_up, preferred_element_type=jnp.float32) + bias_up
    hidden = gelu_value(preact).astype(jnp.bfloat16)
    ffout = jnp.dot(hidden, full_down, preferred_element_type=jnp.float32) + bias_down
    result, normed_final, inverse_final = norm_forward(mixed + ffout, gain_final, shift_final)
    layer_out = result.astype(jnp.bfloat16).reshape(streams, part_len, width)

    upstream = layer_cotangent.reshape(row_count, width).astype(jnp.float32)
    grad_final_gain = jnp.sum(upstream * normed_final, axis=0)
    grad_final_shift = jnp.sum(upstream, axis=0)
    back_final = norm_backward(upstream, gain_final, normed_final, inverse_final)
    back_ffout = back_final.astype(jnp.bfloat16)
    grad_down_weight = contract_rows(hidden, back_ffout)
    grad_down_bias = jnp.sum(back_ffout.astype(jnp.float32), axis=0)
    back_preact = (times_transpose(back_ffout, full_down) * gelu_slope(preact)).astype(jnp.bfloat16)
    grad_up_weight = contract_rows(upper, back_preact)
    grad_up_bias = jnp.sum(back_preact.astype(jnp.float32), axis=0)
    back_mixed = back_final + times_transpose(back_preact, full_up)
    grad_mixer_gain = jnp.sum(back_mixed * normed_mixer, axis=0)
    grad_mixer_shift = jnp.sum(back_mixed, axis=0)
    back_first = norm_backward(back_mixed, gain_mixer, normed_mixer, inverse_mixer)
    back_attn = back_first.astype(jnp.bfloat16)
    grad_out_weight = contract_rows(context_rows, back_attn)
    grad_out_bias = jnp.sum(back_attn.astype(jnp.float32), axis=0)

    early = pack_lanes(
        [
            grad_out_weight,
            grad_up_weight,
            grad_down_weight.reshape(model, -1),
            grad_out_bias[:, None],
            grad_down_bias[:, None],
            grad_mixer_gain[:, None],
            grad_mixer_shift[:, None],
            grad_final_gain[:, None],
            grad_final_shift[:, None],
            grad_up_bias.reshape(model, -1),
        ]
    )
    early, back_attn = lax.optimization_barrier((early, back_attn))
    early_sum = lax.psum_scatter(early, axes, scatter_dimension=0, tiled=True).astype(jnp.float32)

    input_parts = [None] * streams
    weight_acc, bias_acc = [None, None], [None, None]
    for s in range(streams):
        block = slice(s * part_len, (s + 1) * part_len)
        back_context = times_transpose(back_attn[block], full_out).astype(jnp.bfloat16)
        one_back = lax.all_to_all(
            back_context.reshape(part_len, heads, DH),
            "seq",
            split_axis=1,
            concat_axis=0,
            tiled=True,
        )
        if s >= 2:
            one_back, input_parts[s - 2], weight_acc[s % 2], bias_acc[s % 2] = (
                lax.optimization_barrier(
                    (one_back, input_parts[s - 2], weight_acc[s % 2], bias_acc[s % 2])
                )
            )
        local_heads = one_back.shape[1]
        one_grads = attention_backward(
            head_qkv[s].reshape(LEN, -1), segment[s], logsum[s], one_back.reshape(LEN, -1)
        )
        rows = lax.all_to_all(
            one_grads.reshape(LEN, 3, local_heads, DH), "seq", split_axis=0, concat_axis=2, tiled=True
        ).reshape(part_len, 3 * width)
        weight_part = contract_rows(flat[block], rows)
        bias_part = jnp.sum(rows.astype(jnp.float32), axis=0)
        if s < 2:
            weight_acc[s], bias_acc[s] = weight_part, bias_part
        else:
            weight_acc[s % 2] = weight_acc[s % 2] + weight_part
            bias_acc[s % 2] = bias_acc[s % 2] + bias_part
        input_parts[s] = back_first[block] + times_transpose(rows, full_qkv)
    grad_qkv_weight = weight_acc[0] + weight_acc[1] if streams > 1 else weight_acc[0]
    grad_qkv_bias = bias_acc[0] + bias_acc[1] if streams > 1 else bias_acc[0]
    grad_query_bias = grad_qkv_bias[:width]
    grad_value_bias = grad_qkv_bias[2 * width :]
    input_grad = jnp.stack(input_parts).reshape(streams, part_len, width)
    late = pack_lanes([grad_qkv_weight, grad_query_bias[:, None], grad_value_bias[:, None]])
    late_sum = scatter_two_stage(late).astype(jnp.float32)

    base = width + 2 * ff
    late_tail = late_sum[:, 3 * width :]
    early_tail = early_sum[:, base:]
    return (
        layer_out,
        input_grad,
        late_sum[:, :width],
        late_sum[:, width : 2 * width],
        late_sum[:, 2 * width : 3 * width],
        early_sum[:, :width],
        early_sum[:, width : width + ff],
        early_sum[:, width + ff : width + 2 * ff].reshape(-1, width),
        lane_pick(late_tail, 0),
        lane_pick(late_tail, 1),
        lane_pick(early_tail, 0),
        jnp.stack([lane_pick(early_tail, 6 + i) for i in range(ff // width)], axis=1).reshape(-1),
        lane_pick(early_tail, 1),
        lane_pick(early_tail, 2),
        lane_pick(early_tail, 3),
        lane_pick(early_tail, 4),
        lane_pick(early_tail, 5),
    )


def solution(mesh):
    in_specs = (
        P("shard", "seq", None),
        P("shard", "seq", None),
        P("shard", None),
        P(("seq", "shard"), None),
        P(("seq", "shard"), None),
        P(("seq", "shard"), None),
        P(("seq", "shard"), None),
        P(("seq", "shard"), None),
        P(("seq", "shard"), None),
        P(("seq", "shard")),
        P(("seq", "shard")),
        P(("seq", "shard")),
        P(("seq", "shard")),
        P(("seq", "shard")),
        P(("seq", "shard")),
        P(("seq", "shard")),
        P(("seq", "shard")),
        P(("seq", "shard")),
    )
    out_specs = (
        P("shard", "seq", None),
        P("shard", "seq", None),
        P(("seq", "shard"), None),
        P(("seq", "shard"), None),
        P(("seq", "shard"), None),
        P(("seq", "shard"), None),
        P(("seq", "shard"), None),
        P(("seq", "shard"), None),
        P(("seq", "shard")),
        P(("seq", "shard")),
        P(("seq", "shard")),
        P(("seq", "shard")),
        P(("seq", "shard")),
        P(("seq", "shard")),
        P(("seq", "shard")),
        P(("seq", "shard")),
        P(("seq", "shard")),
    )

    return jax.shard_map(per_device, mesh=mesh, in_specs=in_specs, out_specs=out_specs, check_vma=False)
```

```python
import jax
import jax.numpy as jnp
from jax import lax
from jax.experimental import pallas as pl
from jax.experimental.pallas import tpu as pltpu
from jax.experimental.layout import Layout, with_layout_constraint
from jax.sharding import PartitionSpec as P


DH = 64
LEN = 1024


EPS = 1e-06
NEG = -1e30
ROOT_HALF = 0.7071067811865476
INV_ROOT_TWO_PI = 0.3989422804014327


def contract_rows(left, right):
    return lax.dot_general(
        left, right, (((0,), (0,)), ((), ())), preferred_element_type=jnp.float32
    )


def times_transpose(left, right):
    return lax.dot_general(
        left, right, (((1,), (1,)), ((), ())), preferred_element_type=jnp.float32
    )


def segment_ids(starts, length):
    places = lax.broadcasted_iota(jnp.int32, (1, length, 1), 1)
    return jnp.sum((starts[:, None, :] <= places).astype(jnp.int32), axis=2)


def norm_forward(rows, gain, shift):
    middle = jnp.mean(rows, axis=-1, keepdims=True)
    centred = rows - middle
    spread = jnp.mean(centred * centred, axis=-1, keepdims=True)
    inverse = lax.rsqrt(spread + EPS)
    normed = centred * inverse
    return (normed * gain + shift, normed, inverse)


def norm_backward(upstream, gain, normed, inverse):
    scaled = upstream * gain
    inner = jnp.mean(scaled, axis=-1, keepdims=True)
    along = jnp.mean(scaled * normed, axis=-1, keepdims=True)
    return inverse * (scaled - inner - normed * along)


def gelu_value(value):
    return 0.5 * value * (1.0 + lax.erf(value * ROOT_HALF))


def gelu_slope(value):
    return (
        0.5 * (1.0 + lax.erf(value * ROOT_HALF))
        + value * jnp.exp(-0.5 * value * value) * INV_ROOT_TWO_PI
    )


def lane_pick(block, index):
    lanes = lax.broadcasted_iota(jnp.int32, block.shape, 1)
    return jnp.sum(jnp.where(lanes == index, block, 0.0), axis=1)


def pack_lanes(pieces):
    pieces = [p.astype(jnp.bfloat16) for p in pieces]
    extra = -sum(p.shape[1] for p in pieces) % 256
    if extra:
        pieces.append(jnp.zeros((pieces[0].shape[0], extra), jnp.bfloat16))
    block = jnp.concatenate(pieces, axis=1)
    return with_layout_constraint(block, Layout(major_to_minor=(0, 1)))


ROWS_PER_STEP = 256


def attention_forward_kernel(qkv_ref, seg_col_ref, seg_row_ref, ctx_ref, lse_ref):
    length = qkv_ref.shape[0]
    heads = ctx_ref.shape[1] // DH
    scale = DH ** (-0.5)
    seg_row = seg_row_ref[...]
    for h in range(heads):
        keys = qkv_ref[:, pl.ds((heads + h) * DH, DH)]
        values = qkv_ref[:, pl.ds((2 * heads + h) * DH, DH)]
        for c in range(length // ROWS_PER_STEP):
            rows = pl.ds(c * ROWS_PER_STEP, ROWS_PER_STEP)
            queries = qkv_ref[rows, pl.ds(h * DH, DH)]
            scores = times_transpose(queries, keys) * scale
            scores = jnp.where(seg_col_ref[rows, :] == seg_row, scores, NEG)
            highest = jnp.max(scores, axis=-1, keepdims=True)
            raised = jnp.exp(scores - highest)
            total = jnp.sum(raised, axis=-1, keepdims=True)
            weights = (raised / total).astype(jnp.bfloat16)
            context = jnp.dot(weights, values, preferred_element_type=jnp.float32)
            ctx_ref[rows, pl.ds(h * DH, DH)] = context.astype(ctx_ref.dtype)
            lse_ref[rows, pl.ds(h, 1)] = highest + jnp.log(total)


def attention_backward_kernel(qkv_ref, seg_col_ref, seg_row_ref, lse_ref, up_ref, grad_ref):
    length = qkv_ref.shape[0]
    heads = up_ref.shape[1] // DH
    scale = DH ** (-0.5)
    seg_row = seg_row_ref[...]
    for h in range(heads):
        keys = qkv_ref[:, pl.ds((heads + h) * DH, DH)]
        values = qkv_ref[:, pl.ds((2 * heads + h) * DH, DH)]
        key_acc = jnp.zeros((length, DH), jnp.float32)
        value_acc = jnp.zeros((length, DH), jnp.float32)
        for c in range(length // ROWS_PER_STEP):
            rows = pl.ds(c * ROWS_PER_STEP, ROWS_PER_STEP)
            queries = qkv_ref[rows, pl.ds(h * DH, DH)]
            upstream = up_ref[rows, pl.ds(h * DH, DH)]
            scores = times_transpose(queries, keys) * scale
            scores = jnp.where(seg_col_ref[rows, :] == seg_row, scores, NEG)
            weights = jnp.exp(scores - lse_ref[rows, pl.ds(h, 1)])
            value_acc = value_acc + contract_rows(weights.astype(jnp.bfloat16), upstream)
            slope = times_transpose(upstream, values)
            inner = jnp.sum(weights * slope, axis=-1, keepdims=True)
            score_grad = (weights * (slope - inner)).astype(jnp.bfloat16)
            query_grad = jnp.dot(score_grad, keys, preferred_element_type=jnp.float32) * scale
            grad_ref[rows, pl.ds(h * DH, DH)] = query_grad.astype(grad_ref.dtype)
            key_acc = key_acc + contract_rows(score_grad, queries) * scale
        grad_ref[:, pl.ds((heads + h) * DH, DH)] = key_acc.astype(grad_ref.dtype)
        grad_ref[:, pl.ds((2 * heads + h) * DH, DH)] = value_acc.astype(grad_ref.dtype)


def attention_forward(qkv, segment):
    length, width = qkv.shape
    heads = width // (3 * DH)
    flops = 4 * heads * length * length * DH
    return pl.pallas_call(
        attention_forward_kernel,
        out_shape=(
            jax.ShapeDtypeStruct((length, heads * DH), jnp.bfloat16),
            jax.ShapeDtypeStruct((length, heads), jnp.float32),
        ),
        in_specs=[pl.BlockSpec(memory_space=pltpu.VMEM)] * 3,
        out_specs=(pl.BlockSpec(memory_space=pltpu.VMEM),) * 2,
        cost_estimate=pl.CostEstimate(
            flops=flops, transcendentals=heads * length * length, bytes_accessed=3 * length * width
        ),
    )(qkv, segment.reshape(length, 1), segment.reshape(1, length))


def attention_backward(qkv, segment, logsum, upstream):
    length, width = qkv.shape
    heads = width // (3 * DH)
    flops = 10 * heads * length * length * DH
    return pl.pallas_call(
        attention_backward_kernel,
        out_shape=jax.ShapeDtypeStruct((length, width), jnp.bfloat16),
        in_specs=[pl.BlockSpec(memory_space=pltpu.VMEM)] * 5,
        out_specs=pl.BlockSpec(memory_space=pltpu.VMEM),
        cost_estimate=pl.CostEstimate(
            flops=flops, transcendentals=heads * length * length, bytes_accessed=5 * length * width
        ),
    )(qkv, segment.reshape(length, 1), segment.reshape(1, length), logsum, upstream)


def scatter_two_stage(block):
    outer = lax.axis_size("seq")
    part = lax.psum_scatter(
        block.reshape(outer, block.shape[0] // outer, -1), "shard", scatter_dimension=1, tiled=True
    )
    return lax.psum_scatter(part.reshape(-1, block.shape[1]), "seq", scatter_dimension=0, tiled=True)


def per_device(
    layer_in,
    layer_cotangent,
    doc_starts,
    query_weight,
    key_weight,
    value_weight,
    out_weight,
    up_weight,
    down_weight,
    query_bias,
    value_bias,
    out_bias,
    up_bias,
    down_bias,
    mixer_gain,
    mixer_shift,
    final_gain,
    final_shift,
):
    axes = ("seq", "shard")
    rows, width = query_weight.shape
    ff = up_weight.shape[1]

    def column(vector):
        return vector.reshape(rows, -1)

    first = jnp.concatenate(
        [
            query_weight,
            key_weight,
            value_weight,
            column(query_bias),
            column(value_bias),
            column(out_bias),
            column(down_bias),
            column(mixer_gain),
            column(mixer_shift),
            column(final_gain),
            column(final_shift),
            column(up_bias),
        ],
        axis=1,
    ).astype(jnp.bfloat16)
    second = jnp.concatenate(
        [out_weight, up_weight, down_weight.reshape(rows, -1)], axis=1
    ).astype(jnp.bfloat16)
    full_first = lax.all_gather(first, axes, axis=0, tiled=True)
    full_second = lax.all_gather(second, axes, axis=0, tiled=True)
    model = full_first.shape[0]
    full_qkv = full_first[:, : 3 * width]
    full_out = full_second[:, :width]
    full_up = full_second[:, width : width + ff]
    full_down = full_second[:, width + ff : width + 2 * ff].reshape(ff, width)
    base = 3 * width
    bias_query, bias_value, bias_out, bias_down, gain_mixer, shift_mixer, gain_final, shift_final = (
        full_first[:, base + i].astype(jnp.float32) for i in range(8)
    )
    bias_up = full_first[:, base + 8 :].reshape(ff).astype(jnp.float32)

    streams, part_len, _ = layer_in.shape
    row_count = streams * part_len
    heads = width // DH
    flat = layer_in.reshape(row_count, width)
    qkv_bias = jnp.concatenate([bias_query, jnp.zeros_like(bias_query), bias_value])
    ways = lax.axis_size("seq")
    me = lax.axis_index("seq")
    group = heads // ways * DH

    def rolled(columns, axis):
        shape = columns.shape
        split = columns.reshape(*shape[:axis], ways, group, *shape[axis + 1 :])
        return jnp.roll(split, -me, axis=axis).reshape(shape)

    def unrolled(columns, axis):
        shape = columns.shape
        split = columns.reshape(*shape[:axis], ways, group, *shape[axis + 1 :])
        return jnp.roll(split, me, axis=axis).reshape(shape)

    def send(blocks, sign):
        out = [blocks[0]]
        for k in range(1, ways):
            pairs = [(j, (j + sign * k) % ways) for j in range(ways)]
            out.append(lax.ppermute(blocks[k], "seq", pairs))
        return out

    roll_qkv = rolled(full_qkv.reshape(model, 3, width), 2).reshape(model, 3 * width)
    roll_bias = rolled(qkv_bias.reshape(3, width), 1).reshape(3 * width)
    roll_out = rolled(full_out, 0)
    segment = segment_ids(doc_starts, LEN)
    sources = [(me - k) % ways for k in range(ways)]
    head_qkv, context_parts, logsum, head_segment = [], [], [], []
    for s in range(streams):
        qkv = (
            jnp.dot(flat[s * part_len : (s + 1) * part_len], roll_qkv, preferred_element_type=jnp.float32)
            + roll_bias
        ).astype(jnp.bfloat16).reshape(part_len, 3, ways, group)
        one_qkv = jnp.concatenate(send([qkv[:, :, k] for k in range(ways)], 1), axis=0).reshape(LEN, -1)
        one_segment = jnp.concatenate(
            [lax.dynamic_slice(segment[s], (src * part_len,), (part_len,)) for src in sources]
        )
        context, one_sum = attention_forward(one_qkv, one_segment)
        context_parts.append(
            jnp.concatenate(
                send([context[k * part_len : (k + 1) * part_len] for k in range(ways)], -1), axis=1
            )
        )
        head_qkv.append(one_qkv)
        logsum.append(one_sum)
        head_segment.append(one_segment)
    context_rows = jnp.stack(context_parts).reshape(row_count, width)
    attn = jnp.dot(context_rows, roll_out, preferred_element_type=jnp.float32) + bias_out
    mixed, normed_mixer, inverse_mixer = norm_forward(
        flat.astype(jnp.float32) + attn, gain_mixer, shift_mixer
    )
    upper = mixed.astype(jnp.bfloat16)
    preact = jnp.dot(upper, full_up, preferred_element_type=jnp.float32) + bias_up
    hidden = gelu_value(preact).astype(jnp.bfloat16)
    ffout = jnp.dot(hidden, full_down, preferred_element_type=jnp.float32) + bias_down
    result, normed_final, inverse_final = norm_forward(mixed + ffout, gain_final, shift_final)
    layer_out = result.astype(jnp.bfloat16).reshape(streams, part_len, width)

    upstream = layer_cotangent.reshape(row_count, width).astype(jnp.float32)
    grad_final_gain = jnp.sum(upstream * normed_final, axis=0)
    grad_final_shift = jnp.sum(upstream, axis=0)
    back_final = norm_backward(upstream, gain_final, normed_final, inverse_final)
    back_ffout = back_final.astype(jnp.bfloat16)
    grad_down_weight = contract_rows(hidden, back_ffout)
    grad_down_bias = jnp.sum(back_ffout.astype(jnp.float32), axis=0)
    back_preact = (times_transpose(back_ffout, full_down) * gelu_slope(preact)).astype(jnp.bfloat16)
    grad_up_weight = contract_rows(upper, back_preact)
    grad_up_bias = jnp.sum(back_preact.astype(jnp.float32), axis=0)
    back_mixed = back_final + times_transpose(back_preact, full_up)
    grad_mixer_gain = jnp.sum(back_mixed * normed_mixer, axis=0)
    grad_mixer_shift = jnp.sum(back_mixed, axis=0)
    back_first = norm_backward(back_mixed, gain_mixer, normed_mixer, inverse_mixer)
    back_attn = back_first.astype(jnp.bfloat16)
    grad_out_weight = unrolled(contract_rows(context_rows, back_attn), 0)
    grad_out_bias = jnp.sum(back_attn.astype(jnp.float32), axis=0)

    early = pack_lanes(
        [
            grad_out_weight,
            grad_up_weight,
            grad_down_weight.reshape(model, -1),
            grad_out_bias[:, None],
            grad_down_bias[:, None],
            grad_mixer_gain[:, None],
            grad_mixer_shift[:, None],
            grad_final_gain[:, None],
            grad_final_shift[:, None],
            grad_up_bias.reshape(model, -1),
        ]
    )
    early, back_attn = lax.optimization_barrier((early, back_attn))
    early_sum = lax.psum_scatter(early, axes, scatter_dimension=0, tiled=True).astype(jnp.float32)

    back_parts = []
    for s in range(streams):
        back_context = times_transpose(
            back_attn[s * part_len : (s + 1) * part_len], roll_out
        ).astype(jnp.bfloat16)
        one_back = jnp.concatenate(
            send([back_context[:, k * group : (k + 1) * group] for k in range(ways)], 1), axis=0
        )
        one_grads = attention_backward(head_qkv[s], head_segment[s], logsum[s], one_back)
        returned = send([one_grads[k * part_len : (k + 1) * part_len] for k in range(ways)], -1)
        back_parts.append(
            jnp.stack([r.reshape(part_len, 3, group) for r in returned], axis=2).reshape(
                part_len, 3 * width
            )
        )
    rows_back = jnp.concatenate(back_parts, axis=0)
    grad_qkv_weight = unrolled(contract_rows(flat, rows_back).reshape(model, 3, width), 2).reshape(
        model, 3 * width
    )
    grad_qkv_bias = unrolled(jnp.sum(rows_back.astype(jnp.float32), axis=0).reshape(3, width), 1)
    grad_query_bias = grad_qkv_bias[0]
    grad_value_bias = grad_qkv_bias[2]
    input_grad = (back_first + times_transpose(rows_back, roll_qkv)).reshape(
        streams, part_len, width
    )
    late = pack_lanes([grad_qkv_weight, grad_query_bias[:, None], grad_value_bias[:, None]])
    late_sum = scatter_two_stage(late).astype(jnp.float32)

    base = width + 2 * ff
    late_tail = late_sum[:, 3 * width :]
    early_tail = early_sum[:, base:]
    return (
        layer_out,
        input_grad,
        late_sum[:, :width],
        late_sum[:, width : 2 * width],
        late_sum[:, 2 * width : 3 * width],
        early_sum[:, :width],
        early_sum[:, width : width + ff],
        early_sum[:, width + ff : width + 2 * ff].reshape(-1, width),
        lane_pick(late_tail, 0),
        lane_pick(late_tail, 1),
        lane_pick(early_tail, 0),
        jnp.stack([lane_pick(early_tail, 6 + i) for i in range(ff // width)], axis=1).reshape(-1),
        lane_pick(early_tail, 1),
        lane_pick(early_tail, 2),
        lane_pick(early_tail, 3),
        lane_pick(early_tail, 4),
        lane_pick(early_tail, 5),
    )


def solution(mesh):
    in_specs = (
        P("shard", "seq", None),
        P("shard", "seq", None),
        P("shard", None),
        P(("seq", "shard"), None),
        P(("seq", "shard"), None),
        P(("seq", "shard"), None),
        P(("seq", "shard"), None),
        P(("seq", "shard"), None),
        P(("seq", "shard"), None),
        P(("seq", "shard")),
        P(("seq", "shard")),
        P(("seq", "shard")),
        P(("seq", "shard")),
        P(("seq", "shard")),
        P(("seq", "shard")),
        P(("seq", "shard")),
        P(("seq", "shard")),
        P(("seq", "shard")),
    )
    out_specs = (
        P("shard", "seq", None),
        P("shard", "seq", None),
        P(("seq", "shard"), None),
        P(("seq", "shard"), None),
        P(("seq", "shard"), None),
        P(("seq", "shard"), None),
        P(("seq", "shard"), None),
        P(("seq", "shard"), None),
        P(("seq", "shard")),
        P(("seq", "shard")),
        P(("seq", "shard")),
        P(("seq", "shard")),
        P(("seq", "shard")),
        P(("seq", "shard")),
        P(("seq", "shard")),
        P(("seq", "shard")),
        P(("seq", "shard")),
    )

    return jax.shard_map(per_device, mesh=mesh, in_specs=in_specs, out_specs=out_specs, check_vma=False)
```

```python
import jax
import jax.numpy as jnp
from jax import lax
from jax.experimental import pallas as pl
from jax.experimental.pallas import tpu as pltpu
from jax.experimental.layout import Layout, with_layout_constraint
from jax.sharding import PartitionSpec as P


DH = 64
LEN = 1024


EPS = 1e-06
NEG = -1e30
ROOT_HALF = 0.7071067811865476
INV_ROOT_TWO_PI = 0.3989422804014327


def contract_rows(left, right):
    return lax.dot_general(
        left, right, (((0,), (0,)), ((), ())), preferred_element_type=jnp.float32
    )


def times_transpose(left, right):
    return lax.dot_general(
        left, right, (((1,), (1,)), ((), ())), preferred_element_type=jnp.float32
    )


def segment_ids(starts, length):
    places = lax.broadcasted_iota(jnp.int32, (1, length, 1), 1)
    return jnp.sum((starts[:, None, :] <= places).astype(jnp.int32), axis=2)


def norm_forward(rows, gain, shift):
    middle = jnp.mean(rows, axis=-1, keepdims=True)
    centred = rows - middle
    spread = jnp.mean(centred * centred, axis=-1, keepdims=True)
    inverse = lax.rsqrt(spread + EPS)
    normed = centred * inverse
    return (normed * gain + shift, normed, inverse)


def norm_backward(upstream, gain, normed, inverse):
    scaled = upstream * gain
    inner = jnp.mean(scaled, axis=-1, keepdims=True)
    along = jnp.mean(scaled * normed, axis=-1, keepdims=True)
    return inverse * (scaled - inner - normed * along)


def gelu_value(value):
    return 0.5 * value * (1.0 + lax.erf(value * ROOT_HALF))


def gelu_slope(value):
    return (
        0.5 * (1.0 + lax.erf(value * ROOT_HALF))
        + value * jnp.exp(-0.5 * value * value) * INV_ROOT_TWO_PI
    )


def lane_pick(block, index):
    lanes = lax.broadcasted_iota(jnp.int32, block.shape, 1)
    return jnp.sum(jnp.where(lanes == index, block, 0.0), axis=1)


def pack_lanes(pieces):
    pieces = [p.astype(jnp.bfloat16) for p in pieces]
    extra = -sum(p.shape[1] for p in pieces) % 256
    if extra:
        pieces.append(jnp.zeros((pieces[0].shape[0], extra), jnp.bfloat16))
    block = jnp.concatenate(pieces, axis=1)
    return with_layout_constraint(block, Layout(major_to_minor=(0, 1)))


ROWS_PER_STEP = 256


def attention_forward_kernel(qkv_ref, seg_col_ref, seg_row_ref, ctx_ref, lse_ref):
    length = qkv_ref.shape[0]
    heads = ctx_ref.shape[1] // DH
    scale = DH ** (-0.5)
    seg_row = seg_row_ref[...]
    for h in range(heads):
        keys = qkv_ref[:, pl.ds((heads + h) * DH, DH)]
        values = qkv_ref[:, pl.ds((2 * heads + h) * DH, DH)]
        for c in range(length // ROWS_PER_STEP):
            rows = pl.ds(c * ROWS_PER_STEP, ROWS_PER_STEP)
            queries = qkv_ref[rows, pl.ds(h * DH, DH)]
            scores = times_transpose(queries, keys) * scale
            scores = jnp.where(seg_col_ref[rows, :] == seg_row, scores, NEG)
            highest = jnp.max(scores, axis=-1, keepdims=True)
            raised = jnp.exp(scores - highest)
            total = jnp.sum(raised, axis=-1, keepdims=True)
            weights = (raised / total).astype(jnp.bfloat16)
            context = jnp.dot(weights, values, preferred_element_type=jnp.float32)
            ctx_ref[rows, pl.ds(h * DH, DH)] = context.astype(ctx_ref.dtype)
            lse_ref[rows, pl.ds(h, 1)] = highest + jnp.log(total)


def attention_backward_kernel(qkv_ref, seg_col_ref, seg_row_ref, lse_ref, up_ref, grad_ref):
    length = qkv_ref.shape[0]
    heads = up_ref.shape[1] // DH
    scale = DH ** (-0.5)
    seg_row = seg_row_ref[...]
    for h in range(heads):
        keys = qkv_ref[:, pl.ds((heads + h) * DH, DH)]
        values = qkv_ref[:, pl.ds((2 * heads + h) * DH, DH)]
        key_acc = jnp.zeros((length, DH), jnp.float32)
        value_acc = jnp.zeros((length, DH), jnp.float32)
        for c in range(length // ROWS_PER_STEP):
            rows = pl.ds(c * ROWS_PER_STEP, ROWS_PER_STEP)
            queries = qkv_ref[rows, pl.ds(h * DH, DH)]
            upstream = up_ref[rows, pl.ds(h * DH, DH)]
            scores = times_transpose(queries, keys) * scale
            scores = jnp.where(seg_col_ref[rows, :] == seg_row, scores, NEG)
            weights = jnp.exp(scores - lse_ref[rows, pl.ds(h, 1)])
            value_acc = value_acc + contract_rows(weights.astype(jnp.bfloat16), upstream)
            slope = times_transpose(upstream, values)
            inner = jnp.sum(weights * slope, axis=-1, keepdims=True)
            score_grad = (weights * (slope - inner)).astype(jnp.bfloat16)
            query_grad = jnp.dot(score_grad, keys, preferred_element_type=jnp.float32) * scale
            grad_ref[rows, pl.ds(h * DH, DH)] = query_grad.astype(grad_ref.dtype)
            key_acc = key_acc + contract_rows(score_grad, queries) * scale
        grad_ref[:, pl.ds((heads + h) * DH, DH)] = key_acc.astype(grad_ref.dtype)
        grad_ref[:, pl.ds((2 * heads + h) * DH, DH)] = value_acc.astype(grad_ref.dtype)


def attention_forward(qkv, segment):
    length, width = qkv.shape
    heads = width // (3 * DH)
    flops = 4 * heads * length * length * DH
    return pl.pallas_call(
        attention_forward_kernel,
        out_shape=(
            jax.ShapeDtypeStruct((length, heads * DH), jnp.bfloat16),
            jax.ShapeDtypeStruct((length, heads), jnp.float32),
        ),
        in_specs=[pl.BlockSpec(memory_space=pltpu.VMEM)] * 3,
        out_specs=(pl.BlockSpec(memory_space=pltpu.VMEM),) * 2,
        cost_estimate=pl.CostEstimate(
            flops=flops, transcendentals=heads * length * length, bytes_accessed=3 * length * width
        ),
    )(qkv, segment.reshape(length, 1), segment.reshape(1, length))


def attention_backward(qkv, segment, logsum, upstream):
    length, width = qkv.shape
    heads = width // (3 * DH)
    flops = 10 * heads * length * length * DH
    return pl.pallas_call(
        attention_backward_kernel,
        out_shape=jax.ShapeDtypeStruct((length, width), jnp.bfloat16),
        in_specs=[pl.BlockSpec(memory_space=pltpu.VMEM)] * 5,
        out_specs=pl.BlockSpec(memory_space=pltpu.VMEM),
        cost_estimate=pl.CostEstimate(
            flops=flops, transcendentals=heads * length * length, bytes_accessed=5 * length * width
        ),
    )(qkv, segment.reshape(length, 1), segment.reshape(1, length), logsum, upstream)


def scatter_two_stage(block):
    outer = lax.axis_size("seq")
    part = lax.psum_scatter(
        block.reshape(outer, block.shape[0] // outer, -1), "shard", scatter_dimension=1, tiled=True
    )
    return lax.psum_scatter(part.reshape(-1, block.shape[1]), "seq", scatter_dimension=0, tiled=True)


def per_device(
    layer_in,
    layer_cotangent,
    doc_starts,
    query_weight,
    key_weight,
    value_weight,
    out_weight,
    up_weight,
    down_weight,
    query_bias,
    value_bias,
    out_bias,
    up_bias,
    down_bias,
    mixer_gain,
    mixer_shift,
    final_gain,
    final_shift,
):
    axes = ("seq", "shard")
    rows, width = query_weight.shape
    ff = up_weight.shape[1]

    def column(vector):
        return vector.reshape(rows, -1)

    first = jnp.concatenate(
        [
            query_weight,
            key_weight,
            value_weight,
            column(query_bias),
            column(value_bias),
            column(out_bias),
            column(down_bias),
            column(mixer_gain),
            column(mixer_shift),
            column(final_gain),
            column(final_shift),
            column(up_bias),
        ],
        axis=1,
    ).astype(jnp.bfloat16)
    second = jnp.concatenate(
        [out_weight, up_weight, down_weight.reshape(rows, -1)], axis=1
    ).astype(jnp.bfloat16)
    full_first = lax.all_gather(first, axes, axis=0, tiled=True)
    full_second = lax.all_gather(second, axes, axis=0, tiled=True)
    model = full_first.shape[0]
    full_qkv = full_first[:, : 3 * width]
    full_out = full_second[:, :width]
    full_up = full_second[:, width : width + ff]
    full_down = full_second[:, width + ff : width + 2 * ff].reshape(ff, width)
    base = 3 * width
    bias_query, bias_value, bias_out, bias_down, gain_mixer, shift_mixer, gain_final, shift_final = (
        full_first[:, base + i].astype(jnp.float32) for i in range(8)
    )
    bias_up = full_first[:, base + 8 :].reshape(ff).astype(jnp.float32)

    streams, part_len, _ = layer_in.shape
    row_count = streams * part_len
    heads = width // DH
    flat = layer_in.reshape(row_count, width)
    qkv_bias = jnp.concatenate([bias_query, jnp.zeros_like(bias_query), bias_value])
    ways = lax.axis_size("seq")
    me = lax.axis_index("seq")
    group = heads // ways * DH

    def rolled(columns, axis):
        shape = columns.shape
        split = columns.reshape(*shape[:axis], ways, group, *shape[axis + 1 :])
        return jnp.roll(split, -me, axis=axis).reshape(shape)

    def unrolled(columns, axis):
        shape = columns.shape
        split = columns.reshape(*shape[:axis], ways, group, *shape[axis + 1 :])
        return jnp.roll(split, me, axis=axis).reshape(shape)

    def send(blocks, sign):
        out = [blocks[0]]
        for k in range(1, ways):
            pairs = [(j, (j + sign * k) % ways) for j in range(ways)]
            out.append(lax.ppermute(blocks[k], "seq", pairs))
        return out

    roll_qkv = rolled(full_qkv.reshape(model, 3, width), 2).reshape(model, 3 * width)
    roll_bias = rolled(qkv_bias.reshape(3, width), 1).reshape(3 * width)
    roll_out = rolled(full_out, 0)
    segment = segment_ids(doc_starts, LEN)
    sources = [(me - k) % ways for k in range(ways)]
    head_qkv, context_parts, logsum, head_segment = [], [], [], []
    for s in range(streams):
        qkv = (
            jnp.dot(flat[s * part_len : (s + 1) * part_len], roll_qkv, preferred_element_type=jnp.float32)
            + roll_bias
        ).astype(jnp.bfloat16).reshape(part_len, 3, ways, group)
        one_qkv = jnp.concatenate(send([qkv[:, :, k] for k in range(ways)], 1), axis=0).reshape(LEN, -1)
        one_segment = jnp.concatenate(
            [lax.dynamic_slice(segment[s], (src * part_len,), (part_len,)) for src in sources]
        )
        context, one_sum = attention_forward(one_qkv, one_segment)
        context_parts.append(
            jnp.concatenate(
                send([context[k * part_len : (k + 1) * part_len] for k in range(ways)], -1), axis=1
            )
        )
        head_qkv.append(one_qkv)
        logsum.append(one_sum)
        head_segment.append(one_segment)
    context_rows = jnp.stack(context_parts).reshape(row_count, width)
    attn = jnp.dot(context_rows, roll_out, preferred_element_type=jnp.float32) + bias_out
    mixed, normed_mixer, inverse_mixer = norm_forward(
        flat.astype(jnp.float32) + attn, gain_mixer, shift_mixer
    )
    upper = mixed.astype(jnp.bfloat16)
    preact = jnp.dot(upper, full_up, preferred_element_type=jnp.float32) + bias_up
    hidden = gelu_value(preact).astype(jnp.bfloat16)
    ffout = jnp.dot(hidden, full_down, preferred_element_type=jnp.float32) + bias_down
    result, normed_final, inverse_final = norm_forward(mixed + ffout, gain_final, shift_final)
    layer_out = result.astype(jnp.bfloat16).reshape(streams, part_len, width)

    upstream = layer_cotangent.reshape(row_count, width).astype(jnp.float32)
    grad_final_gain = jnp.sum(upstream * normed_final, axis=0)
    grad_final_shift = jnp.sum(upstream, axis=0)
    back_final = norm_backward(upstream, gain_final, normed_final, inverse_final)
    back_ffout = back_final.astype(jnp.bfloat16)
    grad_down_weight = contract_rows(hidden, back_ffout)
    grad_down_bias = jnp.sum(back_ffout.astype(jnp.float32), axis=0)
    back_preact = (times_transpose(back_ffout, full_down) * gelu_slope(preact)).astype(jnp.bfloat16)
    grad_up_weight = contract_rows(upper, back_preact)
    grad_up_bias = jnp.sum(back_preact.astype(jnp.float32), axis=0)
    back_mixed = back_final + times_transpose(back_preact, full_up)
    grad_mixer_gain = jnp.sum(back_mixed * normed_mixer, axis=0)
    grad_mixer_shift = jnp.sum(back_mixed, axis=0)
    back_first = norm_backward(back_mixed, gain_mixer, normed_mixer, inverse_mixer)
    back_attn = back_first.astype(jnp.bfloat16)
    grad_out_weight = unrolled(contract_rows(context_rows, back_attn), 0)
    grad_out_bias = jnp.sum(back_attn.astype(jnp.float32), axis=0)

    early = pack_lanes(
        [
            grad_out_weight,
            grad_up_weight,
            grad_down_weight.reshape(model, -1),
            grad_out_bias[:, None],
            grad_down_bias[:, None],
            grad_mixer_gain[:, None],
            grad_mixer_shift[:, None],
            grad_final_gain[:, None],
            grad_final_shift[:, None],
            grad_up_bias.reshape(model, -1),
        ]
    )
    early, back_attn = lax.optimization_barrier((early, back_attn))
    early_sum = lax.psum_scatter(early, axes, scatter_dimension=0, tiled=True).astype(jnp.float32)

    back_parts = []
    for s in range(streams):
        back_context = times_transpose(
            back_attn[s * part_len : (s + 1) * part_len], roll_out
        ).astype(jnp.bfloat16)
        one_back = jnp.concatenate(
            send([back_context[:, k * group : (k + 1) * group] for k in range(ways)], 1), axis=0
        )
        one_grads = attention_backward(head_qkv[s], head_segment[s], logsum[s], one_back)
        returned = send([one_grads[k * part_len : (k + 1) * part_len] for k in range(ways)], -1)
        placed = jnp.zeros((part_len, 3, ways, group), jnp.bfloat16)
        for k in range(ways):
            placed = lax.dynamic_update_slice(
                placed, returned[k].reshape(part_len, 3, 1, group), (0, 0, (me + k) % ways, 0)
            )
        back_parts.append(placed.reshape(part_len, 3 * width))
    rows_back = jnp.concatenate(back_parts, axis=0)
    grad_qkv_weight = contract_rows(flat, rows_back)
    grad_qkv_bias = jnp.sum(rows_back.astype(jnp.float32), axis=0).reshape(3, width)
    grad_query_bias = grad_qkv_bias[0]
    grad_value_bias = grad_qkv_bias[2]
    input_grad = (back_first + times_transpose(rows_back, full_qkv)).reshape(
        streams, part_len, width
    )
    late = pack_lanes([grad_qkv_weight, grad_query_bias[:, None], grad_value_bias[:, None]])
    late_sum = scatter_two_stage(late).astype(jnp.float32)

    base = width + 2 * ff
    late_tail = late_sum[:, 3 * width :]
    early_tail = early_sum[:, base:]
    return (
        layer_out,
        input_grad,
        late_sum[:, :width],
        late_sum[:, width : 2 * width],
        late_sum[:, 2 * width : 3 * width],
        early_sum[:, :width],
        early_sum[:, width : width + ff],
        early_sum[:, width + ff : width + 2 * ff].reshape(-1, width),
        lane_pick(late_tail, 0),
        lane_pick(late_tail, 1),
        lane_pick(early_tail, 0),
        jnp.stack([lane_pick(early_tail, 6 + i) for i in range(ff // width)], axis=1).reshape(-1),
        lane_pick(early_tail, 1),
        lane_pick(early_tail, 2),
        lane_pick(early_tail, 3),
        lane_pick(early_tail, 4),
        lane_pick(early_tail, 5),
    )


def solution(mesh):
    in_specs = (
        P("shard", "seq", None),
        P("shard", "seq", None),
        P("shard", None),
        P(("seq", "shard"), None),
        P(("seq", "shard"), None),
        P(("seq", "shard"), None),
        P(("seq", "shard"), None),
        P(("seq", "shard"), None),
        P(("seq", "shard"), None),
        P(("seq", "shard")),
        P(("seq", "shard")),
        P(("seq", "shard")),
        P(("seq", "shard")),
        P(("seq", "shard")),
        P(("seq", "shard")),
        P(("seq", "shard")),
        P(("seq", "shard")),
        P(("seq", "shard")),
    )
    out_specs = (
        P("shard", "seq", None),
        P("shard", "seq", None),
        P(("seq", "shard"), None),
        P(("seq", "shard"), None),
        P(("seq", "shard"), None),
        P(("seq", "shard"), None),
        P(("seq", "shard"), None),
        P(("seq", "shard"), None),
        P(("seq", "shard")),
        P(("seq", "shard")),
        P(("seq", "shard")),
        P(("seq", "shard")),
        P(("seq", "shard")),
        P(("seq", "shard")),
        P(("seq", "shard")),
        P(("seq", "shard")),
        P(("seq", "shard")),
    )

    return jax.shard_map(per_device, mesh=mesh, in_specs=in_specs, out_specs=out_specs, check_vma=False)
```

```python
import jax
import jax.numpy as jnp
from jax import lax
from jax.experimental import pallas as pl
from jax.experimental.pallas import tpu as pltpu
from jax.experimental.layout import Layout, with_layout_constraint
from jax.sharding import PartitionSpec as P


DH = 64
LEN = 1024


EPS = 1e-06
NEG = -1e30
ROOT_HALF = 0.7071067811865476
INV_ROOT_TWO_PI = 0.3989422804014327


def contract_rows(left, right):
    return lax.dot_general(
        left, right, (((0,), (0,)), ((), ())), preferred_element_type=jnp.float32
    )


def times_transpose(left, right):
    return lax.dot_general(
        left, right, (((1,), (1,)), ((), ())), preferred_element_type=jnp.float32
    )


def segment_ids(starts, length):
    places = lax.broadcasted_iota(jnp.int32, (1, length, 1), 1)
    return jnp.sum((starts[:, None, :] <= places).astype(jnp.int32), axis=2)


def norm_forward(rows, gain, shift):
    middle = jnp.mean(rows, axis=-1, keepdims=True)
    centred = rows - middle
    spread = jnp.mean(centred * centred, axis=-1, keepdims=True)
    inverse = lax.rsqrt(spread + EPS)
    normed = centred * inverse
    return (normed * gain + shift, normed, inverse)


def norm_backward(upstream, gain, normed, inverse):
    scaled = upstream * gain
    inner = jnp.mean(scaled, axis=-1, keepdims=True)
    along = jnp.mean(scaled * normed, axis=-1, keepdims=True)
    return inverse * (scaled - inner - normed * along)


def gelu_value(value):
    return 0.5 * value * (1.0 + lax.erf(value * ROOT_HALF))


def gelu_slope(value):
    return (
        0.5 * (1.0 + lax.erf(value * ROOT_HALF))
        + value * jnp.exp(-0.5 * value * value) * INV_ROOT_TWO_PI
    )


def lane_pick(block, index):
    lanes = lax.broadcasted_iota(jnp.int32, block.shape, 1)
    return jnp.sum(jnp.where(lanes == index, block, 0.0), axis=1)


def pack_lanes(pieces):
    pieces = [p.astype(jnp.bfloat16) for p in pieces]
    extra = -sum(p.shape[1] for p in pieces) % 256
    if extra:
        pieces.append(jnp.zeros((pieces[0].shape[0], extra), jnp.bfloat16))
    block = jnp.concatenate(pieces, axis=1)
    return with_layout_constraint(block, Layout(major_to_minor=(0, 1)))


ROWS_PER_STEP = 256


def attention_forward_kernel(qkv_ref, seg_col_ref, seg_row_ref, ctx_ref, lse_ref):
    length = qkv_ref.shape[0]
    heads = ctx_ref.shape[1] // DH
    scale = DH ** (-0.5)
    seg_row = seg_row_ref[...]
    for h in range(heads):
        keys = qkv_ref[:, pl.ds((heads + h) * DH, DH)]
        values = qkv_ref[:, pl.ds((2 * heads + h) * DH, DH)]
        for c in range(length // ROWS_PER_STEP):
            rows = pl.ds(c * ROWS_PER_STEP, ROWS_PER_STEP)
            queries = qkv_ref[rows, pl.ds(h * DH, DH)]
            scores = times_transpose(queries, keys) * scale
            scores = jnp.where(seg_col_ref[rows, :] == seg_row, scores, NEG)
            highest = jnp.max(scores, axis=-1, keepdims=True)
            raised = jnp.exp(scores - highest)
            total = jnp.sum(raised, axis=-1, keepdims=True)
            weights = (raised / total).astype(jnp.bfloat16)
            context = jnp.dot(weights, values, preferred_element_type=jnp.float32)
            ctx_ref[rows, pl.ds(h * DH, DH)] = context.astype(ctx_ref.dtype)
            lse_ref[rows, pl.ds(h, 1)] = highest + jnp.log(total)


def attention_backward_kernel(qkv_ref, seg_col_ref, seg_row_ref, lse_ref, up_ref, grad_ref):
    length = qkv_ref.shape[0]
    heads = up_ref.shape[1] // DH
    scale = DH ** (-0.5)
    seg_row = seg_row_ref[...]
    for h in range(heads):
        keys = qkv_ref[:, pl.ds((heads + h) * DH, DH)]
        values = qkv_ref[:, pl.ds((2 * heads + h) * DH, DH)]
        key_acc = jnp.zeros((length, DH), jnp.float32)
        value_acc = jnp.zeros((length, DH), jnp.float32)
        for c in range(length // ROWS_PER_STEP):
            rows = pl.ds(c * ROWS_PER_STEP, ROWS_PER_STEP)
            queries = qkv_ref[rows, pl.ds(h * DH, DH)]
            upstream = up_ref[rows, pl.ds(h * DH, DH)]
            scores = times_transpose(queries, keys) * scale
            scores = jnp.where(seg_col_ref[rows, :] == seg_row, scores, NEG)
            weights = jnp.exp(scores - lse_ref[rows, pl.ds(h, 1)])
            value_acc = value_acc + contract_rows(weights.astype(jnp.bfloat16), upstream)
            slope = times_transpose(upstream, values)
            inner = jnp.sum(weights * slope, axis=-1, keepdims=True)
            score_grad = (weights * (slope - inner)).astype(jnp.bfloat16)
            query_grad = jnp.dot(score_grad, keys, preferred_element_type=jnp.float32) * scale
            grad_ref[rows, pl.ds(h * DH, DH)] = query_grad.astype(grad_ref.dtype)
            key_acc = key_acc + contract_rows(score_grad, queries) * scale
        grad_ref[:, pl.ds((heads + h) * DH, DH)] = key_acc.astype(grad_ref.dtype)
        grad_ref[:, pl.ds((2 * heads + h) * DH, DH)] = value_acc.astype(grad_ref.dtype)


def attention_forward(qkv, segment):
    length, width = qkv.shape
    heads = width // (3 * DH)
    flops = 4 * heads * length * length * DH
    return pl.pallas_call(
        attention_forward_kernel,
        out_shape=(
            jax.ShapeDtypeStruct((length, heads * DH), jnp.bfloat16),
            jax.ShapeDtypeStruct((length, heads), jnp.float32),
        ),
        in_specs=[pl.BlockSpec(memory_space=pltpu.VMEM)] * 3,
        out_specs=(pl.BlockSpec(memory_space=pltpu.VMEM),) * 2,
        cost_estimate=pl.CostEstimate(
            flops=flops, transcendentals=heads * length * length, bytes_accessed=3 * length * width
        ),
    )(qkv, segment.reshape(length, 1), segment.reshape(1, length))


def attention_backward(qkv, segment, logsum, upstream):
    length, width = qkv.shape
    heads = width // (3 * DH)
    flops = 10 * heads * length * length * DH
    return pl.pallas_call(
        attention_backward_kernel,
        out_shape=jax.ShapeDtypeStruct((length, width), jnp.bfloat16),
        in_specs=[pl.BlockSpec(memory_space=pltpu.VMEM)] * 5,
        out_specs=pl.BlockSpec(memory_space=pltpu.VMEM),
        cost_estimate=pl.CostEstimate(
            flops=flops, transcendentals=heads * length * length, bytes_accessed=5 * length * width
        ),
    )(qkv, segment.reshape(length, 1), segment.reshape(1, length), logsum, upstream)


def scatter_two_stage(block):
    part = lax.psum_scatter(block, "seq", scatter_dimension=0, tiled=True)
    return lax.psum_scatter(part, "shard", scatter_dimension=0, tiled=True)


def per_device(
    layer_in,
    layer_cotangent,
    doc_starts,
    query_weight,
    key_weight,
    value_weight,
    out_weight,
    up_weight,
    down_weight,
    query_bias,
    value_bias,
    out_bias,
    up_bias,
    down_bias,
    mixer_gain,
    mixer_shift,
    final_gain,
    final_shift,
):
    axes = ("seq", "shard")
    rows, width = query_weight.shape
    ff = up_weight.shape[1]

    def column(vector):
        return vector.reshape(rows, -1)

    first = jnp.concatenate(
        [
            query_weight,
            key_weight,
            value_weight,
            column(query_bias),
            column(value_bias),
            column(out_bias),
            column(down_bias),
            column(mixer_gain),
            column(mixer_shift),
            column(final_gain),
            column(final_shift),
            column(up_bias),
        ],
        axis=1,
    ).astype(jnp.bfloat16)
    second = jnp.concatenate(
        [out_weight, up_weight, down_weight.reshape(rows, -1)], axis=1
    ).astype(jnp.bfloat16)
    full_first = lax.all_gather(first, axes, axis=0, tiled=True)
    full_second = lax.all_gather(second, axes, axis=0, tiled=True)
    model = full_first.shape[0]
    full_qkv = full_first[:, : 3 * width]
    full_out = full_second[:, :width]
    full_up = full_second[:, width : width + ff]
    full_down = full_second[:, width + ff : width + 2 * ff].reshape(ff, width)
    base = 3 * width
    bias_query, bias_value, bias_out, bias_down, gain_mixer, shift_mixer, gain_final, shift_final = (
        full_first[:, base + i].astype(jnp.float32) for i in range(8)
    )
    bias_up = full_first[:, base + 8 :].reshape(ff).astype(jnp.float32)

    streams, part_len, _ = layer_in.shape
    row_count = streams * part_len
    heads = width // DH
    flat = layer_in.reshape(row_count, width)
    qkv_bias = jnp.concatenate([bias_query, jnp.zeros_like(bias_query), bias_value])
    ways = lax.axis_size("seq")
    me = lax.axis_index("seq")
    group = heads // ways * DH

    def rolled(columns, axis):
        shape = columns.shape
        split = columns.reshape(*shape[:axis], ways, group, *shape[axis + 1 :])
        return jnp.roll(split, -me, axis=axis).reshape(shape)

    def unrolled(columns, axis):
        shape = columns.shape
        split = columns.reshape(*shape[:axis], ways, group, *shape[axis + 1 :])
        return jnp.roll(split, me, axis=axis).reshape(shape)

    def send(blocks, sign):
        out = [blocks[0]]
        for k in range(1, ways):
            pairs = [(j, (j + sign * k) % ways) for j in range(ways)]
            out.append(lax.ppermute(blocks[k], "seq", pairs))
        return out

    roll_qkv = rolled(full_qkv.reshape(model, 3, width), 2).reshape(model, 3 * width)
    roll_bias = rolled(qkv_bias.reshape(3, width), 1).reshape(3 * width)
    roll_out = rolled(full_out, 0)
    segment = segment_ids(doc_starts, LEN)
    sources = [(me - k) % ways for k in range(ways)]
    head_qkv, context_parts, logsum, head_segment = [], [], [], []
    for s in range(streams):
        qkv = (
            jnp.dot(flat[s * part_len : (s + 1) * part_len], roll_qkv, preferred_element_type=jnp.float32)
            + roll_bias
        ).astype(jnp.bfloat16).reshape(part_len, 3, ways, group)
        one_qkv = jnp.concatenate(send([qkv[:, :, k] for k in range(ways)], 1), axis=0).reshape(LEN, -1)
        one_segment = jnp.concatenate(
            [lax.dynamic_slice(segment[s], (src * part_len,), (part_len,)) for src in sources]
        )
        context, one_sum = attention_forward(one_qkv, one_segment)
        context_parts.append(
            jnp.concatenate(
                send([context[k * part_len : (k + 1) * part_len] for k in range(ways)], -1), axis=1
            )
        )
        head_qkv.append(one_qkv)
        logsum.append(one_sum)
        head_segment.append(one_segment)
    context_rows = jnp.stack(context_parts).reshape(row_count, width)
    attn = jnp.dot(context_rows, roll_out, preferred_element_type=jnp.float32) + bias_out
    mixed, normed_mixer, inverse_mixer = norm_forward(
        flat.astype(jnp.float32) + attn, gain_mixer, shift_mixer
    )
    upper = mixed.astype(jnp.bfloat16)
    preact = jnp.dot(upper, full_up, preferred_element_type=jnp.float32) + bias_up
    hidden = gelu_value(preact).astype(jnp.bfloat16)
    ffout = jnp.dot(hidden, full_down, preferred_element_type=jnp.float32) + bias_down
    result, normed_final, inverse_final = norm_forward(mixed + ffout, gain_final, shift_final)
    layer_out = result.astype(jnp.bfloat16).reshape(streams, part_len, width)

    upstream = layer_cotangent.reshape(row_count, width).astype(jnp.float32)
    grad_final_gain = jnp.sum(upstream * normed_final, axis=0)
    grad_final_shift = jnp.sum(upstream, axis=0)
    back_final = norm_backward(upstream, gain_final, normed_final, inverse_final)
    back_ffout = back_final.astype(jnp.bfloat16)
    grad_down_weight = contract_rows(hidden, back_ffout)
    grad_down_bias = jnp.sum(back_ffout.astype(jnp.float32), axis=0)
    back_preact = (times_transpose(back_ffout, full_down) * gelu_slope(preact)).astype(jnp.bfloat16)
    grad_up_weight = contract_rows(upper, back_preact)
    grad_up_bias = jnp.sum(back_preact.astype(jnp.float32), axis=0)
    back_mixed = back_final + times_transpose(back_preact, full_up)
    grad_mixer_gain = jnp.sum(back_mixed * normed_mixer, axis=0)
    grad_mixer_shift = jnp.sum(back_mixed, axis=0)
    back_first = norm_backward(back_mixed, gain_mixer, normed_mixer, inverse_mixer)
    back_attn = back_first.astype(jnp.bfloat16)
    grad_out_weight = unrolled(contract_rows(context_rows, back_attn), 0)
    grad_out_bias = jnp.sum(back_attn.astype(jnp.float32), axis=0)

    early = pack_lanes(
        [
            grad_out_weight,
            grad_up_weight,
            grad_down_weight.reshape(model, -1),
            grad_out_bias[:, None],
            grad_down_bias[:, None],
            grad_mixer_gain[:, None],
            grad_mixer_shift[:, None],
            grad_final_gain[:, None],
            grad_final_shift[:, None],
            grad_up_bias.reshape(model, -1),
        ]
    )
    early, back_attn = lax.optimization_barrier((early, back_attn))
    early_sum = lax.psum_scatter(early, axes, scatter_dimension=0, tiled=True).astype(jnp.float32)

    back_parts = []
    for s in range(streams):
        back_context = times_transpose(
            back_attn[s * part_len : (s + 1) * part_len], roll_out
        ).astype(jnp.bfloat16)
        one_back = jnp.concatenate(
            send([back_context[:, k * group : (k + 1) * group] for k in range(ways)], 1), axis=0
        )
        one_grads = attention_backward(head_qkv[s], head_segment[s], logsum[s], one_back)
        returned = send([one_grads[k * part_len : (k + 1) * part_len] for k in range(ways)], -1)
        back_parts.append(
            jnp.stack([r.reshape(part_len, 3, group) for r in returned], axis=2).reshape(
                part_len, 3 * width
            )
        )
    rows_back = jnp.concatenate(back_parts, axis=0)
    grad_qkv_weight = unrolled(contract_rows(flat, rows_back).reshape(model, 3, width), 2).reshape(
        model, 3 * width
    )
    grad_qkv_bias = unrolled(jnp.sum(rows_back.astype(jnp.float32), axis=0).reshape(3, width), 1)
    grad_query_bias = grad_qkv_bias[0]
    grad_value_bias = grad_qkv_bias[2]
    input_grad = (back_first + times_transpose(rows_back, roll_qkv)).reshape(
        streams, part_len, width
    )
    late = pack_lanes([grad_qkv_weight, grad_query_bias[:, None], grad_value_bias[:, None]])
    late_sum = scatter_two_stage(late).astype(jnp.float32)

    base = width + 2 * ff
    late_tail = late_sum[:, 3 * width :]
    early_tail = early_sum[:, base:]
    return (
        layer_out,
        input_grad,
        late_sum[:, :width],
        late_sum[:, width : 2 * width],
        late_sum[:, 2 * width : 3 * width],
        early_sum[:, :width],
        early_sum[:, width : width + ff],
        early_sum[:, width + ff : width + 2 * ff].reshape(-1, width),
        lane_pick(late_tail, 0),
        lane_pick(late_tail, 1),
        lane_pick(early_tail, 0),
        jnp.stack([lane_pick(early_tail, 6 + i) for i in range(ff // width)], axis=1).reshape(-1),
        lane_pick(early_tail, 1),
        lane_pick(early_tail, 2),
        lane_pick(early_tail, 3),
        lane_pick(early_tail, 4),
        lane_pick(early_tail, 5),
    )


def solution(mesh):
    in_specs = (
        P("shard", "seq", None),
        P("shard", "seq", None),
        P("shard", None),
        P(("seq", "shard"), None),
        P(("seq", "shard"), None),
        P(("seq", "shard"), None),
        P(("seq", "shard"), None),
        P(("seq", "shard"), None),
        P(("seq", "shard"), None),
        P(("seq", "shard")),
        P(("seq", "shard")),
        P(("seq", "shard")),
        P(("seq", "shard")),
        P(("seq", "shard")),
        P(("seq", "shard")),
        P(("seq", "shard")),
        P(("seq", "shard")),
        P(("seq", "shard")),
    )
    out_specs = (
        P("shard", "seq", None),
        P("shard", "seq", None),
        P(("seq", "shard"), None),
        P(("seq", "shard"), None),
        P(("seq", "shard"), None),
        P(("seq", "shard"), None),
        P(("seq", "shard"), None),
        P(("seq", "shard"), None),
        P(("seq", "shard")),
        P(("seq", "shard")),
        P(("seq", "shard")),
        P(("seq", "shard")),
        P(("seq", "shard")),
        P(("seq", "shard")),
        P(("seq", "shard")),
        P(("seq", "shard")),
        P(("seq", "shard")),
    )

    return jax.shard_map(per_device, mesh=mesh, in_specs=in_specs, out_specs=out_specs, check_vma=False)
```
